32 devices in a mesh: vol: 8 (over z, y), orient: 4 (over x, core).
Axes of the slice: x: 2, y: 2, z: 4, core: 2. Of those that a mesh axis runs over, the one named last changes fastest.
Arguments:
- tomogram: bfloat16 [640, 512, 256], P('vol', 'orient'), may hold values from -40 to 40
- templates: bfloat16 [4, 32, 1024], P('orient'), may hold values from 0 to 5
- corner_z: int32 [8, 60], P('vol', 'orient'), may hold values from 0 to 16
- corner_y: int32 [8, 60], P('vol', 'orient'), may hold values from 0 to 64
- corner_x: int32 [8, 60], P('vol', 'orient'), may hold values from 0 to 192
- loads: int32 [8, 4, 8], P('vol', 'orient'), may hold values from 0 to 2, as said below
Outputs:
- peaks: float32 [8, 60, 4], P('vol', 'orient')
- best: float32 [8, 60], P('vol', 'orient')
The draws below stay inside these ranges and needn't reach their ends.
Inputs may be any that keep to these rules, and one draw needn't show every extreme that they name: `loads`: entry [v, o, m] is the number of candidates that owner (v, o) hands to matcher (m, o). Owner (v, o) holds as many candidates as its row sums to, at most 15, and in every orient column one owner holds exactly 15. Every matcher receives exactly 8 candidates. Some entry equals 2.
All inputs are finite; a program needn't handle non-finite values.
Results may differ from the reference program's by a relative error of at most 0.0064.
Values may be sent and summed in bfloat16 or wider, within the bound.
No kernel may reach another device: no remote copies, remote signals or barrier semaphores. Data moves between devices by JAX's collectives and lax.ppermute only.
A program may use at most 128 MiB of HBM per device.

```python
import math
import jax
import jax.numpy as jnp
from jax import lax

BOX = 64
TMPL = 32
SHIFT = 8
HALF = 33
BZ = 80
BY = 128
BX = 256
ORIENT = 4
LIVE = 8
OWN = 15
N_VOL = 8
N_ORIENT = 4


def draw_tomogram(key, part):
    grid_shape = (N_VOL * BZ, N_ORIENT * BY, BX)
    sub_keys = jax.random.split(key, 4)
    noise_field = jax.random.truncated_normal(sub_keys[0], -4.0, 4.0, grid_shape, jnp.float32)
    log_top = math.log(10.0) / 3.0
    along_z = jax.random.uniform(sub_keys[1], (grid_shape[0], 1, 1), jnp.float32, 0.0, log_top)
    along_y = jax.random.uniform(sub_keys[2], (1, grid_shape[1], 1), jnp.float32, 0.0, log_top)
    along_x = jax.random.uniform(sub_keys[3], (1, 1, grid_shape[2]), jnp.float32, 0.0, log_top)
    return (noise_field * jnp.exp(along_z + along_y + along_x)).astype(jnp.bfloat16)


def draw_loads(key, part):

    def column(column_key):
        sub_keys = jax.random.split(column_key, 4)
        owner_order = jax.random.permutation(sub_keys[0], N_VOL)
        taken_units = jax.random.randint(sub_keys[1], (N_VOL,), 0, LIVE)
        rank_index = jnp.arange(N_VOL)
        group_pos = rank_index % 2
        taken_units = jnp.where((rank_index < 2) & (group_pos > 0), LIVE - 1, taken_units)
        taken_units = jnp.where(group_pos == 0, 0, taken_units)
        group_total = jnp.repeat(jnp.sum(taken_units.reshape(N_VOL // 2, 2), axis=1), 2)
        by_rank = jnp.where(group_pos == 0, LIVE + group_total, LIVE - taken_units)
        counts = jnp.zeros((N_VOL,), jnp.int32).at[owner_order].set(by_rank.astype(jnp.int32))
        prefix = jnp.cumsum(counts) - counts
        offset = jax.random.randint(sub_keys[2], (), 0, N_VOL)
        relabel = jax.random.permutation(sub_keys[3], N_VOL)
        slot_index = jnp.arange(OWN)
        is_live = slot_index[None, :] < counts[:, None]
        matcher = relabel[(offset + prefix[:, None] + slot_index[None, :]) % N_VOL]
        hit_table = (matcher[:, :, None] == jnp.arange(N_VOL)[None, None, :]) & is_live[:, :, None]
        return jnp.sum(hit_table.astype(jnp.int32), axis=1)
    columns = jax.vmap(column)(jax.random.split(key, N_ORIENT))
    return jnp.transpose(columns, (1, 0, 2)).astype(jnp.int32)


def plant(entries, rng, smallest, top_value):
    longest = entries.shape.index(max(entries.shape))
    spots = []
    for shift in (0, 1):
        where = [jax.random.randint(jax.random.fold_in(rng, axis), (), 0, length) for axis, length in enumerate(entries.shape)]
        where[longest] = (where[longest] + shift) % entries.shape[longest]
        spots.append(tuple(where))
    return entries.at[spots[0]].set(smallest).at[spots[1]].set(top_value)


def level_of(rng, extent, pieces, smallest, top_value):
    gain = 1.0
    for axis_at, blocks in pieces:
        steps = jax.random.uniform(jax.random.fold_in(jax.random.fold_in(rng, 6), axis_at), (blocks,), jnp.float32, smallest / len(pieces), top_value / len(pieces))
        gain = gain * jnp.repeat(jnp.exp(steps), extent[axis_at] // blocks).reshape((-1,) + (1,) * (len(extent) - 1 - axis_at))
    return gain


def setup_inputs(seed: int = 0) -> dict:
    streams_of = jax.random.split(jax.random.key(seed), 7)
    return {
        "tomogram": draw_tomogram(jax.random.fold_in(streams_of[6], 71), 0),
        "templates": jnp.clip(5.0 * jax.random.uniform(streams_of[1], (ORIENT, TMPL, TMPL * TMPL), jnp.float32) ** level_of(streams_of[1], (ORIENT, TMPL, TMPL * TMPL), ((0, 4),), -0.2, 0.2), 0.0, 5.0).astype(jnp.bfloat16),
        "corner_z": plant(jax.random.randint(streams_of[2], (N_VOL, N_ORIENT * OWN), 0, BZ - BOX + 1), jax.random.fold_in(streams_of[2], 1), 0, BZ - BOX).astype(jnp.int32),
        "corner_y": plant(jax.random.randint(streams_of[3], (N_VOL, N_ORIENT * OWN), 0, BY - BOX + 1), jax.random.fold_in(streams_of[3], 1), 0, BY - BOX).astype(jnp.int32),
        "corner_x": plant(jax.random.randint(streams_of[4], (N_VOL, N_ORIENT * OWN), 0, BX - BOX + 1), jax.random.fold_in(streams_of[4], 1), 0, BX - BOX).astype(jnp.int32),
        "loads": draw_loads(jax.random.fold_in(streams_of[6], 71), 0),
    }


epsilon = 1e-05

def product(pattern, operand_a, operand_b):
    return jnp.einsum(pattern, operand_a, operand_b, precision=lax.Precision.HIGHEST)

def lower_product(pattern, operand_a, operand_b):
    rounded_a = lax.optimization_barrier(operand_a.astype(jnp.bfloat16))
    rounded_b = lax.optimization_barrier(operand_b.astype(jnp.bfloat16))
    return jnp.einsum(pattern, rounded_a.astype(jnp.float32), rounded_b.astype(jnp.float32), precision=lax.Precision.HIGHEST)

def shift_anchor():
    return (BOX - TMPL) // 2 - SHIFT // 2

def phases(count_out, count_in, offset):
    out_index = jnp.arange(count_out, dtype=jnp.int32) + offset
    in_index = jnp.arange(count_in, dtype=jnp.int32)
    turn_index = out_index[:, None] * in_index[None, :] % BOX
    phase_angle = turn_index.astype(jnp.float32) * (2.0 * math.pi / BOX)
    return (jnp.cos(phase_angle), jnp.sin(phase_angle))

def forward(volume):
    length = volume.shape[0]
    cos_full, sin_full = phases(BOX, length, 0)
    cos_half, sin_half = phases(HALF, length, 0)
    real_a = lower_product('abx,kx->abk', volume, cos_full)
    imag_a = -lower_product('abx,kx->abk', volume, sin_full)
    real_b = lower_product('ayk,jy->ajk', real_a, cos_full) + lower_product('ayk,jy->ajk', imag_a, sin_full)
    imag_b = lower_product('ayk,jy->ajk', imag_a, cos_full) - lower_product('ayk,jy->ajk', real_a, sin_full)
    real_c = lower_product('xjk,hx->hjk', real_b, cos_half) + lower_product('xjk,hx->hjk', imag_b, sin_half)
    imag_c = lower_product('xjk,hx->hjk', imag_b, cos_half) - lower_product('xjk,hx->hjk', real_b, sin_half)
    return jnp.stack([real_c, imag_c])

def template_spectrum(flat_cube):
    volume = flat_cube.astype(jnp.float32).reshape(TMPL, TMPL, TMPL)
    centred = volume - jnp.mean(volume)
    unit_cube = centred / jnp.sqrt(jnp.mean(centred * centred) + epsilon)
    return forward(unit_cube).astype(jnp.bfloat16)

def band_table():
    lower_edge = jnp.arange(SHIFT, dtype=jnp.int32)[:, None] + shift_anchor()
    cell_index = jnp.arange(BOX, dtype=jnp.int32)[None, :]
    return ((cell_index >= lower_edge) & (cell_index < lower_edge + TMPL)).astype(jnp.float32)

def window_rms(volume):
    window_band = band_table()
    squares = volume * volume
    sums_a = product('abc,sa->sbc', squares, window_band)
    sums_b = product('sbc,tb->stc', sums_a, window_band)
    sums_c = product('stc,uc->stu', sums_b, window_band)
    return jnp.sqrt(sums_c / float(TMPL ** 3) + epsilon)

def peaks_of(box_spectra, box_rms, spectrum):
    real_t = spectrum[0].astype(jnp.float32)
    imag_t = spectrum[1].astype(jnp.float32)
    real_v = box_spectra[:, 0]
    imag_v = box_spectra[:, 1]
    real_p = real_t * real_v + imag_t * imag_v
    imag_p = real_t * imag_v - imag_t * real_v
    cos_first, sin_first = phases(SHIFT, HALF, shift_anchor())
    freq_index = jnp.arange(HALF, dtype=jnp.int32)
    weight = jnp.where(freq_index % (BOX // 2) == 0, 1.0, 2.0) / float(BOX ** 3)
    cos_first = cos_first * weight[None, :]
    sin_first = sin_first * weight[None, :]
    real_g = lower_product('chjk,sh->csjk', real_p, cos_first) - lower_product('chjk,sh->csjk', imag_p, sin_first)
    imag_g = lower_product('chjk,sh->csjk', imag_p, cos_first) + lower_product('chjk,sh->csjk', real_p, sin_first)
    cos_rest, sin_rest = phases(SHIFT, BOX, shift_anchor())
    real_h = lower_product('csjk,tj->cstk', real_g, cos_rest) - lower_product('csjk,tj->cstk', imag_g, sin_rest)
    imag_h = lower_product('csjk,tj->cstk', imag_g, cos_rest) + lower_product('csjk,tj->cstk', real_g, sin_rest)
    correlation = lower_product('cstk,uk->cstu', real_h, cos_rest) - lower_product('cstk,uk->cstu', imag_h, sin_rest)
    scores = correlation / (box_rms * math.sqrt(float(TMPL ** 3)))
    return lax.optimization_barrier(jnp.max(scores, axis=(1, 2, 3)))

def reference(tomogram, templates, corner_z, corner_y, corner_x, loads):
    spectra = lax.map(template_spectrum, templates)
    live_count = lax.optimization_barrier(jnp.sum(loads, axis=2))
    slot_index = jnp.arange(N_ORIENT * OWN, dtype=jnp.int32)
    column = slot_index // OWN
    within = slot_index % OWN
    is_live = within[None, :] < live_count[:, column]
    vol_at = jnp.broadcast_to(jnp.arange(N_VOL, dtype=jnp.int32)[:, None], is_live.shape)
    col_at = jnp.broadcast_to(column[None, :], is_live.shape)
    slot_items = (corner_z.reshape(-1), corner_y.reshape(-1), corner_x.reshape(-1), vol_at.reshape(-1), col_at.reshape(-1), is_live.reshape(-1))

    def match_slot(item):
        along_z, along_y, along_x, vol_here, col_here, alive = item

        def compute_peaks(unused):
            box_cube = lax.dynamic_slice(tomogram, ((vol_here * BZ + along_z).astype(jnp.int32), (col_here * BY + along_y).astype(jnp.int32), along_x.astype(jnp.int32)), (BOX, BOX, BOX))
            volume = box_cube.astype(jnp.float32)
            spectrum = forward(volume)
            rms_here = window_rms(volume)
            return lax.map(lambda tspec: peaks_of(spectrum[None], rms_here[None], tspec)[0], spectra)

        def skip_peaks(unused):
            return jnp.zeros((ORIENT,), jnp.float32)
        return lax.cond(alive, compute_peaks, skip_peaks, 0)
    peak_table = lax.map(match_slot, slot_items).reshape(N_VOL, N_ORIENT * OWN, ORIENT)
    return (peak_table, lax.optimization_barrier(jnp.max(peak_table, axis=2)))
```

```python
import math

import jax
import jax.numpy as jnp
from jax import lax
from jax.sharding import PartitionSpec as P

BOX = 64
TMPL = 32
SHIFT = 8
HALF = 33


epsilon = 1e-05


def shift_anchor():
    return (BOX - TMPL) // 2 - SHIFT // 2


def angle_of(turn_index):
    return turn_index.astype(jnp.float32) * (2.0 * math.pi / BOX)


def phases(count_out, count_in, offset):
    out_index = jnp.arange(count_out, dtype=jnp.int32) + offset
    in_index = jnp.arange(count_in, dtype=jnp.int32)
    turn_index = out_index[:, None] * in_index[None, :] % BOX
    phase_angle = angle_of(turn_index)
    return (jnp.cos(phase_angle), jnp.sin(phase_angle))


def bf(x):
    return x.astype(jnp.bfloat16)


def complex_table(cos_t, sin_t, sign_re_from_im, sign_im_from_re):
    c = bf(cos_t).T
    s = bf(sin_t).T
    re_row = jnp.stack([c, sign_im_from_re * s], axis=1)
    im_row = jnp.stack([sign_re_from_im * s, c], axis=1)
    return jnp.stack([re_row, im_row], axis=0)


def section(pattern, operand, table):
    return jnp.einsum(pattern, bf(operand), table, preferred_element_type=jnp.float32)


def forward_tail(stage_one):
    length_a = stage_one.shape[2]
    length_y = stage_one.shape[3]
    cos_full, sin_full = phases(BOX, length_y, 0)
    t_mid = complex_table(cos_full, sin_full, 1.0, -1.0)
    stage_two = section("ncayk,cydj->ndajk", stage_one, t_mid)
    cos_half, sin_half = phases(HALF, length_a, 0)
    t_first = complex_table(cos_half, sin_half, 1.0, -1.0)
    return section("ncajk,cadh->ndhjk", stage_two, t_first)


def template_spectra(cubes):
    volume = cubes.astype(jnp.float32)
    count = volume.shape[0]
    flat = volume.reshape(count, -1)
    centred = flat - jnp.mean(flat, axis=1, keepdims=True)
    unit = centred / jnp.sqrt(jnp.mean(centred * centred, axis=1, keepdims=True) + epsilon)
    unit = unit.reshape(count, TMPL, TMPL, TMPL)
    cos_full, sin_full = phases(BOX, TMPL, 0)
    t_last = jnp.stack([bf(cos_full).T, -bf(sin_full).T], axis=1)
    stage_one = section("nabx,xck->ncabk", unit, t_last)
    return bf(forward_tail(stage_one))


def window_table(corner_x, width):
    pos = jnp.arange(width, dtype=jnp.int32)[None, :] - corner_x[:, None]
    inside = (pos >= 0) & (pos < BOX)
    k = jnp.arange(BOX, dtype=jnp.int32)
    turn = k[None, None, :] * pos[:, :, None] % BOX
    phase_angle = angle_of(turn)
    mask = inside[:, :, None]
    cos_t = jnp.where(mask, bf(jnp.cos(phase_angle)), jnp.zeros((), jnp.bfloat16))
    sin_t = jnp.where(mask, -bf(jnp.sin(phase_angle)), jnp.zeros((), jnp.bfloat16))
    return jnp.stack([cos_t, sin_t], axis=2)


def band_table():
    lower_edge = jnp.arange(SHIFT, dtype=jnp.int32)[:, None] + shift_anchor()
    cell_index = jnp.arange(BOX, dtype=jnp.int32)[None, :]
    return ((cell_index >= lower_edge) & (cell_index < lower_edge + TMPL)).astype(jnp.float32)


def window_band(corner_x, width):
    lower_edge = jnp.arange(SHIFT, dtype=jnp.int32)[None, :, None] + shift_anchor() + corner_x[:, None, None]
    cell_index = jnp.arange(width, dtype=jnp.int32)[None, None, :]
    return ((cell_index >= lower_edge) & (cell_index < lower_edge + TMPL)).astype(jnp.float32)


def window_rms(rows, corner_x):
    width = rows.shape[-1]
    squares = rows.astype(jnp.float32) ** 2
    band_x = window_band(corner_x, width)
    band = band_table()
    hi = lax.Precision.HIGHEST
    sums_c = jnp.einsum("nabx,nux->nabu", squares, band_x, precision=hi)
    sums_b = jnp.einsum("nabu,tb->natu", sums_c, band, precision=hi)
    sums_a = jnp.einsum("natu,sa->nstu", sums_b, band, precision=hi)
    return jnp.sqrt(sums_a / float(TMPL**3) + epsilon)


def match(box_spectra, box_rms, spectra):
    values = lax.map(lambda one: match_one(box_spectra, box_rms, one[None]), spectra)
    return values[:, :, 0].T


def match_one(box_spectra, box_rms, spectra):
    real_t = spectra[:, 0].astype(jnp.float32)[None]
    imag_t = spectra[:, 1].astype(jnp.float32)[None]
    real_v = box_spectra[:, 0][:, None]
    imag_v = box_spectra[:, 1][:, None]
    real_p = real_t * real_v + imag_t * imag_v
    imag_p = real_t * imag_v - imag_t * real_v
    cross = jnp.stack([bf(real_p), bf(imag_p)], axis=2)
    cos_first, sin_first = phases(SHIFT, HALF, shift_anchor())
    freq_index = jnp.arange(HALF, dtype=jnp.int32)
    weight = jnp.where(freq_index % (BOX // 2) == 0, 1.0, 2.0) / float(BOX**3)
    cos_first = cos_first * weight[None, :]
    sin_first = sin_first * weight[None, :]
    t_first = complex_table(cos_first, sin_first, -1.0, 1.0)
    stage_g = section("nrchjk,chds->nrdsjk", cross, t_first)
    cos_rest, sin_rest = phases(SHIFT, BOX, shift_anchor())
    t_mid = complex_table(cos_rest, sin_rest, -1.0, 1.0)
    stage_h = section("nrcsjk,cjdt->nrdstk", stage_g, t_mid)
    t_last = jnp.stack([bf(cos_rest).T, -bf(sin_rest).T], axis=0)
    correlation = section("nrcstk,cku->nrstu", stage_h, t_last)
    scores = correlation / (box_rms[:, None] * math.sqrt(float(TMPL**3)))
    return jnp.max(scores, axis=(2, 3, 4))


def per_device(tomogram, templates, corner_z, corner_y, corner_x, loads):
    own_total = corner_z.shape[1]
    live_count = jnp.sum(loads[0, 0])
    width = tomogram.shape[2]

    def rows_of(cz, cy):
        return lax.dynamic_slice(tomogram, (cz, cy, 0), (BOX, BOX, width))

    rows = jax.vmap(rows_of)(corner_z[0], corner_y[0])
    t_last = window_table(corner_x[0], width)
    stage_one = jnp.einsum("nabx,nxck->ncabk", rows, t_last, preferred_element_type=jnp.float32)
    box_spectra = forward_tail(stage_one)
    box_rms = window_rms(rows, corner_x[0])

    all_templates = lax.all_gather(templates, "orient", axis=0, tiled=True)
    spectra = template_spectra(all_templates.reshape(-1, TMPL, TMPL, TMPL))
    values = match(box_spectra, box_rms, spectra)
    live = jnp.arange(own_total, dtype=jnp.int32) < live_count
    matched = jnp.where(live[:, None], values, 0.0)
    return (matched[None], jnp.max(matched, axis=1)[None])


def solution(mesh):
    return jax.shard_map(
        per_device,
        mesh=mesh,
        in_specs=(
            P("vol", "orient", None),
            P("orient", None, None),
            P("vol", "orient"),
            P("vol", "orient"),
            P("vol", "orient"),
            P("vol", "orient", None),
        ),
        out_specs=(P("vol", "orient", None), P("vol", "orient")),
        check_vma=False,
    )
```

```python
import math

import jax
import jax.numpy as jnp
from jax import lax
from jax.sharding import PartitionSpec as P
from jax.experimental import pallas as pl
from jax.experimental.pallas import tpu as pltpu

BOX = 64
TMPL = 32
SHIFT = 8
HALF = 33


epsilon = 1e-05


def shift_anchor():
    return (BOX - TMPL) // 2 - SHIFT // 2


def angle_of(turn_index):
    return turn_index.astype(jnp.float32) * (2.0 * math.pi / BOX)


def phases(count_out, count_in, offset):
    out_index = jnp.arange(count_out, dtype=jnp.int32) + offset
    in_index = jnp.arange(count_in, dtype=jnp.int32)
    turn_index = out_index[:, None] * in_index[None, :] % BOX
    phase_angle = angle_of(turn_index)
    return (jnp.cos(phase_angle), jnp.sin(phase_angle))


def bf(x):
    return x.astype(jnp.bfloat16)


def complex_table(cos_t, sin_t, sign_re_from_im, sign_im_from_re):
    c = bf(cos_t).T
    s = bf(sin_t).T
    re_row = jnp.stack([c, sign_im_from_re * s], axis=1)
    im_row = jnp.stack([sign_re_from_im * s, c], axis=1)
    return jnp.stack([re_row, im_row], axis=0)


def section(pattern, operand, table):
    return jnp.einsum(pattern, bf(operand), table, preferred_element_type=jnp.float32)


def forward_tail(stage_one):
    length_a = stage_one.shape[2]
    length_y = stage_one.shape[3]
    cos_full, sin_full = phases(BOX, length_y, 0)
    t_mid = complex_table(cos_full, sin_full, 1.0, -1.0)
    stage_two = section("ncayk,cydj->ndajk", stage_one, t_mid)
    cos_half, sin_half = phases(HALF, length_a, 0)
    t_first = complex_table(cos_half, sin_half, 1.0, -1.0)
    return section("ncajk,cadh->ndhjk", stage_two, t_first)


def template_spectra(cubes):
    volume = cubes.astype(jnp.float32)
    count = volume.shape[0]
    flat = volume.reshape(count, -1)
    centred = flat - jnp.mean(flat, axis=1, keepdims=True)
    unit = centred / jnp.sqrt(jnp.mean(centred * centred, axis=1, keepdims=True) + epsilon)
    unit = unit.reshape(count, TMPL, TMPL, TMPL)
    cos_full, sin_full = phases(BOX, TMPL, 0)
    t_last = jnp.stack([bf(cos_full).T, -bf(sin_full).T], axis=1)
    stage_one = section("nabx,xck->ncabk", unit, t_last)
    return bf(forward_tail(stage_one))


def window_table(corner_x, width):
    pos = jnp.arange(width, dtype=jnp.int32)[None, :] - corner_x[:, None]
    inside = (pos >= 0) & (pos < BOX)
    k = jnp.arange(BOX, dtype=jnp.int32)
    turn = k[None, None, :] * pos[:, :, None] % BOX
    phase_angle = angle_of(turn)
    mask = inside[:, :, None]
    cos_t = jnp.where(mask, bf(jnp.cos(phase_angle)), jnp.zeros((), jnp.bfloat16))
    sin_t = jnp.where(mask, -bf(jnp.sin(phase_angle)), jnp.zeros((), jnp.bfloat16))
    return jnp.stack([cos_t, sin_t], axis=2)


def band_table():
    lower_edge = jnp.arange(SHIFT, dtype=jnp.int32)[:, None] + shift_anchor()
    cell_index = jnp.arange(BOX, dtype=jnp.int32)[None, :]
    return ((cell_index >= lower_edge) & (cell_index < lower_edge + TMPL)).astype(jnp.float32)


def window_band(corner_x, width):
    lower_edge = jnp.arange(SHIFT, dtype=jnp.int32)[None, :, None] + shift_anchor() + corner_x[:, None, None]
    cell_index = jnp.arange(width, dtype=jnp.int32)[None, None, :]
    return ((cell_index >= lower_edge) & (cell_index < lower_edge + TMPL)).astype(jnp.float32)


def window_rms(rows, corner_x):
    width = rows.shape[-1]
    squares = rows.astype(jnp.float32) ** 2
    band_x = window_band(corner_x, width)
    band = band_table()
    hi = lax.Precision.HIGHEST
    sums_c = jnp.einsum("nabx,nux->nabu", squares, band_x, precision=hi)
    sums_b = jnp.einsum("nabu,tb->natu", sums_c, band, precision=hi)
    sums_a = jnp.einsum("natu,sa->nstu", sums_b, band, precision=hi)
    return jnp.sqrt(sums_a / float(TMPL**3) + epsilon)


def match(box_spectra, box_rms, spectra):
    values = lax.map(lambda one: match_one(box_spectra, box_rms, one[None]), spectra)
    return values[:, :, 0].T


def match_one(box_spectra, box_rms, spectra):
    real_t = spectra[:, 0].astype(jnp.float32)[None]
    imag_t = spectra[:, 1].astype(jnp.float32)[None]
    real_v = box_spectra[:, 0][:, None]
    imag_v = box_spectra[:, 1][:, None]
    real_p = real_t * real_v + imag_t * imag_v
    imag_p = real_t * imag_v - imag_t * real_v
    cross = jnp.stack([bf(real_p), bf(imag_p)], axis=2)
    cos_first, sin_first = phases(SHIFT, HALF, shift_anchor())
    freq_index = jnp.arange(HALF, dtype=jnp.int32)
    weight = jnp.where(freq_index % (BOX // 2) == 0, 1.0, 2.0) / float(BOX**3)
    cos_first = cos_first * weight[None, :]
    sin_first = sin_first * weight[None, :]
    t_first = complex_table(cos_first, sin_first, -1.0, 1.0)
    stage_g = section("nrchjk,chds->nrdsjk", cross, t_first)
    cos_rest, sin_rest = phases(SHIFT, BOX, shift_anchor())
    t_mid = complex_table(cos_rest, sin_rest, -1.0, 1.0)
    stage_h = section("nrcsjk,cjdt->nrdstk", stage_g, t_mid)
    t_last = jnp.stack([bf(cos_rest).T, -bf(sin_rest).T], axis=0)
    correlation = section("nrcstk,cku->nrstu", stage_h, t_last)
    scores = correlation / (box_rms[:, None] * math.sqrt(float(TMPL**3)))
    return jnp.max(scores, axis=(2, 3, 4))


def front_kernel(cz_ref, slab_ref, t1_ref, l2_ref, ymask_ref, bxt_ref, q2_ref, rsum_ref, w_scr, y_scr):
    depth, rows_y, width = slab_ref.shape
    chunk = 8
    t1 = t1_ref[...]
    l2 = l2_ref[...]

    def transform_chunk(ci, carry):
        z0 = pl.multiple_of(ci * chunk, chunk)
        rows = slab_ref[pl.ds(z0, chunk)].reshape(chunk * rows_y, width)
        p1 = jnp.dot(rows, t1, preferred_element_type=jnp.float32)
        p1 = p1.astype(jnp.bfloat16).astype(jnp.float32).reshape(chunk, rows_y, 2 * BOX)
        p1t = jnp.swapaxes(p1, 1, 2).reshape(chunk * 2 * BOX, rows_y).astype(jnp.bfloat16)
        m2 = jnp.dot(p1t, l2, preferred_element_type=jnp.float32).reshape(chunk, 2, BOX, 2 * BOX)
        part_a = m2[:, 0]
        part_b = m2[:, 1]
        lane = lax.broadcasted_iota(jnp.int32, part_a.shape, 2)
        sign = jnp.where(lane < BOX, 1.0, -1.0).astype(jnp.float32)
        out = pltpu.roll(part_b, BOX, 2) + sign * part_a
        q2_ref[pl.ds(z0, chunk)] = out.astype(jnp.bfloat16)
        return carry

    lax.fori_loop(0, depth // chunk, transform_chunk, 0)

    lo_z = shift_anchor()

    def plane_sq(z):
        v = slab_ref[z].astype(jnp.float32)
        return v * v

    def first_window(z, acc):
        return acc + plane_sq(lo_z + z)

    acc = lax.fori_loop(0, TMPL, first_window, jnp.zeros((rows_y, width), jnp.float32))
    w_scr[0] = acc
    for s_i in range(1, SHIFT):
        acc = acc + plane_sq(lo_z + TMPL + s_i - 1) - plane_sq(lo_z + s_i - 1)
        w_scr[s_i] = acc

    ymask = ymask_ref[...]

    def y_sums(s_i, carry):
        plane = w_scr[s_i]
        for t_i in range(SHIFT):
            y_scr[pl.ds(s_i * SHIFT + t_i, 1), :] = jnp.sum(plane * ymask[:, t_i:t_i + 1], axis=0, keepdims=True)
        return carry

    lax.fori_loop(0, SHIFT, y_sums, 0)
    ysum = y_scr[...]
    hi = ysum.astype(jnp.bfloat16)
    rest = ysum - hi.astype(jnp.float32)
    mid = rest.astype(jnp.bfloat16)
    lo = (rest - mid.astype(jnp.float32)).astype(jnp.bfloat16)
    bxt = bxt_ref[...]
    total = jnp.dot(hi, bxt, preferred_element_type=jnp.float32)
    total = total + jnp.dot(mid, bxt, preferred_element_type=jnp.float32)
    total = total + jnp.dot(lo, bxt, preferred_element_type=jnp.float32)
    rsum_ref[...] = total


def front(tomogram, corner_z, corner_y, corner_x):
    count = corner_z.shape[0]
    rows_y = tomogram.shape[1]
    width = tomogram.shape[2]
    t1 = window_table(corner_x, width).reshape(count, width, 2 * BOX)
    pos_y = jnp.arange(rows_y, dtype=jnp.int32)[None, :] - corner_y[:, None]
    inside_y = (pos_y >= 0) & (pos_y < BOX)
    j = jnp.arange(BOX, dtype=jnp.int32)
    turn_y = pos_y[:, :, None] * j[None, None, :] % BOX
    angle_y = angle_of(turn_y)
    zero = jnp.zeros((), jnp.bfloat16)
    cos_y = jnp.where(inside_y[:, :, None], bf(jnp.cos(angle_y)), zero)
    sin_y = jnp.where(inside_y[:, :, None], bf(jnp.sin(angle_y)), zero)
    l2 = jnp.concatenate([cos_y, sin_y], axis=2)
    lower_y = jnp.arange(SHIFT, dtype=jnp.int32)[None, None, :] + shift_anchor() + corner_y[:, None, None]
    cell_y = jnp.arange(rows_y, dtype=jnp.int32)[None, :, None]
    ymask = ((cell_y >= lower_y) & (cell_y < lower_y + TMPL)).astype(jnp.float32)
    bxt = jnp.swapaxes(window_band(corner_x, width), 1, 2).astype(jnp.bfloat16)

    grid_spec = pltpu.PrefetchScalarGridSpec(
        num_scalar_prefetch=1,
        grid=(count,),
        in_specs=[
            pl.BlockSpec((pl.Element(BOX), pl.Element(rows_y), pl.Element(width)), lambda n, cz: (cz[n], 0, 0)),
            pl.BlockSpec((None, width, 2 * BOX), lambda n, cz: (n, 0, 0)),
            pl.BlockSpec((None, rows_y, 2 * BOX), lambda n, cz: (n, 0, 0)),
            pl.BlockSpec((None, rows_y, SHIFT), lambda n, cz: (n, 0, 0)),
            pl.BlockSpec((None, width, SHIFT), lambda n, cz: (n, 0, 0)),
        ],
        out_specs=[
            pl.BlockSpec((None, BOX, BOX, 2 * BOX), lambda n, cz: (n, 0, 0, 0)),
            pl.BlockSpec((None, SHIFT * SHIFT, SHIFT), lambda n, cz: (n, 0, 0)),
        ],
        scratch_shapes=[
            pltpu.VMEM((SHIFT, rows_y, width), jnp.float32),
            pltpu.VMEM((SHIFT * SHIFT, width), jnp.float32),
        ],
    )
    q2, rsum = pl.pallas_call(
        front_kernel,
        grid_spec=grid_spec,
        out_shape=[
            jax.ShapeDtypeStruct((count, BOX, BOX, 2 * BOX), jnp.bfloat16),
            jax.ShapeDtypeStruct((count, SHIFT * SHIFT, SHIFT), jnp.float32),
        ],
        compiler_params=pltpu.CompilerParams(vmem_limit_bytes=48 * 1024 * 1024),
    )(corner_z, tomogram, t1, l2, ymask, bxt)
    box_rms = jnp.sqrt(rsum.reshape(count, SHIFT, SHIFT, SHIFT) / float(TMPL**3) + epsilon)
    return q2, box_rms


def box_spectra_of(q2):
    cos_half, sin_half = phases(HALF, BOX, 0)
    l3 = jnp.concatenate([bf(cos_half), bf(sin_half)], axis=0)
    m3 = jnp.einsum("nzkq,wz->nwkq", q2, l3, preferred_element_type=jnp.float32)
    top = m3[:, :HALF]
    bottom = m3[:, HALF:]
    real = top[..., :BOX] + bottom[..., BOX:]
    imag = top[..., BOX:] - bottom[..., :BOX]
    return real, imag


def match_kj(real_v, imag_v, box_rms, spectra):
    spectra_kj = jnp.swapaxes(spectra, 3, 4)

    def one(spectrum):
        real_t = spectrum[0].astype(jnp.float32)[None, None]
        imag_t = spectrum[1].astype(jnp.float32)[None, None]
        rv = real_v[:, None]
        iv = imag_v[:, None]
        real_p = real_t * rv + imag_t * iv
        imag_p = real_t * iv - imag_t * rv
        cross = jnp.stack([bf(real_p), bf(imag_p)], axis=2)
        cos_first, sin_first = phases(SHIFT, HALF, shift_anchor())
        freq_index = jnp.arange(HALF, dtype=jnp.int32)
        weight = jnp.where(freq_index % (BOX // 2) == 0, 1.0, 2.0) / float(BOX**3)
        t_first = complex_table(cos_first * weight[None, :], sin_first * weight[None, :], -1.0, 1.0)
        stage_g = section("nrchkj,chds->nrdskj", cross, t_first)
        cos_rest, sin_rest = phases(SHIFT, BOX, shift_anchor())
        t_mid = complex_table(cos_rest, sin_rest, -1.0, 1.0)
        stage_h = section("nrcskj,cjdt->nrdskt", stage_g, t_mid)
        t_last = jnp.stack([bf(cos_rest).T, -bf(sin_rest).T], axis=0)
        correlation = section("nrcskt,cku->nrstu", stage_h, t_last)
        scores = correlation / (box_rms[:, None] * math.sqrt(float(TMPL**3)))
        return jnp.max(scores, axis=(2, 3, 4))[:, 0]

    values = lax.map(one, spectra_kj)
    return values.T


def per_device(tomogram, templates, corner_z, corner_y, corner_x, loads):
    own_total = corner_z.shape[1]
    live_count = jnp.sum(loads[0, 0])
    q2, box_rms = front(tomogram, corner_z[0], corner_y[0], corner_x[0])
    real_v, imag_v = box_spectra_of(q2)

    all_templates = lax.all_gather(templates, "orient", axis=0, tiled=True)
    spectra = template_spectra(all_templates.reshape(-1, TMPL, TMPL, TMPL))
    values = match_kj(real_v, imag_v, box_rms, spectra)
    live = jnp.arange(own_total, dtype=jnp.int32) < live_count
    matched = jnp.where(live[:, None], values, 0.0)
    return (matched[None], jnp.max(matched, axis=1)[None])


def solution(mesh):
    return jax.shard_map(
        per_device,
        mesh=mesh,
        in_specs=(
            P("vol", "orient", None),
            P("orient", None, None),
            P("vol", "orient"),
            P("vol", "orient"),
            P("vol", "orient"),
            P("vol", "orient", None),
        ),
        out_specs=(P("vol", "orient", None), P("vol", "orient")),
        check_vma=False,
    )
```

```python
import math

import jax
import jax.numpy as jnp
from jax import lax
from jax.sharding import PartitionSpec as P
from jax.experimental import pallas as pl
from jax.experimental.pallas import tpu as pltpu

BOX = 64
TMPL = 32
SHIFT = 8
HALF = 33


epsilon = 1e-05


def shift_anchor():
    return (BOX - TMPL) // 2 - SHIFT // 2


def angle_of(turn_index):
    return turn_index.astype(jnp.float32) * (2.0 * math.pi / BOX)


def phases(count_out, count_in, offset):
    out_index = jnp.arange(count_out, dtype=jnp.int32) + offset
    in_index = jnp.arange(count_in, dtype=jnp.int32)
    turn_index = out_index[:, None] * in_index[None, :] % BOX
    phase_angle = angle_of(turn_index)
    return (jnp.cos(phase_angle), jnp.sin(phase_angle))


def bf(x):
    return x.astype(jnp.bfloat16)


def complex_table(cos_t, sin_t, sign_re_from_im, sign_im_from_re):
    c = bf(cos_t).T
    s = bf(sin_t).T
    re_row = jnp.stack([c, sign_im_from_re * s], axis=1)
    im_row = jnp.stack([sign_re_from_im * s, c], axis=1)
    return jnp.stack([re_row, im_row], axis=0)


def section(pattern, operand, table):
    return jnp.einsum(pattern, bf(operand), table, preferred_element_type=jnp.float32)


def forward_tail(stage_one):
    length_a = stage_one.shape[2]
    length_y = stage_one.shape[3]
    cos_full, sin_full = phases(BOX, length_y, 0)
    t_mid = complex_table(cos_full, sin_full, 1.0, -1.0)
    stage_two = section("ncayk,cydj->ndajk", stage_one, t_mid)
    cos_half, sin_half = phases(HALF, length_a, 0)
    t_first = complex_table(cos_half, sin_half, 1.0, -1.0)
    return section("ncajk,cadh->ndhjk", stage_two, t_first)


def template_spectra(cubes):
    volume = cubes.astype(jnp.float32)
    count = volume.shape[0]
    flat = volume.reshape(count, -1)
    centred = flat - jnp.mean(flat, axis=1, keepdims=True)
    unit = centred / jnp.sqrt(jnp.mean(centred * centred, axis=1, keepdims=True) + epsilon)
    unit = unit.reshape(count, TMPL, TMPL, TMPL)
    cos_full, sin_full = phases(BOX, TMPL, 0)
    t_last = jnp.stack([bf(cos_full).T, -bf(sin_full).T], axis=1)
    stage_one = section("nabx,xck->ncabk", unit, t_last)
    return bf(forward_tail(stage_one))


def window_table(corner_x, width):
    pos = jnp.arange(width, dtype=jnp.int32)[None, :] - corner_x[:, None]
    inside = (pos >= 0) & (pos < BOX)
    k = jnp.arange(BOX, dtype=jnp.int32)
    turn = k[None, None, :] * pos[:, :, None] % BOX
    phase_angle = angle_of(turn)
    mask = inside[:, :, None]
    cos_t = jnp.where(mask, bf(jnp.cos(phase_angle)), jnp.zeros((), jnp.bfloat16))
    sin_t = jnp.where(mask, -bf(jnp.sin(phase_angle)), jnp.zeros((), jnp.bfloat16))
    return jnp.stack([cos_t, sin_t], axis=2)


def band_table():
    lower_edge = jnp.arange(SHIFT, dtype=jnp.int32)[:, None] + shift_anchor()
    cell_index = jnp.arange(BOX, dtype=jnp.int32)[None, :]
    return ((cell_index >= lower_edge) & (cell_index < lower_edge + TMPL)).astype(jnp.float32)


def window_band(corner_x, width):
    lower_edge = jnp.arange(SHIFT, dtype=jnp.int32)[None, :, None] + shift_anchor() + corner_x[:, None, None]
    cell_index = jnp.arange(width, dtype=jnp.int32)[None, None, :]
    return ((cell_index >= lower_edge) & (cell_index < lower_edge + TMPL)).astype(jnp.float32)


def window_rms(rows, corner_x):
    width = rows.shape[-1]
    squares = rows.astype(jnp.float32) ** 2
    band_x = window_band(corner_x, width)
    band = band_table()
    hi = lax.Precision.HIGHEST
    sums_c = jnp.einsum("nabx,nux->nabu", squares, band_x, precision=hi)
    sums_b = jnp.einsum("nabu,tb->natu", sums_c, band, precision=hi)
    sums_a = jnp.einsum("natu,sa->nstu", sums_b, band, precision=hi)
    return jnp.sqrt(sums_a / float(TMPL**3) + epsilon)


def match(box_spectra, box_rms, spectra):
    values = lax.map(lambda one: match_one(box_spectra, box_rms, one[None]), spectra)
    return values[:, :, 0].T


def match_one(box_spectra, box_rms, spectra):
    real_t = spectra[:, 0].astype(jnp.float32)[None]
    imag_t = spectra[:, 1].astype(jnp.float32)[None]
    real_v = box_spectra[:, 0][:, None]
    imag_v = box_spectra[:, 1][:, None]
    real_p = real_t * real_v + imag_t * imag_v
    imag_p = real_t * imag_v - imag_t * real_v
    cross = jnp.stack([bf(real_p), bf(imag_p)], axis=2)
    cos_first, sin_first = phases(SHIFT, HALF, shift_anchor())
    freq_index = jnp.arange(HALF, dtype=jnp.int32)
    weight = jnp.where(freq_index % (BOX // 2) == 0, 1.0, 2.0) / float(BOX**3)
    cos_first = cos_first * weight[None, :]
    sin_first = sin_first * weight[None, :]
    t_first = complex_table(cos_first, sin_first, -1.0, 1.0)
    stage_g = section("nrchjk,chds->nrdsjk", cross, t_first)
    cos_rest, sin_rest = phases(SHIFT, BOX, shift_anchor())
    t_mid = complex_table(cos_rest, sin_rest, -1.0, 1.0)
    stage_h = section("nrcsjk,cjdt->nrdstk", stage_g, t_mid)
    t_last = jnp.stack([bf(cos_rest).T, -bf(sin_rest).T], axis=0)
    correlation = section("nrcstk,cku->nrstu", stage_h, t_last)
    scores = correlation / (box_rms[:, None] * math.sqrt(float(TMPL**3)))
    return jnp.max(scores, axis=(2, 3, 4))


def front_kernel(cz_ref, slab_ref, t1_ref, l2_ref, ymask_ref, bxt_ref, q2_ref, rsum_ref, w_scr, y_scr):
    depth, rows_y, width = slab_ref.shape
    chunk = 8
    t1 = t1_ref[...]
    l2 = l2_ref[...]

    def transform_chunk(ci, carry):
        z0 = pl.multiple_of(ci * chunk, chunk)
        rows = slab_ref[pl.ds(z0, chunk)].reshape(chunk * rows_y, width)
        p1 = jnp.dot(rows, t1, preferred_element_type=jnp.float32)
        p1 = p1.astype(jnp.bfloat16).astype(jnp.float32).reshape(chunk, rows_y, 2 * BOX)
        p1t = jnp.swapaxes(p1, 1, 2).reshape(chunk * 2 * BOX, rows_y).astype(jnp.bfloat16)
        m2 = jnp.dot(p1t, l2, preferred_element_type=jnp.float32).reshape(chunk, 2, BOX, 2 * BOX)
        part_a = m2[:, 0]
        part_b = m2[:, 1]
        lane = lax.broadcasted_iota(jnp.int32, part_a.shape, 2)
        sign = jnp.where(lane < BOX, 1.0, -1.0).astype(jnp.float32)
        out = (pltpu.roll(part_b, BOX, 2) + sign * part_a).astype(jnp.bfloat16).astype(jnp.float32)
        q2_ref[0, pl.ds(z0, chunk)] = out.astype(jnp.bfloat16)
        swapped = sign * pltpu.roll(out, BOX, 2)
        q2_ref[1, pl.ds(z0, chunk)] = swapped.astype(jnp.bfloat16)
        return carry

    lax.fori_loop(0, depth // chunk, transform_chunk, 0)

    lo_z = shift_anchor()

    def plane_sq(z):
        v = slab_ref[z].astype(jnp.float32)
        return v * v

    def first_window(z, acc):
        return acc + plane_sq(lo_z + z)

    acc = lax.fori_loop(0, TMPL, first_window, jnp.zeros((rows_y, width), jnp.float32))
    w_scr[0] = acc
    for s_i in range(1, SHIFT):
        acc = acc + plane_sq(lo_z + TMPL + s_i - 1) - plane_sq(lo_z + s_i - 1)
        w_scr[s_i] = acc

    ymask = ymask_ref[...]

    def y_sums(s_i, carry):
        plane = w_scr[s_i]
        for t_i in range(SHIFT):
            y_scr[pl.ds(s_i * SHIFT + t_i, 1), :] = jnp.sum(plane * ymask[:, t_i:t_i + 1], axis=0, keepdims=True)
        return carry

    lax.fori_loop(0, SHIFT, y_sums, 0)
    ysum = y_scr[...]
    hi = ysum.astype(jnp.bfloat16)
    rest = ysum - hi.astype(jnp.float32)
    mid = rest.astype(jnp.bfloat16)
    lo = (rest - mid.astype(jnp.float32)).astype(jnp.bfloat16)
    bxt = bxt_ref[...]
    total = jnp.dot(hi, bxt, preferred_element_type=jnp.float32)
    total = total + jnp.dot(mid, bxt, preferred_element_type=jnp.float32)
    total = total + jnp.dot(lo, bxt, preferred_element_type=jnp.float32)
    rsum_ref[...] = total


def front(tomogram, corner_z, corner_y, corner_x):
    count = corner_z.shape[0]
    rows_y = tomogram.shape[1]
    width = tomogram.shape[2]
    t1 = window_table(corner_x, width).reshape(count, width, 2 * BOX)
    pos_y = jnp.arange(rows_y, dtype=jnp.int32)[None, :] - corner_y[:, None]
    inside_y = (pos_y >= 0) & (pos_y < BOX)
    j = jnp.arange(BOX, dtype=jnp.int32)
    turn_y = pos_y[:, :, None] * j[None, None, :] % BOX
    angle_y = angle_of(turn_y)
    zero = jnp.zeros((), jnp.bfloat16)
    cos_y = jnp.where(inside_y[:, :, None], bf(jnp.cos(angle_y)), zero)
    sin_y = jnp.where(inside_y[:, :, None], bf(jnp.sin(angle_y)), zero)
    l2 = jnp.concatenate([cos_y, sin_y], axis=2)
    lower_y = jnp.arange(SHIFT, dtype=jnp.int32)[None, None, :] + shift_anchor() + corner_y[:, None, None]
    cell_y = jnp.arange(rows_y, dtype=jnp.int32)[None, :, None]
    ymask = ((cell_y >= lower_y) & (cell_y < lower_y + TMPL)).astype(jnp.float32)
    bxt = jnp.swapaxes(window_band(corner_x, width), 1, 2).astype(jnp.bfloat16)

    grid_spec = pltpu.PrefetchScalarGridSpec(
        num_scalar_prefetch=1,
        grid=(count,),
        in_specs=[
            pl.BlockSpec((pl.Element(BOX), pl.Element(rows_y), pl.Element(width)), lambda n, cz: (cz[n], 0, 0)),
            pl.BlockSpec((None, width, 2 * BOX), lambda n, cz: (n, 0, 0)),
            pl.BlockSpec((None, rows_y, 2 * BOX), lambda n, cz: (n, 0, 0)),
            pl.BlockSpec((None, rows_y, SHIFT), lambda n, cz: (n, 0, 0)),
            pl.BlockSpec((None, width, SHIFT), lambda n, cz: (n, 0, 0)),
        ],
        out_specs=[
            pl.BlockSpec((None, 2, BOX, BOX, 2 * BOX), lambda n, cz: (n, 0, 0, 0, 0)),
            pl.BlockSpec((None, SHIFT * SHIFT, SHIFT), lambda n, cz: (n, 0, 0)),
        ],
        scratch_shapes=[
            pltpu.VMEM((SHIFT, rows_y, width), jnp.float32),
            pltpu.VMEM((SHIFT * SHIFT, width), jnp.float32),
        ],
    )
    q2, rsum = pl.pallas_call(
        front_kernel,
        grid_spec=grid_spec,
        out_shape=[
            jax.ShapeDtypeStruct((count, 2, BOX, BOX, 2 * BOX), jnp.bfloat16),
            jax.ShapeDtypeStruct((count, SHIFT * SHIFT, SHIFT), jnp.float32),
        ],
        compiler_params=pltpu.CompilerParams(vmem_limit_bytes=48 * 1024 * 1024),
    )(corner_z, tomogram, t1, l2, ymask, bxt)
    box_rms = jnp.sqrt(rsum.reshape(count, SHIFT, SHIFT, SHIFT) / float(TMPL**3) + epsilon)
    return q2, box_rms


def box_spectra_of(q2):
    cos_half, sin_half = phases(HALF, BOX, 0)
    l3 = jnp.stack([bf(cos_half).T, bf(sin_half).T], axis=0)
    return jnp.einsum("nwzkq,wzh->nhkq", q2, l3, preferred_element_type=jnp.float32)


def match_kj(spectrum_v, box_rms, spectra):
    spectra_kj = jnp.swapaxes(spectra, 3, 4)
    real_v = spectrum_v[..., :BOX]
    imag_v = spectrum_v[..., BOX:]

    def one(spectrum):
        real_t = spectrum[0].astype(jnp.float32)[None, None]
        imag_t = spectrum[1].astype(jnp.float32)[None, None]
        rv = real_v[:, None]
        iv = imag_v[:, None]
        real_p = real_t * rv + imag_t * iv
        imag_p = real_t * iv - imag_t * rv
        cross = jnp.stack([bf(real_p), bf(imag_p)], axis=2)
        cos_first, sin_first = phases(SHIFT, HALF, shift_anchor())
        freq_index = jnp.arange(HALF, dtype=jnp.int32)
        weight = jnp.where(freq_index % (BOX // 2) == 0, 1.0, 2.0) / float(BOX**3)
        t_first = complex_table(cos_first * weight[None, :], sin_first * weight[None, :], -1.0, 1.0)
        stage_g = section("nrchkj,chds->nrdskj", cross, t_first)
        cos_rest, sin_rest = phases(SHIFT, BOX, shift_anchor())
        t_mid = complex_table(cos_rest, sin_rest, -1.0, 1.0)
        stage_h = section("nrcskj,cjdt->nrdskt", stage_g, t_mid)
        t_last = jnp.stack([bf(cos_rest).T, -bf(sin_rest).T], axis=0)
        correlation = section("nrcskt,cku->nrstu", stage_h, t_last)
        scores = correlation / (box_rms[:, None] * math.sqrt(float(TMPL**3)))
        return jnp.max(scores, axis=(2, 3, 4))[:, 0]

    values = lax.map(one, spectra_kj)
    return values.T


def per_device(tomogram, templates, corner_z, corner_y, corner_x, loads):
    own_total = corner_z.shape[1]
    live_count = jnp.sum(loads[0, 0])
    q2, box_rms = front(tomogram, corner_z[0], corner_y[0], corner_x[0])
    spectrum_v = box_spectra_of(q2)

    all_templates = lax.all_gather(templates, "orient", axis=0, tiled=True)
    spectra = template_spectra(all_templates.reshape(-1, TMPL, TMPL, TMPL))
    values = match_kj(spectrum_v, box_rms, spectra)
    live = jnp.arange(own_total, dtype=jnp.int32) < live_count
    matched = jnp.where(live[:, None], values, 0.0)
    return (matched[None], jnp.max(matched, axis=1)[None])


def solution(mesh):
    return jax.shard_map(
        per_device,
        mesh=mesh,
        in_specs=(
            P("vol", "orient", None),
            P("orient", None, None),
            P("vol", "orient"),
            P("vol", "orient"),
            P("vol", "orient"),
            P("vol", "orient", None),
        ),
        out_specs=(P("vol", "orient", None), P("vol", "orient")),
        check_vma=False,
    )
```

```python
import math

import jax
import jax.numpy as jnp
from jax import lax
from jax.sharding import PartitionSpec as P
from jax.experimental import pallas as pl
from jax.experimental.pallas import tpu as pltpu

BOX = 64
TMPL = 32
SHIFT = 8
HALF = 33


epsilon = 1e-05


def shift_anchor():
    return (BOX - TMPL) // 2 - SHIFT // 2


def angle_of(turn_index):
    return turn_index.astype(jnp.float32) * (2.0 * math.pi / BOX)


def phases(count_out, count_in, offset):
    out_index = jnp.arange(count_out, dtype=jnp.int32) + offset
    in_index = jnp.arange(count_in, dtype=jnp.int32)
    turn_index = out_index[:, None] * in_index[None, :] % BOX
    phase_angle = angle_of(turn_index)
    return (jnp.cos(phase_angle), jnp.sin(phase_angle))


def bf(x):
    return x.astype(jnp.bfloat16)


def complex_table(cos_t, sin_t, sign_re_from_im, sign_im_from_re):
    c = bf(cos_t).T
    s = bf(sin_t).T
    re_row = jnp.stack([c, sign_im_from_re * s], axis=1)
    im_row = jnp.stack([sign_re_from_im * s, c], axis=1)
    return jnp.stack([re_row, im_row], axis=0)


def section(pattern, operand, table):
    return jnp.einsum(pattern, bf(operand), table, preferred_element_type=jnp.float32)


def forward_tail(stage_one):
    length_a = stage_one.shape[2]
    length_y = stage_one.shape[3]
    cos_full, sin_full = phases(BOX, length_y, 0)
    t_mid = complex_table(cos_full, sin_full, 1.0, -1.0)
    stage_two = section("ncayk,cydj->ndajk", stage_one, t_mid)
    cos_half, sin_half = phases(HALF, length_a, 0)
    t_first = complex_table(cos_half, sin_half, 1.0, -1.0)
    return section("ncajk,cadh->ndhjk", stage_two, t_first)


def template_spectra(cubes):
    volume = cubes.astype(jnp.float32)
    count = volume.shape[0]
    flat = volume.reshape(count, -1)
    centred = flat - jnp.mean(flat, axis=1, keepdims=True)
    unit = centred / jnp.sqrt(jnp.mean(centred * centred, axis=1, keepdims=True) + epsilon)
    unit = unit.reshape(count, TMPL, TMPL, TMPL)
    cos_full, sin_full = phases(BOX, TMPL, 0)
    t_last = jnp.stack([bf(cos_full).T, -bf(sin_full).T], axis=1)
    stage_one = section("nabx,xck->ncabk", unit, t_last)
    return bf(forward_tail(stage_one))


def window_table(corner_x, width):
    pos = jnp.arange(width, dtype=jnp.int32)[None, :] - corner_x[:, None]
    inside = (pos >= 0) & (pos < BOX)
    k = jnp.arange(BOX, dtype=jnp.int32)
    turn = k[None, None, :] * pos[:, :, None] % BOX
    phase_angle = angle_of(turn)
    mask = inside[:, :, None]
    cos_t = jnp.where(mask, bf(jnp.cos(phase_angle)), jnp.zeros((), jnp.bfloat16))
    sin_t = jnp.where(mask, -bf(jnp.sin(phase_angle)), jnp.zeros((), jnp.bfloat16))
    return jnp.stack([cos_t, sin_t], axis=2)


def band_table():
    lower_edge = jnp.arange(SHIFT, dtype=jnp.int32)[:, None] + shift_anchor()
    cell_index = jnp.arange(BOX, dtype=jnp.int32)[None, :]
    return ((cell_index >= lower_edge) & (cell_index < lower_edge + TMPL)).astype(jnp.float32)


def window_band(corner_x, width):
    lower_edge = jnp.arange(SHIFT, dtype=jnp.int32)[None, :, None] + shift_anchor() + corner_x[:, None, None]
    cell_index = jnp.arange(width, dtype=jnp.int32)[None, None, :]
    return ((cell_index >= lower_edge) & (cell_index < lower_edge + TMPL)).astype(jnp.float32)


def window_rms(rows, corner_x):
    width = rows.shape[-1]
    squares = rows.astype(jnp.float32) ** 2
    band_x = window_band(corner_x, width)
    band = band_table()
    hi = lax.Precision.HIGHEST
    sums_c = jnp.einsum("nabx,nux->nabu", squares, band_x, precision=hi)
    sums_b = jnp.einsum("nabu,tb->natu", sums_c, band, precision=hi)
    sums_a = jnp.einsum("natu,sa->nstu", sums_b, band, precision=hi)
    return jnp.sqrt(sums_a / float(TMPL**3) + epsilon)


def match(box_spectra, box_rms, spectra):
    values = lax.map(lambda one: match_one(box_spectra, box_rms, one[None]), spectra)
    return values[:, :, 0].T


def match_one(box_spectra, box_rms, spectra):
    real_t = spectra[:, 0].astype(jnp.float32)[None]
    imag_t = spectra[:, 1].astype(jnp.float32)[None]
    real_v = box_spectra[:, 0][:, None]
    imag_v = box_spectra[:, 1][:, None]
    real_p = real_t * real_v + imag_t * imag_v
    imag_p = real_t * imag_v - imag_t * real_v
    cross = jnp.stack([bf(real_p), bf(imag_p)], axis=2)
    cos_first, sin_first = phases(SHIFT, HALF, shift_anchor())
    freq_index = jnp.arange(HALF, dtype=jnp.int32)
    weight = jnp.where(freq_index % (BOX // 2) == 0, 1.0, 2.0) / float(BOX**3)
    cos_first = cos_first * weight[None, :]
    sin_first = sin_first * weight[None, :]
    t_first = complex_table(cos_first, sin_first, -1.0, 1.0)
    stage_g = section("nrchjk,chds->nrdsjk", cross, t_first)
    cos_rest, sin_rest = phases(SHIFT, BOX, shift_anchor())
    t_mid = complex_table(cos_rest, sin_rest, -1.0, 1.0)
    stage_h = section("nrcsjk,cjdt->nrdstk", stage_g, t_mid)
    t_last = jnp.stack([bf(cos_rest).T, -bf(sin_rest).T], axis=0)
    correlation = section("nrcstk,cku->nrstu", stage_h, t_last)
    scores = correlation / (box_rms[:, None] * math.sqrt(float(TMPL**3)))
    return jnp.max(scores, axis=(2, 3, 4))


def front_kernel(cz_ref, slab_ref, t1_ref, l2_ref, ymask_ref, bxt_ref, q2_ref, rsum_ref, w_scr, y_scr):
    depth, rows_y, width = slab_ref.shape
    chunk = 8
    t1 = t1_ref[...]
    l2 = l2_ref[...]

    def transform_chunk(ci, carry):
        z0 = pl.multiple_of(ci * chunk, chunk)
        rows = slab_ref[pl.ds(z0, chunk)].reshape(chunk * rows_y, width)
        p1 = jnp.dot(rows, t1, preferred_element_type=jnp.float32)
        p1 = p1.astype(jnp.bfloat16).astype(jnp.float32).reshape(chunk, rows_y, 2 * BOX)
        p1t = jnp.swapaxes(p1, 1, 2).reshape(chunk * 2 * BOX, rows_y).astype(jnp.bfloat16)
        m2 = jnp.dot(p1t, l2, preferred_element_type=jnp.float32).reshape(chunk, 2, BOX, 2 * BOX)
        part_a = m2[:, 0]
        part_b = m2[:, 1]
        lane = lax.broadcasted_iota(jnp.int32, part_a.shape, 2)
        sign = jnp.where(lane < BOX, 1.0, -1.0).astype(jnp.float32)
        out = (pltpu.roll(part_b, BOX, 2) + sign * part_a).astype(jnp.bfloat16).astype(jnp.float32)
        q2_ref[0, pl.ds(z0, chunk)] = out.astype(jnp.bfloat16)
        swapped = sign * pltpu.roll(out, BOX, 2)
        q2_ref[1, pl.ds(z0, chunk)] = swapped.astype(jnp.bfloat16)
        return carry

    lax.fori_loop(0, depth // chunk, transform_chunk, 0)

    lo_z = shift_anchor()

    def plane_sq(z):
        v = slab_ref[z].astype(jnp.float32)
        return v * v

    def first_window(z, acc):
        return acc + plane_sq(lo_z + z)

    acc = lax.fori_loop(0, TMPL, first_window, jnp.zeros((rows_y, width), jnp.float32))
    w_scr[0] = acc
    for s_i in range(1, SHIFT):
        acc = acc + plane_sq(lo_z + TMPL + s_i - 1) - plane_sq(lo_z + s_i - 1)
        w_scr[s_i] = acc

    ymask = ymask_ref[...]

    def y_sums(s_i, carry):
        plane = w_scr[s_i]
        for t_i in range(SHIFT):
            y_scr[pl.ds(s_i * SHIFT + t_i, 1), :] = jnp.sum(plane * ymask[:, t_i:t_i + 1], axis=0, keepdims=True)
        return carry

    lax.fori_loop(0, SHIFT, y_sums, 0)
    ysum = y_scr[...]
    hi = ysum.astype(jnp.bfloat16)
    rest = ysum - hi.astype(jnp.float32)
    mid = rest.astype(jnp.bfloat16)
    lo = (rest - mid.astype(jnp.float32)).astype(jnp.bfloat16)
    bxt = bxt_ref[...]
    total = jnp.dot(hi, bxt, preferred_element_type=jnp.float32)
    total = total + jnp.dot(mid, bxt, preferred_element_type=jnp.float32)
    total = total + jnp.dot(lo, bxt, preferred_element_type=jnp.float32)
    rsum_ref[...] = total


def front(tomogram, corner_z, corner_y, corner_x):
    count = corner_z.shape[0]
    rows_y = tomogram.shape[1]
    width = tomogram.shape[2]
    t1 = window_table(corner_x, width).reshape(count, width, 2 * BOX)
    pos_y = jnp.arange(rows_y, dtype=jnp.int32)[None, :] - corner_y[:, None]
    inside_y = (pos_y >= 0) & (pos_y < BOX)
    j = jnp.arange(BOX, dtype=jnp.int32)
    turn_y = pos_y[:, :, None] * j[None, None, :] % BOX
    angle_y = angle_of(turn_y)
    zero = jnp.zeros((), jnp.bfloat16)
    cos_y = jnp.where(inside_y[:, :, None], bf(jnp.cos(angle_y)), zero)
    sin_y = jnp.where(inside_y[:, :, None], bf(jnp.sin(angle_y)), zero)
    l2 = jnp.concatenate([cos_y, sin_y], axis=2)
    lower_y = jnp.arange(SHIFT, dtype=jnp.int32)[None, None, :] + shift_anchor() + corner_y[:, None, None]
    cell_y = jnp.arange(rows_y, dtype=jnp.int32)[None, :, None]
    ymask = ((cell_y >= lower_y) & (cell_y < lower_y + TMPL)).astype(jnp.float32)
    bxt = jnp.swapaxes(window_band(corner_x, width), 1, 2).astype(jnp.bfloat16)

    grid_spec = pltpu.PrefetchScalarGridSpec(
        num_scalar_prefetch=1,
        grid=(count,),
        in_specs=[
            pl.BlockSpec((pl.Element(BOX), pl.Element(rows_y), pl.Element(width)), lambda n, cz: (cz[n], 0, 0)),
            pl.BlockSpec((None, width, 2 * BOX), lambda n, cz: (n, 0, 0)),
            pl.BlockSpec((None, rows_y, 2 * BOX), lambda n, cz: (n, 0, 0)),
            pl.BlockSpec((None, rows_y, SHIFT), lambda n, cz: (n, 0, 0)),
            pl.BlockSpec((None, width, SHIFT), lambda n, cz: (n, 0, 0)),
        ],
        out_specs=[
            pl.BlockSpec((None, 2, BOX, BOX, 2 * BOX), lambda n, cz: (n, 0, 0, 0, 0)),
            pl.BlockSpec((None, SHIFT * SHIFT, SHIFT), lambda n, cz: (n, 0, 0)),
        ],
        scratch_shapes=[
            pltpu.VMEM((SHIFT, rows_y, width), jnp.float32),
            pltpu.VMEM((SHIFT * SHIFT, width), jnp.float32),
        ],
    )
    q2, rsum = pl.pallas_call(
        front_kernel,
        grid_spec=grid_spec,
        out_shape=[
            jax.ShapeDtypeStruct((count, 2, BOX, BOX, 2 * BOX), jnp.bfloat16),
            jax.ShapeDtypeStruct((count, SHIFT * SHIFT, SHIFT), jnp.float32),
        ],
        compiler_params=pltpu.CompilerParams(vmem_limit_bytes=48 * 1024 * 1024),
    )(corner_z, tomogram, t1, l2, ymask, bxt)
    box_rms = jnp.sqrt(rsum.reshape(count, SHIFT, SHIFT, SHIFT) / float(TMPL**3) + epsilon)
    return q2, box_rms


def box_spectra_of(q2):
    cos_half, sin_half = phases(HALF, BOX, 0)
    l3 = jnp.stack([bf(cos_half).T, bf(sin_half).T], axis=0)
    return jnp.einsum("nwzkq,wzh->nhkq", q2, l3, preferred_element_type=jnp.float32)


def match_kj(spectrum_v, box_rms, spectra):
    count_r = spectra.shape[0]
    spectra_kq = jnp.transpose(spectra, (0, 2, 4, 1, 3)).reshape(count_r, HALF, BOX, 2 * BOX)
    real_v = spectrum_v[..., :BOX]
    imag_v = spectrum_v[..., BOX:]
    cos_first, sin_first = phases(SHIFT, HALF, shift_anchor())
    freq_index = jnp.arange(HALF, dtype=jnp.int32)
    weight = jnp.where(freq_index % (BOX // 2) == 0, 1.0, 2.0) / float(BOX**3)
    t_first = jnp.stack([bf(cos_first * weight[None, :]).T, bf(sin_first * weight[None, :]).T], axis=0)
    cos_rest, sin_rest = phases(SHIFT, BOX, shift_anchor())
    c_rest = bf(cos_rest).T
    s_rest = bf(sin_rest).T
    t_mid = jnp.concatenate(
        [jnp.concatenate([c_rest, s_rest], axis=1), jnp.concatenate([-s_rest, c_rest], axis=1)], axis=0
    )
    t_last = jnp.stack([c_rest, -s_rest], axis=0)

    def one(spectrum):
        real_t = spectrum[None, ..., :BOX].astype(jnp.float32)
        imag_t = spectrum[None, ..., BOX:].astype(jnp.float32)
        real_p = bf(real_t * real_v + imag_t * imag_v)
        imag_p = bf(real_t * imag_v - imag_t * real_v)
        plain = jnp.concatenate([real_p, imag_p], axis=-1)
        turned = jnp.concatenate([-imag_p, real_p], axis=-1)
        cross = jnp.stack([plain, turned], axis=1)
        stage_g = jnp.einsum("nwhkq,whs->nskq", cross, t_first, preferred_element_type=jnp.float32)
        stage_h = jnp.einsum("nskq,qp->nskp", bf(stage_g), t_mid, preferred_element_type=jnp.float32)
        stage_h = bf(stage_h).reshape(stage_h.shape[0], SHIFT, BOX, 2, SHIFT)
        correlation = jnp.einsum("nskdt,dku->nstu", stage_h, t_last, preferred_element_type=jnp.float32)
        scores = correlation / (box_rms * math.sqrt(float(TMPL**3)))
        return jnp.max(scores, axis=(1, 2, 3))

    values = lax.map(one, spectra_kq)
    return values.T


def per_device(tomogram, templates, corner_z, corner_y, corner_x, loads):
    own_total = corner_z.shape[1]
    live_count = jnp.sum(loads[0, 0])
    q2, box_rms = front(tomogram, corner_z[0], corner_y[0], corner_x[0])
    spectrum_v = box_spectra_of(q2)

    all_templates = lax.all_gather(templates, "orient", axis=0, tiled=True)
    spectra = template_spectra(all_templates.reshape(-1, TMPL, TMPL, TMPL))
    values = match_kj(spectrum_v, box_rms, spectra)
    live = jnp.arange(own_total, dtype=jnp.int32) < live_count
    matched = jnp.where(live[:, None], values, 0.0)
    return (matched[None], jnp.max(matched, axis=1)[None])


def solution(mesh):
    return jax.shard_map(
        per_device,
        mesh=mesh,
        in_specs=(
            P("vol", "orient", None),
            P("orient", None, None),
            P("vol", "orient"),
            P("vol", "orient"),
            P("vol", "orient"),
            P("vol", "orient", None),
        ),
        out_specs=(P("vol", "orient", None), P("vol", "orient")),
        check_vma=False,
    )
```

```python
import math

import jax
import jax.numpy as jnp
from jax import lax
from jax.sharding import PartitionSpec as P
from jax.experimental import pallas as pl
from jax.experimental.pallas import tpu as pltpu

BOX = 64
TMPL = 32
SHIFT = 8
HALF = 33


epsilon = 1e-05


def shift_anchor():
    return (BOX - TMPL) // 2 - SHIFT // 2


def angle_of(turn_index):
    return turn_index.astype(jnp.float32) * (2.0 * math.pi / BOX)


def phases(count_out, count_in, offset):
    out_index = jnp.arange(count_out, dtype=jnp.int32) + offset
    in_index = jnp.arange(count_in, dtype=jnp.int32)
    turn_index = out_index[:, None] * in_index[None, :] % BOX
    phase_angle = angle_of(turn_index)
    return (jnp.cos(phase_angle), jnp.sin(phase_angle))


def bf(x):
    return x.astype(jnp.bfloat16)


def complex_table(cos_t, sin_t, sign_re_from_im, sign_im_from_re):
    c = bf(cos_t).T
    s = bf(sin_t).T
    re_row = jnp.stack([c, sign_im_from_re * s], axis=1)
    im_row = jnp.stack([sign_re_from_im * s, c], axis=1)
    return jnp.stack([re_row, im_row], axis=0)


def section(pattern, operand, table):
    return jnp.einsum(pattern, bf(operand), table, preferred_element_type=jnp.float32)


def forward_tail(stage_one):
    length_a = stage_one.shape[2]
    length_y = stage_one.shape[3]
    cos_full, sin_full = phases(BOX, length_y, 0)
    t_mid = complex_table(cos_full, sin_full, 1.0, -1.0)
    stage_two = section("ncayk,cydj->ndajk", stage_one, t_mid)
    cos_half, sin_half = phases(HALF, length_a, 0)
    t_first = complex_table(cos_half, sin_half, 1.0, -1.0)
    return section("ncajk,cadh->ndhjk", stage_two, t_first)


def template_spectra(cubes):
    volume = cubes.astype(jnp.float32)
    count = volume.shape[0]
    flat = volume.reshape(count, -1)
    centred = flat - jnp.mean(flat, axis=1, keepdims=True)
    unit = centred / jnp.sqrt(jnp.mean(centred * centred, axis=1, keepdims=True) + epsilon)
    unit = unit.reshape(count, TMPL, TMPL, TMPL)
    cos_full, sin_full = phases(BOX, TMPL, 0)
    t_last = jnp.stack([bf(cos_full).T, -bf(sin_full).T], axis=1)
    stage_one = section("nabx,xck->ncabk", unit, t_last)
    return bf(forward_tail(stage_one))


def window_table(corner_x, width):
    pos = jnp.arange(width, dtype=jnp.int32)[None, :] - corner_x[:, None]
    inside = (pos >= 0) & (pos < BOX)
    k = jnp.arange(BOX, dtype=jnp.int32)
    turn = k[None, None, :] * pos[:, :, None] % BOX
    phase_angle = angle_of(turn)
    mask = inside[:, :, None]
    cos_t = jnp.where(mask, bf(jnp.cos(phase_angle)), jnp.zeros((), jnp.bfloat16))
    sin_t = jnp.where(mask, -bf(jnp.sin(phase_angle)), jnp.zeros((), jnp.bfloat16))
    return jnp.stack([cos_t, sin_t], axis=2)


def band_table():
    lower_edge = jnp.arange(SHIFT, dtype=jnp.int32)[:, None] + shift_anchor()
    cell_index = jnp.arange(BOX, dtype=jnp.int32)[None, :]
    return ((cell_index >= lower_edge) & (cell_index < lower_edge + TMPL)).astype(jnp.float32)


def window_band(corner_x, width):
    lower_edge = jnp.arange(SHIFT, dtype=jnp.int32)[None, :, None] + shift_anchor() + corner_x[:, None, None]
    cell_index = jnp.arange(width, dtype=jnp.int32)[None, None, :]
    return ((cell_index >= lower_edge) & (cell_index < lower_edge + TMPL)).astype(jnp.float32)


def window_rms(rows, corner_x):
    width = rows.shape[-1]
    squares = rows.astype(jnp.float32) ** 2
    band_x = window_band(corner_x, width)
    band = band_table()
    hi = lax.Precision.HIGHEST
    sums_c = jnp.einsum("nabx,nux->nabu", squares, band_x, precision=hi)
    sums_b = jnp.einsum("nabu,tb->natu", sums_c, band, precision=hi)
    sums_a = jnp.einsum("natu,sa->nstu", sums_b, band, precision=hi)
    return jnp.sqrt(sums_a / float(TMPL**3) + epsilon)


def match(box_spectra, box_rms, spectra):
    values = lax.map(lambda one: match_one(box_spectra, box_rms, one[None]), spectra)
    return values[:, :, 0].T


def match_one(box_spectra, box_rms, spectra):
    real_t = spectra[:, 0].astype(jnp.float32)[None]
    imag_t = spectra[:, 1].astype(jnp.float32)[None]
    real_v = box_spectra[:, 0][:, None]
    imag_v = box_spectra[:, 1][:, None]
    real_p = real_t * real_v + imag_t * imag_v
    imag_p = real_t * imag_v - imag_t * real_v
    cross = jnp.stack([bf(real_p), bf(imag_p)], axis=2)
    cos_first, sin_first = phases(SHIFT, HALF, shift_anchor())
    freq_index = jnp.arange(HALF, dtype=jnp.int32)
    weight = jnp.where(freq_index % (BOX // 2) == 0, 1.0, 2.0) / float(BOX**3)
    cos_first = cos_first * weight[None, :]
    sin_first = sin_first * weight[None, :]
    t_first = complex_table(cos_first, sin_first, -1.0, 1.0)
    stage_g = section("nrchjk,chds->nrdsjk", cross, t_first)
    cos_rest, sin_rest = phases(SHIFT, BOX, shift_anchor())
    t_mid = complex_table(cos_rest, sin_rest, -1.0, 1.0)
    stage_h = section("nrcsjk,cjdt->nrdstk", stage_g, t_mid)
    t_last = jnp.stack([bf(cos_rest).T, -bf(sin_rest).T], axis=0)
    correlation = section("nrcstk,cku->nrstu", stage_h, t_last)
    scores = correlation / (box_rms[:, None] * math.sqrt(float(TMPL**3)))
    return jnp.max(scores, axis=(2, 3, 4))


def front_kernel(cz_ref, slab_ref, t1_ref, l2_ref, ymask_ref, bxt_ref, q2_ref, rsum_ref, w_scr, y_scr):
    depth, rows_y, width = slab_ref.shape
    chunk = 8
    t1 = t1_ref[...]
    l2 = l2_ref[...]

    def transform_chunk(ci, carry):
        z0 = pl.multiple_of(ci * chunk, chunk)
        rows = slab_ref[pl.ds(z0, chunk)].reshape(chunk * rows_y, width)
        p1 = jnp.dot(rows, t1, preferred_element_type=jnp.float32)
        p1 = p1.astype(jnp.bfloat16).astype(jnp.float32).reshape(chunk, rows_y, 2 * BOX)
        p1t = jnp.swapaxes(p1, 1, 2).reshape(chunk * 2 * BOX, rows_y).astype(jnp.bfloat16)
        m2 = jnp.dot(p1t, l2, preferred_element_type=jnp.float32).reshape(chunk, 2, BOX, 2 * BOX)
        part_a = m2[:, 0]
        part_b = m2[:, 1]
        lane = lax.broadcasted_iota(jnp.int32, part_a.shape, 2)
        sign = jnp.where(lane < BOX, 1.0, -1.0).astype(jnp.float32)
        out = (pltpu.roll(part_b, BOX, 2) + sign * part_a).astype(jnp.bfloat16).astype(jnp.float32)
        q2_ref[0, pl.ds(z0, chunk)] = out.astype(jnp.bfloat16)
        swapped = sign * pltpu.roll(out, BOX, 2)
        q2_ref[1, pl.ds(z0, chunk)] = swapped.astype(jnp.bfloat16)
        return carry

    lax.fori_loop(0, depth // chunk, transform_chunk, 0)

    lo_z = shift_anchor()

    def plane_sq(z):
        v = slab_ref[z].astype(jnp.float32)
        return v * v

    def first_window(z, acc):
        return acc + plane_sq(lo_z + z)

    acc = lax.fori_loop(0, TMPL, first_window, jnp.zeros((rows_y, width), jnp.float32))
    w_scr[0] = acc
    for s_i in range(1, SHIFT):
        acc = acc + plane_sq(lo_z + TMPL + s_i - 1) - plane_sq(lo_z + s_i - 1)
        w_scr[s_i] = acc

    ymask = ymask_ref[...]

    def y_sums(s_i, carry):
        plane = w_scr[s_i]
        for t_i in range(SHIFT):
            y_scr[pl.ds(s_i * SHIFT + t_i, 1), :] = jnp.sum(plane * ymask[:, t_i:t_i + 1], axis=0, keepdims=True)
        return carry

    lax.fori_loop(0, SHIFT, y_sums, 0)
    ysum = y_scr[...]
    hi = ysum.astype(jnp.bfloat16)
    rest = ysum - hi.astype(jnp.float32)
    mid = rest.astype(jnp.bfloat16)
    lo = (rest - mid.astype(jnp.float32)).astype(jnp.bfloat16)
    bxt = bxt_ref[...]
    total = jnp.dot(hi, bxt, preferred_element_type=jnp.float32)
    total = total + jnp.dot(mid, bxt, preferred_element_type=jnp.float32)
    total = total + jnp.dot(lo, bxt, preferred_element_type=jnp.float32)
    rsum_ref[...] = total


def front(tomogram, corner_z, corner_y, corner_x):
    count = corner_z.shape[0]
    rows_y = tomogram.shape[1]
    width = tomogram.shape[2]
    t1 = window_table(corner_x, width).reshape(count, width, 2 * BOX)
    pos_y = jnp.arange(rows_y, dtype=jnp.int32)[None, :] - corner_y[:, None]
    inside_y = (pos_y >= 0) & (pos_y < BOX)
    j = jnp.arange(BOX, dtype=jnp.int32)
    turn_y = pos_y[:, :, None] * j[None, None, :] % BOX
    angle_y = angle_of(turn_y)
    zero = jnp.zeros((), jnp.bfloat16)
    cos_y = jnp.where(inside_y[:, :, None], bf(jnp.cos(angle_y)), zero)
    sin_y = jnp.where(inside_y[:, :, None], bf(jnp.sin(angle_y)), zero)
    l2 = jnp.concatenate([cos_y, sin_y], axis=2)
    lower_y = jnp.arange(SHIFT, dtype=jnp.int32)[None, None, :] + shift_anchor() + corner_y[:, None, None]
    cell_y = jnp.arange(rows_y, dtype=jnp.int32)[None, :, None]
    ymask = ((cell_y >= lower_y) & (cell_y < lower_y + TMPL)).astype(jnp.float32)
    bxt = jnp.swapaxes(window_band(corner_x, width), 1, 2).astype(jnp.bfloat16)

    grid_spec = pltpu.PrefetchScalarGridSpec(
        num_scalar_prefetch=1,
        grid=(count,),
        in_specs=[
            pl.BlockSpec((pl.Element(BOX), pl.Element(rows_y), pl.Element(width)), lambda n, cz: (cz[n], 0, 0)),
            pl.BlockSpec((None, width, 2 * BOX), lambda n, cz: (n, 0, 0)),
            pl.BlockSpec((None, rows_y, 2 * BOX), lambda n, cz: (n, 0, 0)),
            pl.BlockSpec((None, rows_y, SHIFT), lambda n, cz: (n, 0, 0)),
            pl.BlockSpec((None, width, SHIFT), lambda n, cz: (n, 0, 0)),
        ],
        out_specs=[
            pl.BlockSpec((None, 2, BOX, BOX, 2 * BOX), lambda n, cz: (n, 0, 0, 0, 0)),
            pl.BlockSpec((None, SHIFT * SHIFT, SHIFT), lambda n, cz: (n, 0, 0)),
        ],
        scratch_shapes=[
            pltpu.VMEM((SHIFT, rows_y, width), jnp.float32),
            pltpu.VMEM((SHIFT * SHIFT, width), jnp.float32),
        ],
    )
    q2, rsum = pl.pallas_call(
        front_kernel,
        grid_spec=grid_spec,
        out_shape=[
            jax.ShapeDtypeStruct((count, 2, BOX, BOX, 2 * BOX), jnp.bfloat16),
            jax.ShapeDtypeStruct((count, SHIFT * SHIFT, SHIFT), jnp.float32),
        ],
        compiler_params=pltpu.CompilerParams(vmem_limit_bytes=48 * 1024 * 1024),
    )(corner_z, tomogram, t1, l2, ymask, bxt)
    box_rms = jnp.sqrt(rsum.reshape(count, SHIFT, SHIFT, SHIFT) / float(TMPL**3) + epsilon)
    return q2, box_rms


def box_spectra_of(q2):
    cos_half, sin_half = phases(HALF, BOX, 0)
    l3 = jnp.stack([bf(cos_half).T, bf(sin_half).T], axis=0)
    return jnp.einsum("nwzkq,wzh->nhkq", q2, l3, preferred_element_type=jnp.float32)


def match_kj(spectrum_v, box_rms, spectra):
    spectra_kj = jnp.swapaxes(spectra, 3, 4)

    def one(spectrum):
        real_v = spectrum_v[..., :BOX]
        imag_v = spectrum_v[..., BOX:]
        real_t = spectrum[0].astype(jnp.float32)[None, None]
        imag_t = spectrum[1].astype(jnp.float32)[None, None]
        rv = real_v[:, None]
        iv = imag_v[:, None]
        real_p = real_t * rv + imag_t * iv
        imag_p = real_t * iv - imag_t * rv
        cross = jnp.stack([bf(real_p), bf(imag_p)], axis=2)
        cos_first, sin_first = phases(SHIFT, HALF, shift_anchor())
        freq_index = jnp.arange(HALF, dtype=jnp.int32)
        weight = jnp.where(freq_index % (BOX // 2) == 0, 1.0, 2.0) / float(BOX**3)
        t_first = complex_table(cos_first * weight[None, :], sin_first * weight[None, :], -1.0, 1.0)
        stage_g = section("nrchkj,chds->nrdskj", cross, t_first)
        cos_rest, sin_rest = phases(SHIFT, BOX, shift_anchor())
        t_mid = complex_table(cos_rest, sin_rest, -1.0, 1.0)
        stage_h = section("nrcskj,cjdt->nrdskt", stage_g, t_mid)
        t_last = jnp.stack([bf(cos_rest).T, -bf(sin_rest).T], axis=0)
        correlation = section("nrcskt,cku->nrstu", stage_h, t_last)
        scores = correlation / (box_rms[:, None] * math.sqrt(float(TMPL**3)))
        return jnp.max(scores, axis=(2, 3, 4))[:, 0]

    count_r = spectra_kj.shape[0]
    group = min(4, count_r)

    def one_group(block):
        return jnp.stack([one(block[i]) for i in range(group)], axis=0)

    blocks = spectra_kj.reshape((count_r // group, group) + spectra_kj.shape[1:])
    if count_r == group:
        values = one_group(blocks[0])
    else:
        values = lax.map(one_group, blocks).reshape((count_r,) + (spectrum_v.shape[0],))
    return values.T


def per_device(tomogram, templates, corner_z, corner_y, corner_x, loads):
    own_total = corner_z.shape[1]
    live_count = jnp.sum(loads[0, 0])
    q2, box_rms = front(tomogram, corner_z[0], corner_y[0], corner_x[0])
    spectrum_v = box_spectra_of(q2)

    all_templates = lax.all_gather(templates, "orient", axis=0, tiled=True)
    spectra = template_spectra(all_templates.reshape(-1, TMPL, TMPL, TMPL))
    values = match_kj(spectrum_v, box_rms, spectra)
    live = jnp.arange(own_total, dtype=jnp.int32) < live_count
    matched = jnp.where(live[:, None], values, 0.0)
    return (matched[None], jnp.max(matched, axis=1)[None])


def solution(mesh):
    return jax.shard_map(
        per_device,
        mesh=mesh,
        in_specs=(
            P("vol", "orient", None),
            P("orient", None, None),
            P("vol", "orient"),
            P("vol", "orient"),
            P("vol", "orient"),
            P("vol", "orient", None),
        ),
        out_specs=(P("vol", "orient", None), P("vol", "orient")),
        check_vma=False,
    )
```

```python
import math

import jax
import jax.numpy as jnp
from jax import lax
from jax.sharding import PartitionSpec as P
from jax.experimental import pallas as pl
from jax.experimental.pallas import tpu as pltpu

BOX = 64
TMPL = 32
SHIFT = 8
HALF = 33


epsilon = 1e-05


def shift_anchor():
    return (BOX - TMPL) // 2 - SHIFT // 2


def angle_of(turn_index):
    return turn_index.astype(jnp.float32) * (2.0 * math.pi / BOX)


def phases(count_out, count_in, offset):
    out_index = jnp.arange(count_out, dtype=jnp.int32) + offset
    in_index = jnp.arange(count_in, dtype=jnp.int32)
    turn_index = out_index[:, None] * in_index[None, :] % BOX
    phase_angle = angle_of(turn_index)
    return (jnp.cos(phase_angle), jnp.sin(phase_angle))


def bf(x):
    return x.astype(jnp.bfloat16)


def complex_table(cos_t, sin_t, sign_re_from_im, sign_im_from_re):
    c = bf(cos_t).T
    s = bf(sin_t).T
    re_row = jnp.stack([c, sign_im_from_re * s], axis=1)
    im_row = jnp.stack([sign_re_from_im * s, c], axis=1)
    return jnp.stack([re_row, im_row], axis=0)


def section(pattern, operand, table):
    return jnp.einsum(pattern, bf(operand), table, preferred_element_type=jnp.float32)


def forward_tail(stage_one):
    length_a = stage_one.shape[2]
    length_y = stage_one.shape[3]
    cos_full, sin_full = phases(BOX, length_y, 0)
    t_mid = complex_table(cos_full, sin_full, 1.0, -1.0)
    stage_two = section("ncayk,cydj->ndajk", stage_one, t_mid)
    cos_half, sin_half = phases(HALF, length_a, 0)
    t_first = complex_table(cos_half, sin_half, 1.0, -1.0)
    return section("ncajk,cadh->ndhjk", stage_two, t_first)


def template_spectra(cubes):
    volume = cubes.astype(jnp.float32)
    count = volume.shape[0]
    flat = volume.reshape(count, -1)
    centred = flat - jnp.mean(flat, axis=1, keepdims=True)
    unit = centred / jnp.sqrt(jnp.mean(centred * centred, axis=1, keepdims=True) + epsilon)
    unit = unit.reshape(count, TMPL, TMPL, TMPL)
    cos_full, sin_full = phases(BOX, TMPL, 0)
    t_last = jnp.stack([bf(cos_full).T, -bf(sin_full).T], axis=1)
    stage_one = section("nabx,xck->ncabk", unit, t_last)
    return bf(forward_tail(stage_one))


def window_table(corner_x, width):
    pos = jnp.arange(width, dtype=jnp.int32)[None, :] - corner_x[:, None]
    inside = (pos >= 0) & (pos < BOX)
    k = jnp.arange(BOX, dtype=jnp.int32)
    turn = k[None, None, :] * pos[:, :, None] % BOX
    phase_angle = angle_of(turn)
    mask = inside[:, :, None]
    cos_t = jnp.where(mask, bf(jnp.cos(phase_angle)), jnp.zeros((), jnp.bfloat16))
    sin_t = jnp.where(mask, -bf(jnp.sin(phase_angle)), jnp.zeros((), jnp.bfloat16))
    return jnp.stack([cos_t, sin_t], axis=2)


def band_table():
    lower_edge = jnp.arange(SHIFT, dtype=jnp.int32)[:, None] + shift_anchor()
    cell_index = jnp.arange(BOX, dtype=jnp.int32)[None, :]
    return ((cell_index >= lower_edge) & (cell_index < lower_edge + TMPL)).astype(jnp.float32)


def window_band(corner_x, width):
    lower_edge = jnp.arange(SHIFT, dtype=jnp.int32)[None, :, None] + shift_anchor() + corner_x[:, None, None]
    cell_index = jnp.arange(width, dtype=jnp.int32)[None, None, :]
    return ((cell_index >= lower_edge) & (cell_index < lower_edge + TMPL)).astype(jnp.float32)


def window_rms(rows, corner_x):
    width = rows.shape[-1]
    squares = rows.astype(jnp.float32) ** 2
    band_x = window_band(corner_x, width)
    band = band_table()
    hi = lax.Precision.HIGHEST
    sums_c = jnp.einsum("nabx,nux->nabu", squares, band_x, precision=hi)
    sums_b = jnp.einsum("nabu,tb->natu", sums_c, band, precision=hi)
    sums_a = jnp.einsum("natu,sa->nstu", sums_b, band, precision=hi)
    return jnp.sqrt(sums_a / float(TMPL**3) + epsilon)


def match(box_spectra, box_rms, spectra):
    values = lax.map(lambda one: match_one(box_spectra, box_rms, one[None]), spectra)
    return values[:, :, 0].T


def match_one(box_spectra, box_rms, spectra):
    real_t = spectra[:, 0].astype(jnp.float32)[None]
    imag_t = spectra[:, 1].astype(jnp.float32)[None]
    real_v = box_spectra[:, 0][:, None]
    imag_v = box_spectra[:, 1][:, None]
    real_p = real_t * real_v + imag_t * imag_v
    imag_p = real_t * imag_v - imag_t * real_v
    cross = jnp.stack([bf(real_p), bf(imag_p)], axis=2)
    cos_first, sin_first = phases(SHIFT, HALF, shift_anchor())
    freq_index = jnp.arange(HALF, dtype=jnp.int32)
    weight = jnp.where(freq_index % (BOX // 2) == 0, 1.0, 2.0) / float(BOX**3)
    cos_first = cos_first * weight[None, :]
    sin_first = sin_first * weight[None, :]
    t_first = complex_table(cos_first, sin_first, -1.0, 1.0)
    stage_g = section("nrchjk,chds->nrdsjk", cross, t_first)
    cos_rest, sin_rest = phases(SHIFT, BOX, shift_anchor())
    t_mid = complex_table(cos_rest, sin_rest, -1.0, 1.0)
    stage_h = section("nrcsjk,cjdt->nrdstk", stage_g, t_mid)
    t_last = jnp.stack([bf(cos_rest).T, -bf(sin_rest).T], axis=0)
    correlation = section("nrcstk,cku->nrstu", stage_h, t_last)
    scores = correlation / (box_rms[:, None] * math.sqrt(float(TMPL**3)))
    return jnp.max(scores, axis=(2, 3, 4))


def front_kernel(cz_ref, slab_ref, t1_ref, l2_ref, q2_ref):
    depth, rows_y, width = slab_ref.shape
    chunk = 8
    t1 = t1_ref[...]
    l2 = l2_ref[...]

    def transform_chunk(ci, carry):
        z0 = pl.multiple_of(ci * chunk, chunk)
        rows = slab_ref[pl.ds(z0, chunk)].reshape(chunk * rows_y, width)
        p1 = jnp.dot(rows, t1, preferred_element_type=jnp.float32)
        p1 = p1.astype(jnp.bfloat16).astype(jnp.float32).reshape(chunk, rows_y, 2 * BOX)
        p1t = jnp.swapaxes(p1, 1, 2).reshape(chunk * 2 * BOX, rows_y).astype(jnp.bfloat16)
        m2 = jnp.dot(p1t, l2, preferred_element_type=jnp.float32).reshape(chunk, 2, BOX, 2 * BOX)
        part_a = m2[:, 0]
        part_b = m2[:, 1]
        lane = lax.broadcasted_iota(jnp.int32, part_a.shape, 2)
        sign = jnp.where(lane < BOX, 1.0, -1.0).astype(jnp.float32)
        out = (pltpu.roll(part_b, BOX, 2) + sign * part_a).astype(jnp.bfloat16).astype(jnp.float32)
        q2_ref[0, pl.ds(z0, chunk)] = out.astype(jnp.bfloat16)
        swapped = sign * pltpu.roll(out, BOX, 2)
        q2_ref[1, pl.ds(z0, chunk)] = swapped.astype(jnp.bfloat16)
        return carry

    lax.fori_loop(0, depth // chunk, transform_chunk, 0)


def window_bands(corner, length):
    lower_edge = jnp.arange(SHIFT, dtype=jnp.int32)[None, :, None] + shift_anchor() + corner[:, None, None]
    cell_index = jnp.arange(length, dtype=jnp.int32)[None, None, :]
    return ((cell_index >= lower_edge) & (cell_index < lower_edge + TMPL)).astype(jnp.float32)


def block_rms(tomogram, corner_z, corner_y, corner_x):
    depth, rows_y, width = tomogram.shape
    count = corner_z.shape[0]
    hi = lax.Precision.HIGHEST
    values = tomogram.astype(jnp.float32)
    squares = (values * values).reshape(depth * rows_y, width)
    band_x = window_bands(corner_x, width).reshape(count * SHIFT, width)
    sums_x = jnp.dot(squares, band_x.T, precision=hi).reshape(depth, rows_y, count, SHIFT)
    band_y = window_bands(corner_y, rows_y)
    sums_y = jnp.einsum("zynu,nty->nztu", sums_x, band_y, precision=hi)
    band_z = window_bands(corner_z, depth)
    sums_z = jnp.einsum("nztu,nsz->nstu", sums_y, band_z, precision=hi)
    return jnp.sqrt(sums_z / float(TMPL**3) + epsilon)


def front(tomogram, corner_z, corner_y, corner_x):
    count = corner_z.shape[0]
    rows_y = tomogram.shape[1]
    width = tomogram.shape[2]
    t1 = window_table(corner_x, width).reshape(count, width, 2 * BOX)
    pos_y = jnp.arange(rows_y, dtype=jnp.int32)[None, :] - corner_y[:, None]
    inside_y = (pos_y >= 0) & (pos_y < BOX)
    j = jnp.arange(BOX, dtype=jnp.int32)
    turn_y = pos_y[:, :, None] * j[None, None, :] % BOX
    angle_y = angle_of(turn_y)
    zero = jnp.zeros((), jnp.bfloat16)
    cos_y = jnp.where(inside_y[:, :, None], bf(jnp.cos(angle_y)), zero)
    sin_y = jnp.where(inside_y[:, :, None], bf(jnp.sin(angle_y)), zero)
    l2 = jnp.concatenate([cos_y, sin_y], axis=2)

    grid_spec = pltpu.PrefetchScalarGridSpec(
        num_scalar_prefetch=1,
        grid=(count,),
        in_specs=[
            pl.BlockSpec((pl.Element(BOX), pl.Element(rows_y), pl.Element(width)), lambda n, cz: (cz[n], 0, 0)),
            pl.BlockSpec((None, width, 2 * BOX), lambda n, cz: (n, 0, 0)),
            pl.BlockSpec((None, rows_y, 2 * BOX), lambda n, cz: (n, 0, 0)),
        ],
        out_specs=pl.BlockSpec((None, 2, BOX, BOX, 2 * BOX), lambda n, cz: (n, 0, 0, 0, 0)),
    )
    q2 = pl.pallas_call(
        front_kernel,
        grid_spec=grid_spec,
        out_shape=jax.ShapeDtypeStruct((count, 2, BOX, BOX, 2 * BOX), jnp.bfloat16),
        compiler_params=pltpu.CompilerParams(vmem_limit_bytes=48 * 1024 * 1024),
    )(corner_z, tomogram, t1, l2)
    return q2, block_rms(tomogram, corner_z, corner_y, corner_x)


def box_spectra_of(q2):
    cos_half, sin_half = phases(HALF, BOX, 0)
    l3 = jnp.stack([bf(cos_half).T, bf(sin_half).T], axis=0)
    return jnp.einsum("nwzkq,wzh->nhkq", q2, l3, preferred_element_type=jnp.float32)


def match_kj(spectrum_v, box_rms, spectra):
    spectra_kj = jnp.swapaxes(spectra, 3, 4)

    def one(spectrum):
        real_v = spectrum_v[..., :BOX]
        imag_v = spectrum_v[..., BOX:]
        real_t = spectrum[0].astype(jnp.float32)[None, None]
        imag_t = spectrum[1].astype(jnp.float32)[None, None]
        rv = real_v[:, None]
        iv = imag_v[:, None]
        real_p = real_t * rv + imag_t * iv
        imag_p = real_t * iv - imag_t * rv
        cross = jnp.stack([bf(real_p), bf(imag_p)], axis=2)
        cos_first, sin_first = phases(SHIFT, HALF, shift_anchor())
        freq_index = jnp.arange(HALF, dtype=jnp.int32)
        weight = jnp.where(freq_index % (BOX // 2) == 0, 1.0, 2.0) / float(BOX**3)
        t_first = complex_table(cos_first * weight[None, :], sin_first * weight[None, :], -1.0, 1.0)
        stage_g = section("nrchkj,chds->nrdskj", cross, t_first)
        cos_rest, sin_rest = phases(SHIFT, BOX, shift_anchor())
        t_mid = complex_table(cos_rest, sin_rest, -1.0, 1.0)
        stage_h = section("nrcskj,cjdt->nrdskt", stage_g, t_mid)
        t_last = jnp.stack([bf(cos_rest).T, -bf(sin_rest).T], axis=0)
        correlation = section("nrcskt,cku->nrstu", stage_h, t_last)
        scores = correlation / (box_rms[:, None] * math.sqrt(float(TMPL**3)))
        return jnp.max(scores, axis=(2, 3, 4))[:, 0]

    count_r = spectra_kj.shape[0]
    group = min(4, count_r)

    def one_group(block):
        return jnp.stack([one(block[i]) for i in range(group)], axis=0)

    blocks = spectra_kj.reshape((count_r // group, group) + spectra_kj.shape[1:])
    if count_r == group:
        values = one_group(blocks[0])
    else:
        values = lax.map(one_group, blocks).reshape((count_r,) + (spectrum_v.shape[0],))
    return values.T


def per_device(tomogram, templates, corner_z, corner_y, corner_x, loads):
    own_total = corner_z.shape[1]
    live_count = jnp.sum(loads[0, 0])
    q2, box_rms = front(tomogram, corner_z[0], corner_y[0], corner_x[0])
    spectrum_v = box_spectra_of(q2)

    all_templates = lax.all_gather(templates, "orient", axis=0, tiled=True)
    spectra = template_spectra(all_templates.reshape(-1, TMPL, TMPL, TMPL))
    values = match_kj(spectrum_v, box_rms, spectra)
    live = jnp.arange(own_total, dtype=jnp.int32) < live_count
    matched = jnp.where(live[:, None], values, 0.0)
    return (matched[None], jnp.max(matched, axis=1)[None])


def solution(mesh):
    return jax.shard_map(
        per_device,
        mesh=mesh,
        in_specs=(
            P("vol", "orient", None),
            P("orient", None, None),
            P("vol", "orient"),
            P("vol", "orient"),
            P("vol", "orient"),
            P("vol", "orient", None),
        ),
        out_specs=(P("vol", "orient", None), P("vol", "orient")),
        check_vma=False,
    )
```

```python
import math

import jax
import jax.numpy as jnp
from jax import lax
from jax.sharding import PartitionSpec as P
from jax.experimental import pallas as pl
from jax.experimental.pallas import tpu as pltpu

BOX = 64
TMPL = 32
SHIFT = 8
HALF = 33


epsilon = 1e-05


def shift_anchor():
    return (BOX - TMPL) // 2 - SHIFT // 2


def angle_of(turn_index):
    return turn_index.astype(jnp.float32) * (2.0 * math.pi / BOX)


def phases(count_out, count_in, offset):
    out_index = jnp.arange(count_out, dtype=jnp.int32) + offset
    in_index = jnp.arange(count_in, dtype=jnp.int32)
    turn_index = out_index[:, None] * in_index[None, :] % BOX
    phase_angle = angle_of(turn_index)
    return (jnp.cos(phase_angle), jnp.sin(phase_angle))


def bf(x):
    return x.astype(jnp.bfloat16)


def complex_table(cos_t, sin_t, sign_re_from_im, sign_im_from_re):
    c = bf(cos_t).T
    s = bf(sin_t).T
    re_row = jnp.stack([c, sign_im_from_re * s], axis=1)
    im_row = jnp.stack([sign_re_from_im * s, c], axis=1)
    return jnp.stack([re_row, im_row], axis=0)


def section(pattern, operand, table):
    return jnp.einsum(pattern, bf(operand), table, preferred_element_type=jnp.float32)


def forward_tail(stage_one):
    length_a = stage_one.shape[2]
    length_y = stage_one.shape[3]
    cos_full, sin_full = phases(BOX, length_y, 0)
    t_mid = complex_table(cos_full, sin_full, 1.0, -1.0)
    stage_two = section("ncayk,cydj->ndajk", stage_one, t_mid)
    cos_half, sin_half = phases(HALF, length_a, 0)
    t_first = complex_table(cos_half, sin_half, 1.0, -1.0)
    return section("ncajk,cadh->ndhjk", stage_two, t_first)


def template_spectra(cubes):
    volume = cubes.astype(jnp.float32)
    count = volume.shape[0]
    flat = volume.reshape(count, -1)
    centred = flat - jnp.mean(flat, axis=1, keepdims=True)
    unit = centred / jnp.sqrt(jnp.mean(centred * centred, axis=1, keepdims=True) + epsilon)
    unit = unit.reshape(count, TMPL, TMPL, TMPL)
    cos_full, sin_full = phases(BOX, TMPL, 0)
    t_last = jnp.stack([bf(cos_full).T, -bf(sin_full).T], axis=1)
    stage_one = section("nabx,xck->ncabk", unit, t_last)
    return bf(forward_tail(stage_one))


def window_table(corner_x, width):
    pos = jnp.arange(width, dtype=jnp.int32)[None, :] - corner_x[:, None]
    inside = (pos >= 0) & (pos < BOX)
    k = jnp.arange(BOX, dtype=jnp.int32)
    turn = k[None, None, :] * pos[:, :, None] % BOX
    phase_angle = angle_of(turn)
    mask = inside[:, :, None]
    cos_t = jnp.where(mask, bf(jnp.cos(phase_angle)), jnp.zeros((), jnp.bfloat16))
    sin_t = jnp.where(mask, -bf(jnp.sin(phase_angle)), jnp.zeros((), jnp.bfloat16))
    return jnp.stack([cos_t, sin_t], axis=2)


def band_table():
    lower_edge = jnp.arange(SHIFT, dtype=jnp.int32)[:, None] + shift_anchor()
    cell_index = jnp.arange(BOX, dtype=jnp.int32)[None, :]
    return ((cell_index >= lower_edge) & (cell_index < lower_edge + TMPL)).astype(jnp.float32)


def window_band(corner_x, width):
    lower_edge = jnp.arange(SHIFT, dtype=jnp.int32)[None, :, None] + shift_anchor() + corner_x[:, None, None]
    cell_index = jnp.arange(width, dtype=jnp.int32)[None, None, :]
    return ((cell_index >= lower_edge) & (cell_index < lower_edge + TMPL)).astype(jnp.float32)


def window_rms(rows, corner_x):
    width = rows.shape[-1]
    squares = rows.astype(jnp.float32) ** 2
    band_x = window_band(corner_x, width)
    band = band_table()
    hi = lax.Precision.HIGHEST
    sums_c = jnp.einsum("nabx,nux->nabu", squares, band_x, precision=hi)
    sums_b = jnp.einsum("nabu,tb->natu", sums_c, band, precision=hi)
    sums_a = jnp.einsum("natu,sa->nstu", sums_b, band, precision=hi)
    return jnp.sqrt(sums_a / float(TMPL**3) + epsilon)


def match(box_spectra, box_rms, spectra):
    values = lax.map(lambda one: match_one(box_spectra, box_rms, one[None]), spectra)
    return values[:, :, 0].T


def match_one(box_spectra, box_rms, spectra):
    real_t = spectra[:, 0].astype(jnp.float32)[None]
    imag_t = spectra[:, 1].astype(jnp.float32)[None]
    real_v = box_spectra[:, 0][:, None]
    imag_v = box_spectra[:, 1][:, None]
    real_p = real_t * real_v + imag_t * imag_v
    imag_p = real_t * imag_v - imag_t * real_v
    cross = jnp.stack([bf(real_p), bf(imag_p)], axis=2)
    cos_first, sin_first = phases(SHIFT, HALF, shift_anchor())
    freq_index = jnp.arange(HALF, dtype=jnp.int32)
    weight = jnp.where(freq_index % (BOX // 2) == 0, 1.0, 2.0) / float(BOX**3)
    cos_first = cos_first * weight[None, :]
    sin_first = sin_first * weight[None, :]
    t_first = complex_table(cos_first, sin_first, -1.0, 1.0)
    stage_g = section("nrchjk,chds->nrdsjk", cross, t_first)
    cos_rest, sin_rest = phases(SHIFT, BOX, shift_anchor())
    t_mid = complex_table(cos_rest, sin_rest, -1.0, 1.0)
    stage_h = section("nrcsjk,cjdt->nrdstk", stage_g, t_mid)
    t_last = jnp.stack([bf(cos_rest).T, -bf(sin_rest).T], axis=0)
    correlation = section("nrcstk,cku->nrstu", stage_h, t_last)
    scores = correlation / (box_rms[:, None] * math.sqrt(float(TMPL**3)))
    return jnp.max(scores, axis=(2, 3, 4))


def front_kernel(cz_ref, slab_ref, t1_ref, l2_ref, q2_ref):
    depth, rows_y, width = slab_ref.shape
    chunk = 8
    t1 = t1_ref[...]
    l2 = l2_ref[...]

    def transform_chunk(ci, carry):
        z0 = pl.multiple_of(ci * chunk, chunk)
        rows = slab_ref[pl.ds(z0, chunk)].reshape(chunk * rows_y, width)
        p1 = jnp.dot(rows, t1, preferred_element_type=jnp.float32)
        p1 = p1.astype(jnp.bfloat16).astype(jnp.float32).reshape(chunk, rows_y, 2 * BOX)
        p1t = jnp.swapaxes(p1, 1, 2)
        stacked = jnp.concatenate([p1t[:, :BOX], p1t[:, BOX:]], axis=2)
        stacked = stacked.reshape(chunk * BOX, 2 * rows_y).astype(jnp.bfloat16)
        m2 = jnp.dot(stacked, l2, preferred_element_type=jnp.float32).reshape(chunk, BOX, 2 * BOX)
        lane = lax.broadcasted_iota(jnp.int32, m2.shape, 2)
        sign = jnp.where(lane < BOX, 1.0, -1.0).astype(jnp.float32)
        out = m2.astype(jnp.bfloat16).astype(jnp.float32)
        q2_ref[0, pl.ds(z0, chunk)] = out.astype(jnp.bfloat16)
        swapped = sign * pltpu.roll(out, BOX, 2)
        q2_ref[1, pl.ds(z0, chunk)] = swapped.astype(jnp.bfloat16)
        return carry

    lax.fori_loop(0, depth // chunk, transform_chunk, 0)


def window_bands(corner, length):
    lower_edge = jnp.arange(SHIFT, dtype=jnp.int32)[None, :, None] + shift_anchor() + corner[:, None, None]
    cell_index = jnp.arange(length, dtype=jnp.int32)[None, None, :]
    return ((cell_index >= lower_edge) & (cell_index < lower_edge + TMPL)).astype(jnp.float32)


def block_rms(tomogram, corner_z, corner_y, corner_x):
    depth, rows_y, width = tomogram.shape
    count = corner_z.shape[0]
    hi = lax.Precision.HIGHEST
    values = tomogram.astype(jnp.float32)
    squares = (values * values).reshape(depth * rows_y, width)
    square_hi = bf(squares)
    square_lo = bf(squares - square_hi.astype(jnp.float32))
    band_x = bf(window_bands(corner_x, width).reshape(count * SHIFT, width).T)
    sums_x = jnp.dot(square_hi, band_x, preferred_element_type=jnp.float32)
    sums_x = sums_x + jnp.dot(square_lo, band_x, preferred_element_type=jnp.float32)
    sums_x = sums_x.reshape(depth, rows_y, count, SHIFT)
    band_y = window_bands(corner_y, rows_y)
    sums_y = jnp.einsum("zynu,nty->nztu", sums_x, band_y, precision=hi)
    band_z = window_bands(corner_z, depth)
    sums_z = jnp.einsum("nztu,nsz->nstu", sums_y, band_z, precision=hi)
    return jnp.sqrt(sums_z / float(TMPL**3) + epsilon)


def front(tomogram, corner_z, corner_y, corner_x):
    count = corner_z.shape[0]
    rows_y = tomogram.shape[1]
    width = tomogram.shape[2]
    t1 = window_table(corner_x, width).reshape(count, width, 2 * BOX)
    pos_y = jnp.arange(rows_y, dtype=jnp.int32)[None, :] - corner_y[:, None]
    inside_y = (pos_y >= 0) & (pos_y < BOX)
    j = jnp.arange(BOX, dtype=jnp.int32)
    turn_y = pos_y[:, :, None] * j[None, None, :] % BOX
    angle_y = angle_of(turn_y)
    zero = jnp.zeros((), jnp.bfloat16)
    cos_y = jnp.where(inside_y[:, :, None], bf(jnp.cos(angle_y)), zero)
    sin_y = jnp.where(inside_y[:, :, None], bf(jnp.sin(angle_y)), zero)
    l2 = jnp.concatenate(
        [jnp.concatenate([cos_y, -sin_y], axis=2), jnp.concatenate([sin_y, cos_y], axis=2)], axis=1
    )

    grid_spec = pltpu.PrefetchScalarGridSpec(
        num_scalar_prefetch=1,
        grid=(count,),
        in_specs=[
            pl.BlockSpec((pl.Element(BOX), pl.Element(rows_y), pl.Element(width)), lambda n, cz: (cz[n], 0, 0)),
            pl.BlockSpec((None, width, 2 * BOX), lambda n, cz: (n, 0, 0)),
            pl.BlockSpec((None, 2 * rows_y, 2 * BOX), lambda n, cz: (n, 0, 0)),
        ],
        out_specs=pl.BlockSpec((None, 2, BOX, BOX, 2 * BOX), lambda n, cz: (n, 0, 0, 0, 0)),
    )
    q2 = pl.pallas_call(
        front_kernel,
        grid_spec=grid_spec,
        out_shape=jax.ShapeDtypeStruct((count, 2, BOX, BOX, 2 * BOX), jnp.bfloat16),
        compiler_params=pltpu.CompilerParams(vmem_limit_bytes=48 * 1024 * 1024),
    )(corner_z, tomogram, t1, l2)
    return q2, block_rms(tomogram, corner_z, corner_y, corner_x)


def box_spectra_of(q2):
    cos_half, sin_half = phases(HALF, BOX, 0)
    l3 = jnp.stack([bf(cos_half).T, bf(sin_half).T], axis=0)
    return jnp.einsum("nwzkq,wzh->nhkq", q2, l3, preferred_element_type=jnp.float32)


def match_kj(spectrum_v, box_rms, spectra):
    spectra_kj = jnp.swapaxes(spectra, 3, 4)

    def one(spectrum):
        real_v = spectrum_v[..., :BOX]
        imag_v = spectrum_v[..., BOX:]
        real_t = spectrum[0].astype(jnp.float32)[None, None]
        imag_t = spectrum[1].astype(jnp.float32)[None, None]
        rv = real_v[:, None]
        iv = imag_v[:, None]
        real_p = real_t * rv + imag_t * iv
        imag_p = real_t * iv - imag_t * rv
        cross = jnp.stack([bf(real_p), bf(imag_p)], axis=2)
        cos_first, sin_first = phases(SHIFT, HALF, shift_anchor())
        freq_index = jnp.arange(HALF, dtype=jnp.int32)
        weight = jnp.where(freq_index % (BOX // 2) == 0, 1.0, 2.0) / float(BOX**3)
        t_first = complex_table(cos_first * weight[None, :], sin_first * weight[None, :], -1.0, 1.0)
        stage_g = section("nrchkj,chds->nrdskj", cross, t_first)
        cos_rest, sin_rest = phases(SHIFT, BOX, shift_anchor())
        t_mid = complex_table(cos_rest, sin_rest, -1.0, 1.0)
        stage_h = section("nrcskj,cjdt->nrdskt", stage_g, t_mid)
        t_last = jnp.stack([bf(cos_rest).T, -bf(sin_rest).T], axis=0)
        correlation = section("nrcskt,cku->nrstu", stage_h, t_last)
        scores = correlation / (box_rms[:, None] * math.sqrt(float(TMPL**3)))
        return jnp.max(scores, axis=(2, 3, 4))[:, 0]

    count_r = spectra_kj.shape[0]
    group = min(4, count_r)

    def one_group(block):
        return jnp.stack([one(block[i]) for i in range(group)], axis=0)

    blocks = spectra_kj.reshape((count_r // group, group) + spectra_kj.shape[1:])
    if count_r == group:
        values = one_group(blocks[0])
    else:
        values = lax.map(one_group, blocks).reshape((count_r,) + (spectrum_v.shape[0],))
    return values.T


def per_device(tomogram, templates, corner_z, corner_y, corner_x, loads):
    own_total = corner_z.shape[1]
    live_count = jnp.sum(loads[0, 0])
    q2, box_rms = front(tomogram, corner_z[0], corner_y[0], corner_x[0])
    spectrum_v = box_spectra_of(q2)

    all_templates = lax.all_gather(templates, "orient", axis=0, tiled=True)
    spectra = template_spectra(all_templates.reshape(-1, TMPL, TMPL, TMPL))
    values = match_kj(spectrum_v, box_rms, spectra)
    live = jnp.arange(own_total, dtype=jnp.int32) < live_count
    matched = jnp.where(live[:, None], values, 0.0)
    return (matched[None], jnp.max(matched, axis=1)[None])


def solution(mesh):
    return jax.shard_map(
        per_device,
        mesh=mesh,
        in_specs=(
            P("vol", "orient", None),
            P("orient", None, None),
            P("vol", "orient"),
            P("vol", "orient"),
            P("vol", "orient"),
            P("vol", "orient", None),
        ),
        out_specs=(P("vol", "orient", None), P("vol", "orient")),
        check_vma=False,
    )
```

```python
import math

import jax
import jax.numpy as jnp
from jax import lax
from jax.sharding import PartitionSpec as P
from jax.experimental import pallas as pl
from jax.experimental.pallas import tpu as pltpu

BOX = 64
TMPL = 32
SHIFT = 8
HALF = 33


epsilon = 1e-05


def shift_anchor():
    return (BOX - TMPL) // 2 - SHIFT // 2


def angle_of(turn_index):
    return turn_index.astype(jnp.float32) * (2.0 * math.pi / BOX)


def phases(count_out, count_in, offset):
    out_index = jnp.arange(count_out, dtype=jnp.int32) + offset
    in_index = jnp.arange(count_in, dtype=jnp.int32)
    turn_index = out_index[:, None] * in_index[None, :] % BOX
    phase_angle = angle_of(turn_index)
    return (jnp.cos(phase_angle), jnp.sin(phase_angle))


def bf(x):
    return x.astype(jnp.bfloat16)


def complex_table(cos_t, sin_t, sign_re_from_im, sign_im_from_re):
    c = bf(cos_t).T
    s = bf(sin_t).T
    re_row = jnp.stack([c, sign_im_from_re * s], axis=1)
    im_row = jnp.stack([sign_re_from_im * s, c], axis=1)
    return jnp.stack([re_row, im_row], axis=0)


def section(pattern, operand, table):
    return jnp.einsum(pattern, bf(operand), table, preferred_element_type=jnp.float32)


def forward_tail(stage_one):
    length_a = stage_one.shape[2]
    length_y = stage_one.shape[3]
    cos_full, sin_full = phases(BOX, length_y, 0)
    t_mid = complex_table(cos_full, sin_full, 1.0, -1.0)
    stage_two = section("ncayk,cydj->ndajk", stage_one, t_mid)
    cos_half, sin_half = phases(HALF, length_a, 0)
    t_first = complex_table(cos_half, sin_half, 1.0, -1.0)
    return section("ncajk,cadh->ndhjk", stage_two, t_first)


def template_spectra(cubes):
    volume = cubes.astype(jnp.float32)
    count = volume.shape[0]
    flat = volume.reshape(count, -1)
    centred = flat - jnp.mean(flat, axis=1, keepdims=True)
    unit = centred / jnp.sqrt(jnp.mean(centred * centred, axis=1, keepdims=True) + epsilon)
    cos_full, sin_full = phases(BOX, TMPL, 0)
    c_full = bf(cos_full).T
    s_full = bf(sin_full).T
    t_last = jnp.concatenate([c_full, -s_full], axis=1)
    stage_one = jnp.dot(bf(unit).reshape(count * TMPL * TMPL, TMPL), t_last, preferred_element_type=jnp.float32)
    stage_one = bf(stage_one).reshape(count, TMPL, TMPL, 2, BOX)
    stacked = jnp.transpose(stage_one, (0, 1, 4, 3, 2)).reshape(count * TMPL * BOX, 2 * TMPL)
    t_mid = jnp.concatenate(
        [jnp.concatenate([c_full, -s_full], axis=1), jnp.concatenate([s_full, c_full], axis=1)], axis=0
    )
    stage_two = jnp.dot(stacked, t_mid, preferred_element_type=jnp.float32)
    stage_two = bf(stage_two).reshape(count, TMPL, BOX, 2 * BOX)
    swapped = jnp.concatenate([stage_two[..., BOX:], -stage_two[..., :BOX]], axis=-1)
    pair = jnp.stack([stage_two, swapped], axis=1)
    cos_half, sin_half = phases(HALF, TMPL, 0)
    t_first = jnp.stack([bf(cos_half).T, bf(sin_half).T], axis=0)
    return bf(jnp.einsum("rwakq,wah->rhkq", pair, t_first, preferred_element_type=jnp.float32))


def window_table(corner_x, width):
    pos = jnp.arange(width, dtype=jnp.int32)[None, :] - corner_x[:, None]
    inside = (pos >= 0) & (pos < BOX)
    k = jnp.arange(BOX, dtype=jnp.int32)
    turn = k[None, None, :] * pos[:, :, None] % BOX
    phase_angle = angle_of(turn)
    mask = inside[:, :, None]
    cos_t = jnp.where(mask, bf(jnp.cos(phase_angle)), jnp.zeros((), jnp.bfloat16))
    sin_t = jnp.where(mask, -bf(jnp.sin(phase_angle)), jnp.zeros((), jnp.bfloat16))
    return jnp.stack([cos_t, sin_t], axis=2)


def band_table():
    lower_edge = jnp.arange(SHIFT, dtype=jnp.int32)[:, None] + shift_anchor()
    cell_index = jnp.arange(BOX, dtype=jnp.int32)[None, :]
    return ((cell_index >= lower_edge) & (cell_index < lower_edge + TMPL)).astype(jnp.float32)


def window_band(corner_x, width):
    lower_edge = jnp.arange(SHIFT, dtype=jnp.int32)[None, :, None] + shift_anchor() + corner_x[:, None, None]
    cell_index = jnp.arange(width, dtype=jnp.int32)[None, None, :]
    return ((cell_index >= lower_edge) & (cell_index < lower_edge + TMPL)).astype(jnp.float32)


def window_rms(rows, corner_x):
    width = rows.shape[-1]
    squares = rows.astype(jnp.float32) ** 2
    band_x = window_band(corner_x, width)
    band = band_table()
    hi = lax.Precision.HIGHEST
    sums_c = jnp.einsum("nabx,nux->nabu", squares, band_x, precision=hi)
    sums_b = jnp.einsum("nabu,tb->natu", sums_c, band, precision=hi)
    sums_a = jnp.einsum("natu,sa->nstu", sums_b, band, precision=hi)
    return jnp.sqrt(sums_a / float(TMPL**3) + epsilon)


def match(box_spectra, box_rms, spectra):
    values = lax.map(lambda one: match_one(box_spectra, box_rms, one[None]), spectra)
    return values[:, :, 0].T


def match_one(box_spectra, box_rms, spectra):
    real_t = spectra[:, 0].astype(jnp.float32)[None]
    imag_t = spectra[:, 1].astype(jnp.float32)[None]
    real_v = box_spectra[:, 0][:, None]
    imag_v = box_spectra[:, 1][:, None]
    real_p = real_t * real_v + imag_t * imag_v
    imag_p = real_t * imag_v - imag_t * real_v
    cross = jnp.stack([bf(real_p), bf(imag_p)], axis=2)
    cos_first, sin_first = phases(SHIFT, HALF, shift_anchor())
    freq_index = jnp.arange(HALF, dtype=jnp.int32)
    weight = jnp.where(freq_index % (BOX // 2) == 0, 1.0, 2.0) / float(BOX**3)
    cos_first = cos_first * weight[None, :]
    sin_first = sin_first * weight[None, :]
    t_first = complex_table(cos_first, sin_first, -1.0, 1.0)
    stage_g = section("nrchjk,chds->nrdsjk", cross, t_first)
    cos_rest, sin_rest = phases(SHIFT, BOX, shift_anchor())
    t_mid = complex_table(cos_rest, sin_rest, -1.0, 1.0)
    stage_h = section("nrcsjk,cjdt->nrdstk", stage_g, t_mid)
    t_last = jnp.stack([bf(cos_rest).T, -bf(sin_rest).T], axis=0)
    correlation = section("nrcstk,cku->nrstu", stage_h, t_last)
    scores = correlation / (box_rms[:, None] * math.sqrt(float(TMPL**3)))
    return jnp.max(scores, axis=(2, 3, 4))


def front_kernel(cz_ref, slab_ref, t1_ref, l2_ref, q2_ref):
    depth, rows_y, width = slab_ref.shape
    chunk = 8
    t1 = t1_ref[...]
    l2 = l2_ref[...]

    def transform_chunk(ci, carry):
        z0 = pl.multiple_of(ci * chunk, chunk)
        rows = slab_ref[pl.ds(z0, chunk)].reshape(chunk * rows_y, width)
        p1 = jnp.dot(rows, t1, preferred_element_type=jnp.float32)
        p1 = p1.astype(jnp.bfloat16).astype(jnp.float32).reshape(chunk, rows_y, 2 * BOX)
        p1t = jnp.swapaxes(p1, 1, 2)
        stacked = jnp.concatenate([p1t[:, :BOX], p1t[:, BOX:]], axis=2)
        stacked = stacked.reshape(chunk * BOX, 2 * rows_y).astype(jnp.bfloat16)
        m2 = jnp.dot(stacked, l2, preferred_element_type=jnp.float32).reshape(chunk, BOX, 2 * BOX)
        lane = lax.broadcasted_iota(jnp.int32, m2.shape, 2)
        sign = jnp.where(lane < BOX, 1.0, -1.0).astype(jnp.float32)
        out = m2.astype(jnp.bfloat16).astype(jnp.float32)
        q2_ref[0, pl.ds(z0, chunk)] = out.astype(jnp.bfloat16)
        swapped = sign * pltpu.roll(out, BOX, 2)
        q2_ref[1, pl.ds(z0, chunk)] = swapped.astype(jnp.bfloat16)
        return carry

    lax.fori_loop(0, depth // chunk, transform_chunk, 0)


def window_bands(corner, length):
    lower_edge = jnp.arange(SHIFT, dtype=jnp.int32)[None, :, None] + shift_anchor() + corner[:, None, None]
    cell_index = jnp.arange(length, dtype=jnp.int32)[None, None, :]
    return ((cell_index >= lower_edge) & (cell_index < lower_edge + TMPL)).astype(jnp.float32)


def block_rms(tomogram, corner_z, corner_y, corner_x):
    depth, rows_y, width = tomogram.shape
    count = corner_z.shape[0]
    hi = lax.Precision.HIGHEST
    values = tomogram.astype(jnp.float32)
    squares = (values * values).reshape(depth * rows_y, width)
    square_hi = bf(squares)
    square_lo = bf(squares - square_hi.astype(jnp.float32))
    band_x = bf(window_bands(corner_x, width).reshape(count * SHIFT, width).T)
    sums_x = jnp.dot(square_hi, band_x, preferred_element_type=jnp.float32)
    sums_x = sums_x + jnp.dot(square_lo, band_x, preferred_element_type=jnp.float32)
    sums_x = sums_x.reshape(depth, rows_y, count, SHIFT)
    band_y = window_bands(corner_y, rows_y)
    sums_y = jnp.einsum("zynu,nty->nztu", sums_x, band_y, precision=hi)
    band_z = window_bands(corner_z, depth)
    sums_z = jnp.einsum("nztu,nsz->nstu", sums_y, band_z, precision=hi)
    return jnp.sqrt(sums_z / float(TMPL**3) + epsilon)


def front(tomogram, corner_z, corner_y, corner_x):
    count = corner_z.shape[0]
    rows_y = tomogram.shape[1]
    width = tomogram.shape[2]
    t1 = window_table(corner_x, width).reshape(count, width, 2 * BOX)
    pos_y = jnp.arange(rows_y, dtype=jnp.int32)[None, :] - corner_y[:, None]
    inside_y = (pos_y >= 0) & (pos_y < BOX)
    j = jnp.arange(BOX, dtype=jnp.int32)
    turn_y = pos_y[:, :, None] * j[None, None, :] % BOX
    angle_y = angle_of(turn_y)
    zero = jnp.zeros((), jnp.bfloat16)
    cos_y = jnp.where(inside_y[:, :, None], bf(jnp.cos(angle_y)), zero)
    sin_y = jnp.where(inside_y[:, :, None], bf(jnp.sin(angle_y)), zero)
    l2 = jnp.concatenate(
        [jnp.concatenate([cos_y, -sin_y], axis=2), jnp.concatenate([sin_y, cos_y], axis=2)], axis=1
    )

    grid_spec = pltpu.PrefetchScalarGridSpec(
        num_scalar_prefetch=1,
        grid=(count,),
        in_specs=[
            pl.BlockSpec((pl.Element(BOX), pl.Element(rows_y), pl.Element(width)), lambda n, cz: (cz[n], 0, 0)),
            pl.BlockSpec((None, width, 2 * BOX), lambda n, cz: (n, 0, 0)),
            pl.BlockSpec((None, 2 * rows_y, 2 * BOX), lambda n, cz: (n, 0, 0)),
        ],
        out_specs=pl.BlockSpec((None, 2, BOX, BOX, 2 * BOX), lambda n, cz: (n, 0, 0, 0, 0)),
    )
    q2 = pl.pallas_call(
        front_kernel,
        grid_spec=grid_spec,
        out_shape=jax.ShapeDtypeStruct((count, 2, BOX, BOX, 2 * BOX), jnp.bfloat16),
        compiler_params=pltpu.CompilerParams(vmem_limit_bytes=48 * 1024 * 1024),
    )(corner_z, tomogram, t1, l2)
    return q2, block_rms(tomogram, corner_z, corner_y, corner_x)


def box_spectra_of(q2):
    cos_half, sin_half = phases(HALF, BOX, 0)
    l3 = jnp.stack([bf(cos_half).T, bf(sin_half).T], axis=0)
    return jnp.einsum("nwzkq,wzh->nhkq", q2, l3, preferred_element_type=jnp.float32)


def match_kj(spectrum_v, box_rms, spectra):
    spectra_kj = spectra

    def one(spectrum):
        real_v = spectrum_v[..., :BOX]
        imag_v = spectrum_v[..., BOX:]
        real_t = spectrum[..., :BOX].astype(jnp.float32)[None, None]
        imag_t = spectrum[..., BOX:].astype(jnp.float32)[None, None]
        rv = real_v[:, None]
        iv = imag_v[:, None]
        real_p = real_t * rv + imag_t * iv
        imag_p = real_t * iv - imag_t * rv
        cross = jnp.stack([bf(real_p), bf(imag_p)], axis=2)
        cos_first, sin_first = phases(SHIFT, HALF, shift_anchor())
        freq_index = jnp.arange(HALF, dtype=jnp.int32)
        weight = jnp.where(freq_index % (BOX // 2) == 0, 1.0, 2.0) / float(BOX**3)
        t_first = complex_table(cos_first * weight[None, :], sin_first * weight[None, :], -1.0, 1.0)
        stage_g = section("nrchkj,chds->nrdskj", cross, t_first)
        cos_rest, sin_rest = phases(SHIFT, BOX, shift_anchor())
        t_mid = complex_table(cos_rest, sin_rest, -1.0, 1.0)
        stage_h = section("nrcskj,cjdt->nrdskt", stage_g, t_mid)
        t_last = jnp.stack([bf(cos_rest).T, -bf(sin_rest).T], axis=0)
        correlation = section("nrcskt,cku->nrstu", stage_h, t_last)
        scores = correlation / (box_rms[:, None] * math.sqrt(float(TMPL**3)))
        return jnp.max(scores, axis=(2, 3, 4))[:, 0]

    count_r = spectra_kj.shape[0]
    group = min(4, count_r)

    def one_group(block):
        return jnp.stack([one(block[i]) for i in range(group)], axis=0)

    blocks = spectra_kj.reshape((count_r // group, group) + spectra_kj.shape[1:])
    if count_r == group:
        values = one_group(blocks[0])
    else:
        values = lax.map(one_group, blocks).reshape((count_r,) + (spectrum_v.shape[0],))
    return values.T


def per_device(tomogram, templates, corner_z, corner_y, corner_x, loads):
    own_total = corner_z.shape[1]
    live_count = jnp.sum(loads[0, 0])
    q2, box_rms = front(tomogram, corner_z[0], corner_y[0], corner_x[0])
    spectrum_v = box_spectra_of(q2)

    all_templates = lax.all_gather(templates, "orient", axis=0, tiled=True)
    spectra = template_spectra(all_templates.reshape(-1, TMPL, TMPL, TMPL))
    values = match_kj(spectrum_v, box_rms, spectra)
    live = jnp.arange(own_total, dtype=jnp.int32) < live_count
    matched = jnp.where(live[:, None], values, 0.0)
    return (matched[None], jnp.max(matched, axis=1)[None])


def solution(mesh):
    return jax.shard_map(
        per_device,
        mesh=mesh,
        in_specs=(
            P("vol", "orient", None),
            P("orient", None, None),
            P("vol", "orient"),
            P("vol", "orient"),
            P("vol", "orient"),
            P("vol", "orient", None),
        ),
        out_specs=(P("vol", "orient", None), P("vol", "orient")),
        check_vma=False,
    )
```

```python
import math

import jax
import jax.numpy as jnp
from jax import lax
from jax.sharding import PartitionSpec as P
from jax.experimental import pallas as pl
from jax.experimental.pallas import tpu as pltpu

BOX = 64
TMPL = 32
SHIFT = 8
HALF = 33


epsilon = 1e-05


def shift_anchor():
    return (BOX - TMPL) // 2 - SHIFT // 2


def angle_of(turn_index):
    return turn_index.astype(jnp.float32) * (2.0 * math.pi / BOX)


def phases(count_out, count_in, offset):
    out_index = jnp.arange(count_out, dtype=jnp.int32) + offset
    in_index = jnp.arange(count_in, dtype=jnp.int32)
    turn_index = out_index[:, None] * in_index[None, :] % BOX
    phase_angle = angle_of(turn_index)
    return (jnp.cos(phase_angle), jnp.sin(phase_angle))


def bf(x):
    return x.astype(jnp.bfloat16)


def complex_table(cos_t, sin_t, sign_re_from_im, sign_im_from_re):
    c = bf(cos_t).T
    s = bf(sin_t).T
    re_row = jnp.stack([c, sign_im_from_re * s], axis=1)
    im_row = jnp.stack([sign_re_from_im * s, c], axis=1)
    return jnp.stack([re_row, im_row], axis=0)


def section(pattern, operand, table):
    return jnp.einsum(pattern, bf(operand), table, preferred_element_type=jnp.float32)


def forward_tail(stage_one):
    length_a = stage_one.shape[2]
    length_y = stage_one.shape[3]
    cos_full, sin_full = phases(BOX, length_y, 0)
    t_mid = complex_table(cos_full, sin_full, 1.0, -1.0)
    stage_two = section("ncayk,cydj->ndajk", stage_one, t_mid)
    cos_half, sin_half = phases(HALF, length_a, 0)
    t_first = complex_table(cos_half, sin_half, 1.0, -1.0)
    return section("ncajk,cadh->ndhjk", stage_two, t_first)


def template_spectra(cubes):
    volume = cubes.astype(jnp.float32)
    count = volume.shape[0]
    flat = volume.reshape(count, -1)
    centred = flat - jnp.mean(flat, axis=1, keepdims=True)
    unit = centred / jnp.sqrt(jnp.mean(centred * centred, axis=1, keepdims=True) + epsilon)
    cos_full, sin_full = phases(BOX, TMPL, 0)
    c_full = bf(cos_full).T
    s_full = bf(sin_full).T
    t_last = jnp.concatenate([c_full, -s_full], axis=1)
    stage_one = jnp.dot(bf(unit).reshape(count * TMPL * TMPL, TMPL), t_last, preferred_element_type=jnp.float32)
    stage_one = bf(stage_one).reshape(count, TMPL, TMPL, 2, BOX)
    stacked = jnp.transpose(stage_one, (0, 1, 4, 3, 2)).reshape(count * TMPL * BOX, 2 * TMPL)
    t_mid = jnp.concatenate(
        [jnp.concatenate([c_full, -s_full], axis=1), jnp.concatenate([s_full, c_full], axis=1)], axis=0
    )
    stage_two = jnp.dot(stacked, t_mid, preferred_element_type=jnp.float32)
    stage_two = bf(stage_two).reshape(count, TMPL, BOX, 2 * BOX)
    swapped = jnp.concatenate([stage_two[..., BOX:], -stage_two[..., :BOX]], axis=-1)
    pair = jnp.stack([stage_two, swapped], axis=1)
    cos_half, sin_half = phases(HALF, TMPL, 0)
    t_first = jnp.stack([bf(cos_half).T, bf(sin_half).T], axis=0)
    return bf(jnp.einsum("rwakq,wah->rhkq", pair, t_first, preferred_element_type=jnp.float32))


def window_table(corner_x, width):
    pos = jnp.arange(width, dtype=jnp.int32)[None, :] - corner_x[:, None]
    inside = (pos >= 0) & (pos < BOX)
    k = jnp.arange(BOX, dtype=jnp.int32)
    turn = k[None, None, :] * pos[:, :, None] % BOX
    phase_angle = angle_of(turn)
    mask = inside[:, :, None]
    cos_t = jnp.where(mask, bf(jnp.cos(phase_angle)), jnp.zeros((), jnp.bfloat16))
    sin_t = jnp.where(mask, -bf(jnp.sin(phase_angle)), jnp.zeros((), jnp.bfloat16))
    return jnp.stack([cos_t, sin_t], axis=2)


def band_table():
    lower_edge = jnp.arange(SHIFT, dtype=jnp.int32)[:, None] + shift_anchor()
    cell_index = jnp.arange(BOX, dtype=jnp.int32)[None, :]
    return ((cell_index >= lower_edge) & (cell_index < lower_edge + TMPL)).astype(jnp.float32)


def window_band(corner_x, width):
    lower_edge = jnp.arange(SHIFT, dtype=jnp.int32)[None, :, None] + shift_anchor() + corner_x[:, None, None]
    cell_index = jnp.arange(width, dtype=jnp.int32)[None, None, :]
    return ((cell_index >= lower_edge) & (cell_index < lower_edge + TMPL)).astype(jnp.float32)


def window_rms(rows, corner_x):
    width = rows.shape[-1]
    squares = rows.astype(jnp.float32) ** 2
    band_x = window_band(corner_x, width)
    band = band_table()
    hi = lax.Precision.HIGHEST
    sums_c = jnp.einsum("nabx,nux->nabu", squares, band_x, precision=hi)
    sums_b = jnp.einsum("nabu,tb->natu", sums_c, band, precision=hi)
    sums_a = jnp.einsum("natu,sa->nstu", sums_b, band, precision=hi)
    return jnp.sqrt(sums_a / float(TMPL**3) + epsilon)


def match(box_spectra, box_rms, spectra):
    values = lax.map(lambda one: match_one(box_spectra, box_rms, one[None]), spectra)
    return values[:, :, 0].T


def match_one(box_spectra, box_rms, spectra):
    real_t = spectra[:, 0].astype(jnp.float32)[None]
    imag_t = spectra[:, 1].astype(jnp.float32)[None]
    real_v = box_spectra[:, 0][:, None]
    imag_v = box_spectra[:, 1][:, None]
    real_p = real_t * real_v + imag_t * imag_v
    imag_p = real_t * imag_v - imag_t * real_v
    cross = jnp.stack([bf(real_p), bf(imag_p)], axis=2)
    cos_first, sin_first = phases(SHIFT, HALF, shift_anchor())
    freq_index = jnp.arange(HALF, dtype=jnp.int32)
    weight = jnp.where(freq_index % (BOX // 2) == 0, 1.0, 2.0) / float(BOX**3)
    cos_first = cos_first * weight[None, :]
    sin_first = sin_first * weight[None, :]
    t_first = complex_table(cos_first, sin_first, -1.0, 1.0)
    stage_g = section("nrchjk,chds->nrdsjk", cross, t_first)
    cos_rest, sin_rest = phases(SHIFT, BOX, shift_anchor())
    t_mid = complex_table(cos_rest, sin_rest, -1.0, 1.0)
    stage_h = section("nrcsjk,cjdt->nrdstk", stage_g, t_mid)
    t_last = jnp.stack([bf(cos_rest).T, -bf(sin_rest).T], axis=0)
    correlation = section("nrcstk,cku->nrstu", stage_h, t_last)
    scores = correlation / (box_rms[:, None] * math.sqrt(float(TMPL**3)))
    return jnp.max(scores, axis=(2, 3, 4))


def front_kernel(cz_ref, ys_ref, slab_ref, t1_ref, l2_ref, q2_ref):
    depth, window_y, width = slab_ref.shape
    rows_y = 2 * BOX
    chunk = 8
    t1 = t1_ref[...]
    l2 = l2_ref[...]

    def transform_chunk(ci, carry):
        z0 = pl.multiple_of(ci * chunk, chunk)
        rows = slab_ref[pl.ds(z0, chunk)].reshape(chunk * window_y, width)
        p1 = jnp.dot(rows, t1, preferred_element_type=jnp.float32)
        p1 = p1.astype(jnp.bfloat16).astype(jnp.float32).reshape(chunk, window_y, 2 * BOX)
        pad = jnp.zeros((chunk, rows_y - window_y, 2 * BOX), jnp.float32)
        p1 = jnp.concatenate([p1, pad], axis=1)
        p1t = jnp.swapaxes(p1, 1, 2)
        stacked = jnp.concatenate([p1t[:, :BOX], p1t[:, BOX:]], axis=2)
        stacked = stacked.reshape(chunk * BOX, 2 * rows_y).astype(jnp.bfloat16)
        m2 = jnp.dot(stacked, l2, preferred_element_type=jnp.float32).reshape(chunk, BOX, 2 * BOX)
        lane = lax.broadcasted_iota(jnp.int32, m2.shape, 2)
        sign = jnp.where(lane < BOX, 1.0, -1.0).astype(jnp.float32)
        out = m2.astype(jnp.bfloat16).astype(jnp.float32)
        q2_ref[0, pl.ds(z0, chunk)] = out.astype(jnp.bfloat16)
        swapped = sign * pltpu.roll(out, BOX, 2)
        q2_ref[1, pl.ds(z0, chunk)] = swapped.astype(jnp.bfloat16)
        return carry

    lax.fori_loop(0, depth // chunk, transform_chunk, 0)


def window_bands(corner, length):
    lower_edge = jnp.arange(SHIFT, dtype=jnp.int32)[None, :, None] + shift_anchor() + corner[:, None, None]
    cell_index = jnp.arange(length, dtype=jnp.int32)[None, None, :]
    return ((cell_index >= lower_edge) & (cell_index < lower_edge + TMPL)).astype(jnp.float32)


def block_rms(tomogram, corner_z, corner_y, corner_x):
    depth, rows_y, width = tomogram.shape
    count = corner_z.shape[0]
    hi = lax.Precision.HIGHEST
    values = tomogram.astype(jnp.float32)
    squares = (values * values).reshape(depth * rows_y, width)
    square_hi = bf(squares)
    square_lo = bf(squares - square_hi.astype(jnp.float32))
    band_x = bf(window_bands(corner_x, width).reshape(count * SHIFT, width).T)
    sums_x = jnp.dot(square_hi, band_x, preferred_element_type=jnp.float32)
    sums_x = sums_x + jnp.dot(square_lo, band_x, preferred_element_type=jnp.float32)
    sums_x = sums_x.reshape(depth, rows_y, count, SHIFT)
    band_y = window_bands(corner_y, rows_y)
    sums_y = jnp.einsum("zynu,nty->nztu", sums_x, band_y, precision=hi)
    band_z = window_bands(corner_z, depth)
    sums_z = jnp.einsum("nztu,nsz->nstu", sums_y, band_z, precision=hi)
    return jnp.sqrt(sums_z / float(TMPL**3) + epsilon)


def front(tomogram, corner_z, corner_y, corner_x):
    count = corner_z.shape[0]
    block_y = tomogram.shape[1]
    window_y = BOX + 16
    rows_y = 2 * BOX
    width = tomogram.shape[2]
    start_y = jnp.minimum((corner_y // 16) * 16, block_y - window_y).astype(jnp.int32)
    t1 = window_table(corner_x, width).reshape(count, width, 2 * BOX)
    pos_y = jnp.arange(rows_y, dtype=jnp.int32)[None, :] - (corner_y - start_y)[:, None]
    inside_y = (pos_y >= 0) & (pos_y < BOX)
    j = jnp.arange(BOX, dtype=jnp.int32)
    turn_y = pos_y[:, :, None] * j[None, None, :] % BOX
    angle_y = angle_of(turn_y)
    zero = jnp.zeros((), jnp.bfloat16)
    cos_y = jnp.where(inside_y[:, :, None], bf(jnp.cos(angle_y)), zero)
    sin_y = jnp.where(inside_y[:, :, None], bf(jnp.sin(angle_y)), zero)
    l2 = jnp.concatenate(
        [jnp.concatenate([cos_y, -sin_y], axis=2), jnp.concatenate([sin_y, cos_y], axis=2)], axis=1
    )

    grid_spec = pltpu.PrefetchScalarGridSpec(
        num_scalar_prefetch=2,
        grid=(count,),
        in_specs=[
            pl.BlockSpec(
                (pl.Element(BOX), pl.Element(window_y), pl.Element(width)), lambda n, cz, ys: (cz[n], pl.multiple_of(ys[n], 16), 0)
            ),
            pl.BlockSpec((None, width, 2 * BOX), lambda n, cz, ys: (n, 0, 0)),
            pl.BlockSpec((None, 2 * rows_y, 2 * BOX), lambda n, cz, ys: (n, 0, 0)),
        ],
        out_specs=pl.BlockSpec((None, 2, BOX, BOX, 2 * BOX), lambda n, cz, ys: (n, 0, 0, 0, 0)),
    )
    q2 = pl.pallas_call(
        front_kernel,
        grid_spec=grid_spec,
        out_shape=jax.ShapeDtypeStruct((count, 2, BOX, BOX, 2 * BOX), jnp.bfloat16),
        compiler_params=pltpu.CompilerParams(vmem_limit_bytes=48 * 1024 * 1024),
    )(corner_z, start_y, tomogram, t1, l2)
    return q2, block_rms(tomogram, corner_z, corner_y, corner_x)


def box_spectra_of(q2):
    cos_half, sin_half = phases(HALF, BOX, 0)
    l3 = jnp.stack([bf(cos_half).T, bf(sin_half).T], axis=0)
    return bf(jnp.einsum("nwzkq,wzh->nhkq", q2, l3, preferred_element_type=jnp.float32))


def match_kj(spectrum_v, box_rms, spectra):
    spectra_kj = spectra

    def one(spectrum):
        real_v = spectrum_v[..., :BOX]
        imag_v = spectrum_v[..., BOX:]
        real_t = spectrum[..., :BOX].astype(jnp.float32)[None, None]
        imag_t = spectrum[..., BOX:].astype(jnp.float32)[None, None]
        rv = real_v[:, None]
        iv = imag_v[:, None]
        real_p = real_t * rv + imag_t * iv
        imag_p = real_t * iv - imag_t * rv
        cross = jnp.stack([bf(real_p), bf(imag_p)], axis=2)
        cos_first, sin_first = phases(SHIFT, HALF, shift_anchor())
        freq_index = jnp.arange(HALF, dtype=jnp.int32)
        weight = jnp.where(freq_index % (BOX // 2) == 0, 1.0, 2.0) / float(BOX**3)
        t_first = complex_table(cos_first * weight[None, :], sin_first * weight[None, :], -1.0, 1.0)
        stage_g = section("nrchkj,chds->nrdskj", cross, t_first)
        cos_rest, sin_rest = phases(SHIFT, BOX, shift_anchor())
        t_mid = complex_table(cos_rest, sin_rest, -1.0, 1.0)
        stage_h = section("nrcskj,cjdt->nrdskt", stage_g, t_mid)
        t_last = jnp.stack([bf(cos_rest).T, -bf(sin_rest).T], axis=0)
        correlation = section("nrcskt,cku->nrstu", stage_h, t_last)
        scores = correlation / (box_rms[:, None] * math.sqrt(float(TMPL**3)))
        return jnp.max(scores, axis=(2, 3, 4))[:, 0]

    count_r = spectra_kj.shape[0]
    group = min(4, count_r)

    def one_group(block):
        return jnp.stack([one(block[i]) for i in range(group)], axis=0)

    blocks = spectra_kj.reshape((count_r // group, group) + spectra_kj.shape[1:])
    if count_r == group:
        values = one_group(blocks[0])
    else:
        values = lax.map(one_group, blocks).reshape((count_r,) + (spectrum_v.shape[0],))
    return values.T


def per_device(tomogram, templates, corner_z, corner_y, corner_x, loads):
    own_total = corner_z.shape[1]
    live_count = jnp.sum(loads[0, 0])
    q2, box_rms = front(tomogram, corner_z[0], corner_y[0], corner_x[0])
    spectrum_v = box_spectra_of(q2)

    all_templates = lax.all_gather(templates, "orient", axis=0, tiled=True)
    spectra = template_spectra(all_templates.reshape(-1, TMPL, TMPL, TMPL))
    values = match_kj(spectrum_v, box_rms, spectra)
    live = jnp.arange(own_total, dtype=jnp.int32) < live_count
    matched = jnp.where(live[:, None], values, 0.0)
    return (matched[None], jnp.max(matched, axis=1)[None])


def solution(mesh):
    return jax.shard_map(
        per_device,
        mesh=mesh,
        in_specs=(
            P("vol", "orient", None),
            P("orient", None, None),
            P("vol", "orient"),
            P("vol", "orient"),
            P("vol", "orient"),
            P("vol", "orient", None),
        ),
        out_specs=(P("vol", "orient", None), P("vol", "orient")),
        check_vma=False,
    )
```

```python
import math

import jax
import jax.numpy as jnp
from jax import lax
from jax.sharding import PartitionSpec as P
from jax.experimental import pallas as pl
from jax.experimental.pallas import tpu as pltpu

BOX = 64
TMPL = 32
SHIFT = 8
HALF = 33


epsilon = 1e-05


def shift_anchor():
    return (BOX - TMPL) // 2 - SHIFT // 2


def angle_of(turn_index):
    return turn_index.astype(jnp.float32) * (2.0 * math.pi / BOX)


def phases(count_out, count_in, offset):
    out_index = jnp.arange(count_out, dtype=jnp.int32) + offset
    in_index = jnp.arange(count_in, dtype=jnp.int32)
    turn_index = out_index[:, None] * in_index[None, :] % BOX
    phase_angle = angle_of(turn_index)
    return (jnp.cos(phase_angle), jnp.sin(phase_angle))


def bf(x):
    return x.astype(jnp.bfloat16)


def complex_table(cos_t, sin_t, sign_re_from_im, sign_im_from_re):
    c = bf(cos_t).T
    s = bf(sin_t).T
    re_row = jnp.stack([c, sign_im_from_re * s], axis=1)
    im_row = jnp.stack([sign_re_from_im * s, c], axis=1)
    return jnp.stack([re_row, im_row], axis=0)


def section(pattern, operand, table):
    return jnp.einsum(pattern, bf(operand), table, preferred_element_type=jnp.float32)


def forward_tail(stage_one):
    length_a = stage_one.shape[2]
    length_y = stage_one.shape[3]
    cos_full, sin_full = phases(BOX, length_y, 0)
    t_mid = complex_table(cos_full, sin_full, 1.0, -1.0)
    stage_two = section("ncayk,cydj->ndajk", stage_one, t_mid)
    cos_half, sin_half = phases(HALF, length_a, 0)
    t_first = complex_table(cos_half, sin_half, 1.0, -1.0)
    return section("ncajk,cadh->ndhjk", stage_two, t_first)


def template_spectra(cubes):
    volume = cubes.astype(jnp.float32)
    count = volume.shape[0]
    flat = volume.reshape(count, -1)
    centred = flat - jnp.mean(flat, axis=1, keepdims=True)
    unit = centred / jnp.sqrt(jnp.mean(centred * centred, axis=1, keepdims=True) + epsilon)
    cos_full, sin_full = phases(BOX, TMPL, 0)
    c_full = bf(cos_full).T
    s_full = bf(sin_full).T
    t_last = jnp.concatenate([c_full, -s_full], axis=1)
    stage_one = jnp.dot(bf(unit).reshape(count * TMPL * TMPL, TMPL), t_last, preferred_element_type=jnp.float32)
    stage_one = bf(stage_one).reshape(count, TMPL, TMPL, 2, BOX)
    stacked = jnp.transpose(stage_one, (0, 1, 4, 3, 2)).reshape(count * TMPL * BOX, 2 * TMPL)
    t_mid = jnp.concatenate(
        [jnp.concatenate([c_full, -s_full], axis=1), jnp.concatenate([s_full, c_full], axis=1)], axis=0
    )
    stage_two = jnp.dot(stacked, t_mid, preferred_element_type=jnp.float32)
    stage_two = bf(stage_two).reshape(count, TMPL, BOX, 2 * BOX)
    swapped = jnp.concatenate([stage_two[..., BOX:], -stage_two[..., :BOX]], axis=-1)
    pair = jnp.stack([stage_two, swapped], axis=1)
    cos_half, sin_half = phases(HALF, TMPL, 0)
    t_first = jnp.stack([bf(cos_half).T, bf(sin_half).T], axis=0)
    return bf(jnp.einsum("rwakq,wah->rhkq", pair, t_first, preferred_element_type=jnp.float32))


def window_table(corner_x, width):
    pos = jnp.arange(width, dtype=jnp.int32)[None, :] - corner_x[:, None]
    inside = (pos >= 0) & (pos < BOX)
    k = jnp.arange(BOX, dtype=jnp.int32)
    turn = k[None, None, :] * pos[:, :, None] % BOX
    phase_angle = angle_of(turn)
    mask = inside[:, :, None]
    cos_t = jnp.where(mask, bf(jnp.cos(phase_angle)), jnp.zeros((), jnp.bfloat16))
    sin_t = jnp.where(mask, -bf(jnp.sin(phase_angle)), jnp.zeros((), jnp.bfloat16))
    return jnp.stack([cos_t, sin_t], axis=2)


def band_table():
    lower_edge = jnp.arange(SHIFT, dtype=jnp.int32)[:, None] + shift_anchor()
    cell_index = jnp.arange(BOX, dtype=jnp.int32)[None, :]
    return ((cell_index >= lower_edge) & (cell_index < lower_edge + TMPL)).astype(jnp.float32)


def window_band(corner_x, width):
    lower_edge = jnp.arange(SHIFT, dtype=jnp.int32)[None, :, None] + shift_anchor() + corner_x[:, None, None]
    cell_index = jnp.arange(width, dtype=jnp.int32)[None, None, :]
    return ((cell_index >= lower_edge) & (cell_index < lower_edge + TMPL)).astype(jnp.float32)


def window_rms(rows, corner_x):
    width = rows.shape[-1]
    squares = rows.astype(jnp.float32) ** 2
    band_x = window_band(corner_x, width)
    band = band_table()
    hi = lax.Precision.HIGHEST
    sums_c = jnp.einsum("nabx,nux->nabu", squares, band_x, precision=hi)
    sums_b = jnp.einsum("nabu,tb->natu", sums_c, band, precision=hi)
    sums_a = jnp.einsum("natu,sa->nstu", sums_b, band, precision=hi)
    return jnp.sqrt(sums_a / float(TMPL**3) + epsilon)


def match(box_spectra, box_rms, spectra):
    values = lax.map(lambda one: match_one(box_spectra, box_rms, one[None]), spectra)
    return values[:, :, 0].T


def match_one(box_spectra, box_rms, spectra):
    real_t = spectra[:, 0].astype(jnp.float32)[None]
    imag_t = spectra[:, 1].astype(jnp.float32)[None]
    real_v = box_spectra[:, 0][:, None]
    imag_v = box_spectra[:, 1][:, None]
    real_p = real_t * real_v + imag_t * imag_v
    imag_p = real_t * imag_v - imag_t * real_v
    cross = jnp.stack([bf(real_p), bf(imag_p)], axis=2)
    cos_first, sin_first = phases(SHIFT, HALF, shift_anchor())
    freq_index = jnp.arange(HALF, dtype=jnp.int32)
    weight = jnp.where(freq_index % (BOX // 2) == 0, 1.0, 2.0) / float(BOX**3)
    cos_first = cos_first * weight[None, :]
    sin_first = sin_first * weight[None, :]
    t_first = complex_table(cos_first, sin_first, -1.0, 1.0)
    stage_g = section("nrchjk,chds->nrdsjk", cross, t_first)
    cos_rest, sin_rest = phases(SHIFT, BOX, shift_anchor())
    t_mid = complex_table(cos_rest, sin_rest, -1.0, 1.0)
    stage_h = section("nrcsjk,cjdt->nrdstk", stage_g, t_mid)
    t_last = jnp.stack([bf(cos_rest).T, -bf(sin_rest).T], axis=0)
    correlation = section("nrcstk,cku->nrstu", stage_h, t_last)
    scores = correlation / (box_rms[:, None] * math.sqrt(float(TMPL**3)))
    return jnp.max(scores, axis=(2, 3, 4))


def front_kernel(cz_ref, ys_ref, slab_ref, t1_ref, l2_ref, q2_ref):
    depth, window_y, width = slab_ref.shape
    rows_y = 2 * BOX
    chunk = 8
    t1 = t1_ref[...]
    l2 = l2_ref[...]

    def transform_chunk(ci, carry):
        z0 = pl.multiple_of(ci * chunk, chunk)
        rows = slab_ref[pl.ds(z0, chunk)].reshape(chunk * window_y, width)
        p1 = jnp.dot(rows, t1, preferred_element_type=jnp.float32)
        p1 = p1.astype(jnp.bfloat16).astype(jnp.float32).reshape(chunk, window_y, 2 * BOX)
        pad = jnp.zeros((chunk, rows_y - window_y, 2 * BOX), jnp.float32)
        p1 = jnp.concatenate([p1, pad], axis=1)
        p1t = jnp.swapaxes(p1, 1, 2)
        stacked = jnp.concatenate([p1t[:, :BOX], p1t[:, BOX:]], axis=2)
        stacked = stacked.reshape(chunk * BOX, 2 * rows_y).astype(jnp.bfloat16)
        m2 = jnp.dot(stacked, l2, preferred_element_type=jnp.float32).reshape(chunk, BOX, 2 * BOX)
        lane = lax.broadcasted_iota(jnp.int32, m2.shape, 2)
        sign = jnp.where(lane < BOX, 1.0, -1.0).astype(jnp.float32)
        out = m2.astype(jnp.bfloat16).astype(jnp.float32)
        q2_ref[0, pl.ds(z0, chunk)] = out.astype(jnp.bfloat16)
        swapped = sign * pltpu.roll(out, BOX, 2)
        q2_ref[1, pl.ds(z0, chunk)] = swapped.astype(jnp.bfloat16)
        return carry

    lax.fori_loop(0, depth // chunk, transform_chunk, 0)


def window_bands(corner, length):
    lower_edge = jnp.arange(SHIFT, dtype=jnp.int32)[None, :, None] + shift_anchor() + corner[:, None, None]
    cell_index = jnp.arange(length, dtype=jnp.int32)[None, None, :]
    return ((cell_index >= lower_edge) & (cell_index < lower_edge + TMPL)).astype(jnp.float32)


def block_rms(tomogram, corner_z, corner_y, corner_x):
    depth, rows_y, width = tomogram.shape
    count = corner_z.shape[0]
    hi = lax.Precision.HIGHEST
    values = tomogram.astype(jnp.float32)
    squares = (values * values).reshape(depth * rows_y, width)
    square_hi = bf(squares)
    square_lo = bf(squares - square_hi.astype(jnp.float32))
    band_x = bf(window_bands(corner_x, width).reshape(count * SHIFT, width).T)
    sums_x = jnp.dot(square_hi, band_x, preferred_element_type=jnp.float32)
    sums_x = sums_x + jnp.dot(square_lo, band_x, preferred_element_type=jnp.float32)
    sums_x = sums_x.reshape(depth, rows_y, count, SHIFT)
    band_y = window_bands(corner_y, rows_y)
    sums_y = jnp.einsum("zynu,nty->nztu", sums_x, band_y, precision=hi)
    band_z = window_bands(corner_z, depth)
    sums_z = jnp.einsum("nztu,nsz->nstu", sums_y, band_z, precision=hi)
    return jnp.sqrt(sums_z / float(TMPL**3) + epsilon)


def front(tomogram, corner_z, corner_y, corner_x):
    count = corner_z.shape[0]
    block_y = tomogram.shape[1]
    window_y = BOX + 16
    rows_y = 2 * BOX
    width = tomogram.shape[2]
    start_y = jnp.minimum((corner_y // 16) * 16, block_y - window_y).astype(jnp.int32)
    t1 = window_table(corner_x, width).reshape(count, width, 2 * BOX)
    pos_y = jnp.arange(rows_y, dtype=jnp.int32)[None, :] - (corner_y - start_y)[:, None]
    inside_y = (pos_y >= 0) & (pos_y < BOX)
    j = jnp.arange(BOX, dtype=jnp.int32)
    turn_y = pos_y[:, :, None] * j[None, None, :] % BOX
    angle_y = angle_of(turn_y)
    zero = jnp.zeros((), jnp.bfloat16)
    cos_y = jnp.where(inside_y[:, :, None], bf(jnp.cos(angle_y)), zero)
    sin_y = jnp.where(inside_y[:, :, None], bf(jnp.sin(angle_y)), zero)
    l2 = jnp.concatenate(
        [jnp.concatenate([cos_y, -sin_y], axis=2), jnp.concatenate([sin_y, cos_y], axis=2)], axis=1
    )

    grid_spec = pltpu.PrefetchScalarGridSpec(
        num_scalar_prefetch=2,
        grid=(count,),
        in_specs=[
            pl.BlockSpec(
                (pl.Element(BOX), pl.Element(window_y), pl.Element(width)), lambda n, cz, ys: (cz[n], pl.multiple_of(ys[n], 16), 0)
            ),
            pl.BlockSpec((None, width, 2 * BOX), lambda n, cz, ys: (n, 0, 0)),
            pl.BlockSpec((None, 2 * rows_y, 2 * BOX), lambda n, cz, ys: (n, 0, 0)),
        ],
        out_specs=pl.BlockSpec((None, 2, BOX, BOX, 2 * BOX), lambda n, cz, ys: (n, 0, 0, 0, 0)),
    )
    q2 = pl.pallas_call(
        front_kernel,
        grid_spec=grid_spec,
        out_shape=jax.ShapeDtypeStruct((count, 2, BOX, BOX, 2 * BOX), jnp.bfloat16),
        compiler_params=pltpu.CompilerParams(vmem_limit_bytes=48 * 1024 * 1024),
    )(corner_z, start_y, tomogram, t1, l2)
    return q2, block_rms(tomogram, corner_z, corner_y, corner_x)


def box_spectra_of(q2):
    cos_half, sin_half = phases(HALF, BOX, 0)
    l3 = jnp.stack([bf(cos_half).T, bf(sin_half).T], axis=0)
    return bf(jnp.einsum("nwzkq,wzh->nhkq", q2, l3, preferred_element_type=jnp.float32))


def match_kj(spectrum_v, box_rms, spectra):
    spectra_kj = spectra

    def one(spectrum):
        real_v = spectrum_v[..., :BOX]
        imag_v = spectrum_v[..., BOX:]
        real_t = spectrum[..., :BOX].astype(jnp.float32)[None, None]
        imag_t = spectrum[..., BOX:].astype(jnp.float32)[None, None]
        rv = real_v[:, None]
        iv = imag_v[:, None]
        real_p = real_t * rv + imag_t * iv
        imag_p = real_t * iv - imag_t * rv
        cross = jnp.stack([bf(real_p), bf(imag_p)], axis=2)
        cos_first, sin_first = phases(SHIFT, HALF, shift_anchor())
        freq_index = jnp.arange(HALF, dtype=jnp.int32)
        weight = jnp.where(freq_index % (BOX // 2) == 0, 1.0, 2.0) / float(BOX**3)
        t_first = complex_table(cos_first * weight[None, :], sin_first * weight[None, :], -1.0, 1.0)
        stage_g = section("nrchkj,chds->nrdskj", cross, t_first)
        cos_rest, sin_rest = phases(SHIFT, BOX, shift_anchor())
        t_mid = complex_table(cos_rest, sin_rest, -1.0, 1.0)
        stage_h = section("nrcskj,cjdt->nrdskt", stage_g, t_mid)
        t_last = jnp.stack([bf(cos_rest).T, -bf(sin_rest).T], axis=0)
        correlation = section("nrcskt,cku->nrstu", stage_h, t_last)
        scores = correlation / (box_rms[:, None] * math.sqrt(float(TMPL**3)))
        return jnp.max(scores, axis=(2, 3, 4))[:, 0]

    count_r = spectra_kj.shape[0]
    group = min(4, count_r)

    def one_group(block):
        return jnp.stack([one(block[i]) for i in range(group)], axis=0)

    blocks = spectra_kj.reshape((count_r // group, group) + spectra_kj.shape[1:])
    if count_r == group:
        values = one_group(blocks[0])
    else:
        values = lax.map(one_group, blocks).reshape((count_r,) + (spectrum_v.shape[0],))
    return values.T


def per_device(tomogram, templates, corner_z, corner_y, corner_x, loads):
    own_total = corner_z.shape[1]
    live_count = jnp.sum(loads[0, 0])
    q2, box_rms = front(tomogram, corner_z[0], corner_y[0], corner_x[0])
    spectrum_v = box_spectra_of(q2)

    own_spectra = template_spectra(templates.reshape(-1, TMPL, TMPL, TMPL))
    spectra = lax.all_gather(own_spectra, "orient", axis=0, tiled=True)
    values = match_kj(spectrum_v, box_rms, spectra)
    live = jnp.arange(own_total, dtype=jnp.int32) < live_count
    matched = jnp.where(live[:, None], values, 0.0)
    return (matched[None], jnp.max(matched, axis=1)[None])


def solution(mesh):
    return jax.shard_map(
        per_device,
        mesh=mesh,
        in_specs=(
            P("vol", "orient", None),
            P("orient", None, None),
            P("vol", "orient"),
            P("vol", "orient"),
            P("vol", "orient"),
            P("vol", "orient", None),
        ),
        out_specs=(P("vol", "orient", None), P("vol", "orient")),
        check_vma=False,
    )
```

```python
import math

import jax
import jax.numpy as jnp
from jax import lax
from jax.sharding import PartitionSpec as P
from jax.experimental import pallas as pl
from jax.experimental.pallas import tpu as pltpu

BOX = 64
TMPL = 32
SHIFT = 8
HALF = 33


epsilon = 1e-05


def shift_anchor():
    return (BOX - TMPL) // 2 - SHIFT // 2


def angle_of(turn_index):
    return turn_index.astype(jnp.float32) * (2.0 * math.pi / BOX)


def phases(count_out, count_in, offset):
    out_index = jnp.arange(count_out, dtype=jnp.int32) + offset
    in_index = jnp.arange(count_in, dtype=jnp.int32)
    turn_index = out_index[:, None] * in_index[None, :] % BOX
    phase_angle = angle_of(turn_index)
    return (jnp.cos(phase_angle), jnp.sin(phase_angle))


def bf(x):
    return x.astype(jnp.bfloat16)


def complex_table(cos_t, sin_t, sign_re_from_im, sign_im_from_re):
    c = bf(cos_t).T
    s = bf(sin_t).T
    re_row = jnp.stack([c, sign_im_from_re * s], axis=1)
    im_row = jnp.stack([sign_re_from_im * s, c], axis=1)
    return jnp.stack([re_row, im_row], axis=0)


def section(pattern, operand, table):
    return jnp.einsum(pattern, bf(operand), table, preferred_element_type=jnp.float32)


def forward_tail(stage_one):
    length_a = stage_one.shape[2]
    length_y = stage_one.shape[3]
    cos_full, sin_full = phases(BOX, length_y, 0)
    t_mid = complex_table(cos_full, sin_full, 1.0, -1.0)
    stage_two = section("ncayk,cydj->ndajk", stage_one, t_mid)
    cos_half, sin_half = phases(HALF, length_a, 0)
    t_first = complex_table(cos_half, sin_half, 1.0, -1.0)
    return section("ncajk,cadh->ndhjk", stage_two, t_first)


def template_spectra(cubes):
    volume = cubes.astype(jnp.float32)
    count = volume.shape[0]
    flat = volume.reshape(count, -1)
    centred = flat - jnp.mean(flat, axis=1, keepdims=True)
    unit = centred / jnp.sqrt(jnp.mean(centred * centred, axis=1, keepdims=True) + epsilon)
    cos_full, sin_full = phases(BOX, TMPL, 0)
    c_full = bf(cos_full).T
    s_full = bf(sin_full).T
    t_last = jnp.concatenate([c_full, -s_full], axis=1)
    stage_one = jnp.dot(bf(unit).reshape(count * TMPL * TMPL, TMPL), t_last, preferred_element_type=jnp.float32)
    stage_one = bf(stage_one).reshape(count, TMPL, TMPL, 2, BOX)
    stacked = jnp.transpose(stage_one, (0, 1, 4, 3, 2)).reshape(count * TMPL * BOX, 2 * TMPL)
    t_mid = jnp.concatenate(
        [jnp.concatenate([c_full, -s_full], axis=1), jnp.concatenate([s_full, c_full], axis=1)], axis=0
    )
    stage_two = jnp.dot(stacked, t_mid, preferred_element_type=jnp.float32)
    stage_two = bf(stage_two).reshape(count, TMPL, BOX, 2 * BOX)
    swapped = jnp.concatenate([stage_two[..., BOX:], -stage_two[..., :BOX]], axis=-1)
    pair = jnp.stack([stage_two, swapped], axis=1)
    cos_half, sin_half = phases(HALF, TMPL, 0)
    t_first = jnp.stack([bf(cos_half).T, bf(sin_half).T], axis=0)
    return bf(jnp.einsum("rwakq,wah->rhkq", pair, t_first, preferred_element_type=jnp.float32))


def window_table(corner_x, width):
    pos = jnp.arange(width, dtype=jnp.int32)[None, :] - corner_x[:, None]
    inside = (pos >= 0) & (pos < BOX)
    k = jnp.arange(BOX, dtype=jnp.int32)
    turn = k[None, None, :] * pos[:, :, None] % BOX
    phase_angle = angle_of(turn)
    mask = inside[:, :, None]
    cos_t = jnp.where(mask, bf(jnp.cos(phase_angle)), jnp.zeros((), jnp.bfloat16))
    sin_t = jnp.where(mask, -bf(jnp.sin(phase_angle)), jnp.zeros((), jnp.bfloat16))
    return jnp.stack([cos_t, sin_t], axis=2)


def band_table():
    lower_edge = jnp.arange(SHIFT, dtype=jnp.int32)[:, None] + shift_anchor()
    cell_index = jnp.arange(BOX, dtype=jnp.int32)[None, :]
    return ((cell_index >= lower_edge) & (cell_index < lower_edge + TMPL)).astype(jnp.float32)


def window_band(corner_x, width):
    lower_edge = jnp.arange(SHIFT, dtype=jnp.int32)[None, :, None] + shift_anchor() + corner_x[:, None, None]
    cell_index = jnp.arange(width, dtype=jnp.int32)[None, None, :]
    return ((cell_index >= lower_edge) & (cell_index < lower_edge + TMPL)).astype(jnp.float32)


def window_rms(rows, corner_x):
    width = rows.shape[-1]
    squares = rows.astype(jnp.float32) ** 2
    band_x = window_band(corner_x, width)
    band = band_table()
    hi = lax.Precision.HIGHEST
    sums_c = jnp.einsum("nabx,nux->nabu", squares, band_x, precision=hi)
    sums_b = jnp.einsum("nabu,tb->natu", sums_c, band, precision=hi)
    sums_a = jnp.einsum("natu,sa->nstu", sums_b, band, precision=hi)
    return jnp.sqrt(sums_a / float(TMPL**3) + epsilon)


def match(box_spectra, box_rms, spectra):
    values = lax.map(lambda one: match_one(box_spectra, box_rms, one[None]), spectra)
    return values[:, :, 0].T


def match_one(box_spectra, box_rms, spectra):
    real_t = spectra[:, 0].astype(jnp.float32)[None]
    imag_t = spectra[:, 1].astype(jnp.float32)[None]
    real_v = box_spectra[:, 0][:, None]
    imag_v = box_spectra[:, 1][:, None]
    real_p = real_t * real_v + imag_t * imag_v
    imag_p = real_t * imag_v - imag_t * real_v
    cross = jnp.stack([bf(real_p), bf(imag_p)], axis=2)
    cos_first, sin_first = phases(SHIFT, HALF, shift_anchor())
    freq_index = jnp.arange(HALF, dtype=jnp.int32)
    weight = jnp.where(freq_index % (BOX // 2) == 0, 1.0, 2.0) / float(BOX**3)
    cos_first = cos_first * weight[None, :]
    sin_first = sin_first * weight[None, :]
    t_first = complex_table(cos_first, sin_first, -1.0, 1.0)
    stage_g = section("nrchjk,chds->nrdsjk", cross, t_first)
    cos_rest, sin_rest = phases(SHIFT, BOX, shift_anchor())
    t_mid = complex_table(cos_rest, sin_rest, -1.0, 1.0)
    stage_h = section("nrcsjk,cjdt->nrdstk", stage_g, t_mid)
    t_last = jnp.stack([bf(cos_rest).T, -bf(sin_rest).T], axis=0)
    correlation = section("nrcstk,cku->nrstu", stage_h, t_last)
    scores = correlation / (box_rms[:, None] * math.sqrt(float(TMPL**3)))
    return jnp.max(scores, axis=(2, 3, 4))


def front_kernel(cz_ref, ys_ref, slab_ref, t1_ref, l2_ref, q2_ref):
    depth, window_y, width = slab_ref.shape
    rows_y = 2 * BOX
    chunk = 16
    t1 = t1_ref[...]
    l2 = l2_ref[...]

    def transform_chunk(ci, carry):
        z0 = pl.multiple_of(ci * chunk, chunk)
        rows = slab_ref[pl.ds(z0, chunk)].reshape(chunk * window_y, width)
        p1 = jnp.dot(rows, t1, preferred_element_type=jnp.float32)
        p1 = p1.astype(jnp.bfloat16).astype(jnp.float32).reshape(chunk, window_y, 2 * BOX)
        pad = jnp.zeros((chunk, rows_y - window_y, 2 * BOX), jnp.float32)
        p1 = jnp.concatenate([p1, pad], axis=1)
        p1t = jnp.swapaxes(p1, 1, 2)
        stacked = jnp.concatenate([p1t[:, :BOX], p1t[:, BOX:]], axis=2)
        stacked = stacked.reshape(chunk * BOX, 2 * rows_y).astype(jnp.bfloat16)
        m2 = jnp.dot(stacked, l2, preferred_element_type=jnp.float32).reshape(chunk, BOX, 2 * BOX)
        lane = lax.broadcasted_iota(jnp.int32, m2.shape, 2)
        sign = jnp.where(lane < BOX, 1.0, -1.0).astype(jnp.float32)
        out = m2.astype(jnp.bfloat16).astype(jnp.float32)
        q2_ref[0, pl.ds(z0, chunk)] = out.astype(jnp.bfloat16)
        swapped = sign * pltpu.roll(out, BOX, 2)
        q2_ref[1, pl.ds(z0, chunk)] = swapped.astype(jnp.bfloat16)
        return carry

    lax.fori_loop(0, depth // chunk, transform_chunk, 0)


def window_bands(corner, length):
    lower_edge = jnp.arange(SHIFT, dtype=jnp.int32)[None, :, None] + shift_anchor() + corner[:, None, None]
    cell_index = jnp.arange(length, dtype=jnp.int32)[None, None, :]
    return ((cell_index >= lower_edge) & (cell_index < lower_edge + TMPL)).astype(jnp.float32)


def block_rms(tomogram, corner_z, corner_y, corner_x):
    depth, rows_y, width = tomogram.shape
    count = corner_z.shape[0]
    hi = lax.Precision.HIGHEST
    values = tomogram.astype(jnp.float32)
    squares = (values * values).reshape(depth * rows_y, width)
    square_hi = bf(squares)
    square_lo = bf(squares - square_hi.astype(jnp.float32))
    band_x = bf(window_bands(corner_x, width).reshape(count * SHIFT, width).T)
    sums_x = jnp.dot(square_hi, band_x, preferred_element_type=jnp.float32)
    sums_x = sums_x + jnp.dot(square_lo, band_x, preferred_element_type=jnp.float32)
    sums_x = sums_x.reshape(depth, rows_y, count, SHIFT)
    band_y = window_bands(corner_y, rows_y)
    sums_y = jnp.einsum("zynu,nty->nztu", sums_x, band_y, precision=hi)
    band_z = window_bands(corner_z, depth)
    sums_z = jnp.einsum("nztu,nsz->nstu", sums_y, band_z, precision=hi)
    return jnp.sqrt(sums_z / float(TMPL**3) + epsilon)


def front(tomogram, corner_z, corner_y, corner_x):
    count = corner_z.shape[0]
    block_y = tomogram.shape[1]
    window_y = BOX + 16
    rows_y = 2 * BOX
    width = tomogram.shape[2]
    start_y = jnp.minimum((corner_y // 16) * 16, block_y - window_y).astype(jnp.int32)
    t1 = window_table(corner_x, width).reshape(count, width, 2 * BOX)
    pos_y = jnp.arange(rows_y, dtype=jnp.int32)[None, :] - (corner_y - start_y)[:, None]
    inside_y = (pos_y >= 0) & (pos_y < BOX)
    j = jnp.arange(BOX, dtype=jnp.int32)
    turn_y = pos_y[:, :, None] * j[None, None, :] % BOX
    angle_y = angle_of(turn_y)
    zero = jnp.zeros((), jnp.bfloat16)
    cos_y = jnp.where(inside_y[:, :, None], bf(jnp.cos(angle_y)), zero)
    sin_y = jnp.where(inside_y[:, :, None], bf(jnp.sin(angle_y)), zero)
    l2 = jnp.concatenate(
        [jnp.concatenate([cos_y, -sin_y], axis=2), jnp.concatenate([sin_y, cos_y], axis=2)], axis=1
    )

    grid_spec = pltpu.PrefetchScalarGridSpec(
        num_scalar_prefetch=2,
        grid=(count,),
        in_specs=[
            pl.BlockSpec(
                (pl.Element(BOX), pl.Element(window_y), pl.Element(width)), lambda n, cz, ys: (cz[n], pl.multiple_of(ys[n], 16), 0)
            ),
            pl.BlockSpec((None, width, 2 * BOX), lambda n, cz, ys: (n, 0, 0)),
            pl.BlockSpec((None, 2 * rows_y, 2 * BOX), lambda n, cz, ys: (n, 0, 0)),
        ],
        out_specs=pl.BlockSpec((None, 2, BOX, BOX, 2 * BOX), lambda n, cz, ys: (n, 0, 0, 0, 0)),
    )
    q2 = pl.pallas_call(
        front_kernel,
        grid_spec=grid_spec,
        out_shape=jax.ShapeDtypeStruct((count, 2, BOX, BOX, 2 * BOX), jnp.bfloat16),
        compiler_params=pltpu.CompilerParams(vmem_limit_bytes=48 * 1024 * 1024),
    )(corner_z, start_y, tomogram, t1, l2)
    return q2, block_rms(tomogram, corner_z, corner_y, corner_x)


def box_spectra_of(q2):
    cos_half, sin_half = phases(HALF, BOX, 0)
    l3 = jnp.stack([bf(cos_half).T, bf(sin_half).T], axis=0)
    return bf(jnp.einsum("nwzkq,wzh->nhkq", q2, l3, preferred_element_type=jnp.float32))


def match_kj(spectrum_v, box_rms, spectra):
    spectra_kj = spectra

    def one(spectrum):
        real_v = spectrum_v[..., :BOX]
        imag_v = spectrum_v[..., BOX:]
        real_t = spectrum[..., :BOX].astype(jnp.float32)[None, None]
        imag_t = spectrum[..., BOX:].astype(jnp.float32)[None, None]
        rv = real_v[:, None]
        iv = imag_v[:, None]
        real_p = real_t * rv + imag_t * iv
        imag_p = real_t * iv - imag_t * rv
        cross = jnp.stack([bf(real_p), bf(imag_p)], axis=2)
        cos_first, sin_first = phases(SHIFT, HALF, shift_anchor())
        freq_index = jnp.arange(HALF, dtype=jnp.int32)
        weight = jnp.where(freq_index % (BOX // 2) == 0, 1.0, 2.0) / float(BOX**3)
        t_first = complex_table(cos_first * weight[None, :], sin_first * weight[None, :], -1.0, 1.0)
        stage_g = section("nrchkj,chds->nrdskj", cross, t_first)
        cos_rest, sin_rest = phases(SHIFT, BOX, shift_anchor())
        t_mid = complex_table(cos_rest, sin_rest, -1.0, 1.0)
        stage_h = section("nrcskj,cjdt->nrdskt", stage_g, t_mid)
        t_last = jnp.stack([bf(cos_rest).T, -bf(sin_rest).T], axis=0)
        correlation = section("nrcskt,cku->nrstu", stage_h, t_last)
        scores = correlation / (box_rms[:, None] * math.sqrt(float(TMPL**3)))
        return jnp.max(scores, axis=(2, 3, 4))[:, 0]

    count_r = spectra_kj.shape[0]
    group = min(4, count_r)

    def one_group(block):
        return jnp.stack([one(block[i]) for i in range(group)], axis=0)

    blocks = spectra_kj.reshape((count_r // group, group) + spectra_kj.shape[1:])
    if count_r == group:
        values = one_group(blocks[0])
    else:
        values = lax.map(one_group, blocks).reshape((count_r,) + (spectrum_v.shape[0],))
    return values.T


def per_device(tomogram, templates, corner_z, corner_y, corner_x, loads):
    own_total = corner_z.shape[1]
    live_count = jnp.sum(loads[0, 0])
    q2, box_rms = front(tomogram, corner_z[0], corner_y[0], corner_x[0])
    spectrum_v = box_spectra_of(q2)

    own_spectra = template_spectra(templates.reshape(-1, TMPL, TMPL, TMPL))
    spectra = lax.all_gather(own_spectra, "orient", axis=0, tiled=True)
    values = match_kj(spectrum_v, box_rms, spectra)
    live = jnp.arange(own_total, dtype=jnp.int32) < live_count
    matched = jnp.where(live[:, None], values, 0.0)
    return (matched[None], jnp.max(matched, axis=1)[None])


def solution(mesh):
    return jax.shard_map(
        per_device,
        mesh=mesh,
        in_specs=(
            P("vol", "orient", None),
            P("orient", None, None),
            P("vol", "orient"),
            P("vol", "orient"),
            P("vol", "orient"),
            P("vol", "orient", None),
        ),
        out_specs=(P("vol", "orient", None), P("vol", "orient")),
        check_vma=False,
    )
```

```python
import math

import jax
import jax.numpy as jnp
from jax import lax
from jax.sharding import PartitionSpec as P
from jax.experimental import pallas as pl
from jax.experimental.pallas import tpu as pltpu

BOX = 64
TMPL = 32
SHIFT = 8
HALF = 33


epsilon = 1e-05


def shift_anchor():
    return (BOX - TMPL) // 2 - SHIFT // 2


def angle_of(turn_index):
    return turn_index.astype(jnp.float32) * (2.0 * math.pi / BOX)


def phases(count_out, count_in, offset):
    out_index = jnp.arange(count_out, dtype=jnp.int32) + offset
    in_index = jnp.arange(count_in, dtype=jnp.int32)
    turn_index = out_index[:, None] * in_index[None, :] % BOX
    phase_angle = angle_of(turn_index)
    return (jnp.cos(phase_angle), jnp.sin(phase_angle))


def bf(x):
    return x.astype(jnp.bfloat16)


def complex_table(cos_t, sin_t, sign_re_from_im, sign_im_from_re):
    c = bf(cos_t).T
    s = bf(sin_t).T
    re_row = jnp.stack([c, sign_im_from_re * s], axis=1)
    im_row = jnp.stack([sign_re_from_im * s, c], axis=1)
    return jnp.stack([re_row, im_row], axis=0)


def section(pattern, operand, table):
    return jnp.einsum(pattern, bf(operand), table, preferred_element_type=jnp.float32)


def forward_tail(stage_one):
    length_a = stage_one.shape[2]
    length_y = stage_one.shape[3]
    cos_full, sin_full = phases(BOX, length_y, 0)
    t_mid = complex_table(cos_full, sin_full, 1.0, -1.0)
    stage_two = section("ncayk,cydj->ndajk", stage_one, t_mid)
    cos_half, sin_half = phases(HALF, length_a, 0)
    t_first = complex_table(cos_half, sin_half, 1.0, -1.0)
    return section("ncajk,cadh->ndhjk", stage_two, t_first)


def template_spectra(cubes):
    volume = cubes.astype(jnp.float32)
    count = volume.shape[0]
    flat = volume.reshape(count, -1)
    centred = flat - jnp.mean(flat, axis=1, keepdims=True)
    unit = centred / jnp.sqrt(jnp.mean(centred * centred, axis=1, keepdims=True) + epsilon)
    cos_full, sin_full = phases(BOX, TMPL, 0)
    c_full = bf(cos_full).T
    s_full = bf(sin_full).T
    t_last = jnp.concatenate([c_full, -s_full], axis=1)
    stage_one = jnp.dot(bf(unit).reshape(count * TMPL * TMPL, TMPL), t_last, preferred_element_type=jnp.float32)
    stage_one = bf(stage_one).reshape(count, TMPL, TMPL, 2, BOX)
    stacked = jnp.transpose(stage_one, (0, 1, 4, 3, 2)).reshape(count * TMPL * BOX, 2 * TMPL)
    t_mid = jnp.concatenate(
        [jnp.concatenate([c_full, -s_full], axis=1), jnp.concatenate([s_full, c_full], axis=1)], axis=0
    )
    stage_two = jnp.dot(stacked, t_mid, preferred_element_type=jnp.float32)
    stage_two = bf(stage_two).reshape(count, TMPL, BOX, 2 * BOX)
    swapped = jnp.concatenate([stage_two[..., BOX:], -stage_two[..., :BOX]], axis=-1)
    pair = jnp.stack([stage_two, swapped], axis=1)
    cos_half, sin_half = phases(HALF, TMPL, 0)
    t_first = jnp.stack([bf(cos_half).T, bf(sin_half).T], axis=0)
    return bf(jnp.einsum("rwakq,wah->rhkq", pair, t_first, preferred_element_type=jnp.float32))


def window_table(corner_x, width):
    pos = jnp.arange(width, dtype=jnp.int32)[None, :] - corner_x[:, None]
    inside = (pos >= 0) & (pos < BOX)
    k = jnp.arange(BOX, dtype=jnp.int32)
    turn = k[None, None, :] * pos[:, :, None] % BOX
    phase_angle = angle_of(turn)
    mask = inside[:, :, None]
    cos_t = jnp.where(mask, bf(jnp.cos(phase_angle)), jnp.zeros((), jnp.bfloat16))
    sin_t = jnp.where(mask, -bf(jnp.sin(phase_angle)), jnp.zeros((), jnp.bfloat16))
    return jnp.stack([cos_t, sin_t], axis=2)


def band_table():
    lower_edge = jnp.arange(SHIFT, dtype=jnp.int32)[:, None] + shift_anchor()
    cell_index = jnp.arange(BOX, dtype=jnp.int32)[None, :]
    return ((cell_index >= lower_edge) & (cell_index < lower_edge + TMPL)).astype(jnp.float32)


def window_band(corner_x, width):
    lower_edge = jnp.arange(SHIFT, dtype=jnp.int32)[None, :, None] + shift_anchor() + corner_x[:, None, None]
    cell_index = jnp.arange(width, dtype=jnp.int32)[None, None, :]
    return ((cell_index >= lower_edge) & (cell_index < lower_edge + TMPL)).astype(jnp.float32)


def window_rms(rows, corner_x):
    width = rows.shape[-1]
    squares = rows.astype(jnp.float32) ** 2
    band_x = window_band(corner_x, width)
    band = band_table()
    hi = lax.Precision.HIGHEST
    sums_c = jnp.einsum("nabx,nux->nabu", squares, band_x, precision=hi)
    sums_b = jnp.einsum("nabu,tb->natu", sums_c, band, precision=hi)
    sums_a = jnp.einsum("natu,sa->nstu", sums_b, band, precision=hi)
    return jnp.sqrt(sums_a / float(TMPL**3) + epsilon)


def match(box_spectra, box_rms, spectra):
    values = lax.map(lambda one: match_one(box_spectra, box_rms, one[None]), spectra)
    return values[:, :, 0].T


def match_one(box_spectra, box_rms, spectra):
    real_t = spectra[:, 0].astype(jnp.float32)[None]
    imag_t = spectra[:, 1].astype(jnp.float32)[None]
    real_v = box_spectra[:, 0][:, None]
    imag_v = box_spectra[:, 1][:, None]
    real_p = real_t * real_v + imag_t * imag_v
    imag_p = real_t * imag_v - imag_t * real_v
    cross = jnp.stack([bf(real_p), bf(imag_p)], axis=2)
    cos_first, sin_first = phases(SHIFT, HALF, shift_anchor())
    freq_index = jnp.arange(HALF, dtype=jnp.int32)
    weight = jnp.where(freq_index % (BOX // 2) == 0, 1.0, 2.0) / float(BOX**3)
    cos_first = cos_first * weight[None, :]
    sin_first = sin_first * weight[None, :]
    t_first = complex_table(cos_first, sin_first, -1.0, 1.0)
    stage_g = section("nrchjk,chds->nrdsjk", cross, t_first)
    cos_rest, sin_rest = phases(SHIFT, BOX, shift_anchor())
    t_mid = complex_table(cos_rest, sin_rest, -1.0, 1.0)
    stage_h = section("nrcsjk,cjdt->nrdstk", stage_g, t_mid)
    t_last = jnp.stack([bf(cos_rest).T, -bf(sin_rest).T], axis=0)
    correlation = section("nrcstk,cku->nrstu", stage_h, t_last)
    scores = correlation / (box_rms[:, None] * math.sqrt(float(TMPL**3)))
    return jnp.max(scores, axis=(2, 3, 4))


def front_kernel(cz_ref, ys_ref, slab_ref, t1_ref, l2_ref, q2_ref):
    depth, window_y, width = slab_ref.shape
    rows_y = 2 * BOX
    chunk = 32
    t1 = t1_ref[...]
    l2 = l2_ref[...]

    def transform_chunk(ci, carry):
        z0 = pl.multiple_of(ci * chunk, chunk)
        rows = slab_ref[pl.ds(z0, chunk)].reshape(chunk * window_y, width)
        p1 = jnp.dot(rows, t1, preferred_element_type=jnp.float32)
        p1 = p1.astype(jnp.bfloat16).astype(jnp.float32).reshape(chunk, window_y, 2 * BOX)
        pad = jnp.zeros((chunk, rows_y - window_y, 2 * BOX), jnp.float32)
        p1 = jnp.concatenate([p1, pad], axis=1)
        p1t = jnp.swapaxes(p1, 1, 2)
        stacked = jnp.concatenate([p1t[:, :BOX], p1t[:, BOX:]], axis=2)
        stacked = stacked.reshape(chunk * BOX, 2 * rows_y).astype(jnp.bfloat16)
        m2 = jnp.dot(stacked, l2, preferred_element_type=jnp.float32).reshape(chunk, BOX, 2 * BOX)
        lane = lax.broadcasted_iota(jnp.int32, m2.shape, 2)
        sign = jnp.where(lane < BOX, 1.0, -1.0).astype(jnp.float32)
        out = m2.astype(jnp.bfloat16).astype(jnp.float32)
        q2_ref[0, pl.ds(z0, chunk)] = out.astype(jnp.bfloat16)
        swapped = sign * pltpu.roll(out, BOX, 2)
        q2_ref[1, pl.ds(z0, chunk)] = swapped.astype(jnp.bfloat16)
        return carry

    lax.fori_loop(0, depth // chunk, transform_chunk, 0)


def window_bands(corner, length):
    lower_edge = jnp.arange(SHIFT, dtype=jnp.int32)[None, :, None] + shift_anchor() + corner[:, None, None]
    cell_index = jnp.arange(length, dtype=jnp.int32)[None, None, :]
    return ((cell_index >= lower_edge) & (cell_index < lower_edge + TMPL)).astype(jnp.float32)


def block_rms(tomogram, corner_z, corner_y, corner_x):
    depth, rows_y, width = tomogram.shape
    count = corner_z.shape[0]
    hi = lax.Precision.HIGHEST
    values = tomogram.astype(jnp.float32)
    squares = (values * values).reshape(depth * rows_y, width)
    square_hi = bf(squares)
    square_lo = bf(squares - square_hi.astype(jnp.float32))
    band_x = bf(window_bands(corner_x, width).reshape(count * SHIFT, width).T)
    sums_x = jnp.dot(square_hi, band_x, preferred_element_type=jnp.float32)
    sums_x = sums_x + jnp.dot(square_lo, band_x, preferred_element_type=jnp.float32)
    sums_x = sums_x.reshape(depth, rows_y, count, SHIFT)
    band_y = window_bands(corner_y, rows_y)
    sums_y = jnp.einsum("zynu,nty->nztu", sums_x, band_y, precision=hi)
    band_z = window_bands(corner_z, depth)
    sums_z = jnp.einsum("nztu,nsz->nstu", sums_y, band_z, precision=hi)
    return jnp.sqrt(sums_z / float(TMPL**3) + epsilon)


def front(tomogram, corner_z, corner_y, corner_x):
    count = corner_z.shape[0]
    block_y = tomogram.shape[1]
    window_y = BOX + 16
    rows_y = 2 * BOX
    width = tomogram.shape[2]
    start_y = jnp.minimum((corner_y // 16) * 16, block_y - window_y).astype(jnp.int32)
    t1 = window_table(corner_x, width).reshape(count, width, 2 * BOX)
    pos_y = jnp.arange(rows_y, dtype=jnp.int32)[None, :] - (corner_y - start_y)[:, None]
    inside_y = (pos_y >= 0) & (pos_y < BOX)
    j = jnp.arange(BOX, dtype=jnp.int32)
    turn_y = pos_y[:, :, None] * j[None, None, :] % BOX
    angle_y = angle_of(turn_y)
    zero = jnp.zeros((), jnp.bfloat16)
    cos_y = jnp.where(inside_y[:, :, None], bf(jnp.cos(angle_y)), zero)
    sin_y = jnp.where(inside_y[:, :, None], bf(jnp.sin(angle_y)), zero)
    l2 = jnp.concatenate(
        [jnp.concatenate([cos_y, -sin_y], axis=2), jnp.concatenate([sin_y, cos_y], axis=2)], axis=1
    )

    grid_spec = pltpu.PrefetchScalarGridSpec(
        num_scalar_prefetch=2,
        grid=(count,),
        in_specs=[
            pl.BlockSpec(
                (pl.Element(BOX), pl.Element(window_y), pl.Element(width)), lambda n, cz, ys: (cz[n], pl.multiple_of(ys[n], 16), 0)
            ),
            pl.BlockSpec((None, width, 2 * BOX), lambda n, cz, ys: (n, 0, 0)),
            pl.BlockSpec((None, 2 * rows_y, 2 * BOX), lambda n, cz, ys: (n, 0, 0)),
        ],
        out_specs=pl.BlockSpec((None, 2, BOX, BOX, 2 * BOX), lambda n, cz, ys: (n, 0, 0, 0, 0)),
    )
    q2 = pl.pallas_call(
        front_kernel,
        grid_spec=grid_spec,
        out_shape=jax.ShapeDtypeStruct((count, 2, BOX, BOX, 2 * BOX), jnp.bfloat16),
        compiler_params=pltpu.CompilerParams(vmem_limit_bytes=48 * 1024 * 1024),
    )(corner_z, start_y, tomogram, t1, l2)
    return q2, block_rms(tomogram, corner_z, corner_y, corner_x)


def box_spectra_of(q2):
    cos_half, sin_half = phases(HALF, BOX, 0)
    l3 = jnp.stack([bf(cos_half).T, bf(sin_half).T], axis=0)
    return bf(jnp.einsum("nwzkq,wzh->nhkq", q2, l3, preferred_element_type=jnp.float32))


def match_kj(spectrum_v, box_rms, spectra):
    spectra_kj = spectra

    def one(spectrum):
        real_v = spectrum_v[..., :BOX]
        imag_v = spectrum_v[..., BOX:]
        real_t = spectrum[..., :BOX].astype(jnp.float32)[None, None]
        imag_t = spectrum[..., BOX:].astype(jnp.float32)[None, None]
        rv = real_v[:, None]
        iv = imag_v[:, None]
        real_p = real_t * rv + imag_t * iv
        imag_p = real_t * iv - imag_t * rv
        cross = jnp.stack([bf(real_p), bf(imag_p)], axis=2)
        cos_first, sin_first = phases(SHIFT, HALF, shift_anchor())
        freq_index = jnp.arange(HALF, dtype=jnp.int32)
        weight = jnp.where(freq_index % (BOX // 2) == 0, 1.0, 2.0) / float(BOX**3)
        t_first = complex_table(cos_first * weight[None, :], sin_first * weight[None, :], -1.0, 1.0)
        stage_g = section("nrchkj,chds->nrdskj", cross, t_first)
        cos_rest, sin_rest = phases(SHIFT, BOX, shift_anchor())
        t_mid = complex_table(cos_rest, sin_rest, -1.0, 1.0)
        stage_h = section("nrcskj,cjdt->nrdskt", stage_g, t_mid)
        t_last = jnp.stack([bf(cos_rest).T, -bf(sin_rest).T], axis=0)
        correlation = section("nrcskt,cku->nrstu", stage_h, t_last)
        scores = correlation / (box_rms[:, None] * math.sqrt(float(TMPL**3)))
        return jnp.max(scores, axis=(2, 3, 4))[:, 0]

    count_r = spectra_kj.shape[0]
    group = min(4, count_r)

    def one_group(block):
        return jnp.stack([one(block[i]) for i in range(group)], axis=0)

    blocks = spectra_kj.reshape((count_r // group, group) + spectra_kj.shape[1:])
    if count_r == group:
        values = one_group(blocks[0])
    else:
        values = lax.map(one_group, blocks).reshape((count_r,) + (spectrum_v.shape[0],))
    return values.T


def per_device(tomogram, templates, corner_z, corner_y, corner_x, loads):
    own_total = corner_z.shape[1]
    live_count = jnp.sum(loads[0, 0])
    q2, box_rms = front(tomogram, corner_z[0], corner_y[0], corner_x[0])
    spectrum_v = box_spectra_of(q2)

    own_spectra = template_spectra(templates.reshape(-1, TMPL, TMPL, TMPL))
    spectra = lax.all_gather(own_spectra, "orient", axis=0, tiled=True)
    values = match_kj(spectrum_v, box_rms, spectra)
    live = jnp.arange(own_total, dtype=jnp.int32) < live_count
    matched = jnp.where(live[:, None], values, 0.0)
    return (matched[None], jnp.max(matched, axis=1)[None])


def solution(mesh):
    return jax.shard_map(
        per_device,
        mesh=mesh,
        in_specs=(
            P("vol", "orient", None),
            P("orient", None, None),
            P("vol", "orient"),
            P("vol", "orient"),
            P("vol", "orient"),
            P("vol", "orient", None),
        ),
        out_specs=(P("vol", "orient", None), P("vol", "orient")),
        check_vma=False,
    )
```

```python
import math

import jax
import jax.numpy as jnp
from jax import lax
from jax.sharding import PartitionSpec as P
from jax.experimental import pallas as pl
from jax.experimental.pallas import tpu as pltpu

BOX = 64
TMPL = 32
SHIFT = 8
HALF = 33


epsilon = 1e-05


def shift_anchor():
    return (BOX - TMPL) // 2 - SHIFT // 2


def angle_of(turn_index):
    return turn_index.astype(jnp.float32) * (2.0 * math.pi / BOX)


def phases(count_out, count_in, offset):
    out_index = jnp.arange(count_out, dtype=jnp.int32) + offset
    in_index = jnp.arange(count_in, dtype=jnp.int32)
    turn_index = out_index[:, None] * in_index[None, :] % BOX
    phase_angle = angle_of(turn_index)
    return (jnp.cos(phase_angle), jnp.sin(phase_angle))


def bf(x):
    return x.astype(jnp.bfloat16)


def complex_table(cos_t, sin_t, sign_re_from_im, sign_im_from_re):
    c = bf(cos_t).T
    s = bf(sin_t).T
    re_row = jnp.stack([c, sign_im_from_re * s], axis=1)
    im_row = jnp.stack([sign_re_from_im * s, c], axis=1)
    return jnp.stack([re_row, im_row], axis=0)


def section(pattern, operand, table):
    return jnp.einsum(pattern, bf(operand), table, preferred_element_type=jnp.float32)


def forward_tail(stage_one):
    length_a = stage_one.shape[2]
    length_y = stage_one.shape[3]
    cos_full, sin_full = phases(BOX, length_y, 0)
    t_mid = complex_table(cos_full, sin_full, 1.0, -1.0)
    stage_two = section("ncayk,cydj->ndajk", stage_one, t_mid)
    cos_half, sin_half = phases(HALF, length_a, 0)
    t_first = complex_table(cos_half, sin_half, 1.0, -1.0)
    return section("ncajk,cadh->ndhjk", stage_two, t_first)


def template_spectra(cubes):
    volume = cubes.astype(jnp.float32)
    count = volume.shape[0]
    flat = volume.reshape(count, -1)
    centred = flat - jnp.mean(flat, axis=1, keepdims=True)
    unit = centred / jnp.sqrt(jnp.mean(centred * centred, axis=1, keepdims=True) + epsilon)
    cos_full, sin_full = phases(BOX, TMPL, 0)
    c_full = bf(cos_full).T
    s_full = bf(sin_full).T
    t_last = jnp.concatenate([c_full, -s_full], axis=1)
    stage_one = jnp.dot(bf(unit).reshape(count * TMPL * TMPL, TMPL), t_last, preferred_element_type=jnp.float32)
    stage_one = bf(stage_one).reshape(count, TMPL, TMPL, 2, BOX)
    stacked = jnp.transpose(stage_one, (0, 1, 4, 3, 2)).reshape(count * TMPL * BOX, 2 * TMPL)
    t_mid = jnp.concatenate(
        [jnp.concatenate([c_full, -s_full], axis=1), jnp.concatenate([s_full, c_full], axis=1)], axis=0
    )
    stage_two = jnp.dot(stacked, t_mid, preferred_element_type=jnp.float32)
    stage_two = bf(stage_two).reshape(count, TMPL, BOX, 2 * BOX)
    swapped = jnp.concatenate([stage_two[..., BOX:], -stage_two[..., :BOX]], axis=-1)
    pair = jnp.stack([stage_two, swapped], axis=1)
    cos_half, sin_half = phases(HALF, TMPL, 0)
    t_first = jnp.stack([bf(cos_half).T, bf(sin_half).T], axis=0)
    return bf(jnp.einsum("rwakq,wah->rhkq", pair, t_first, preferred_element_type=jnp.float32))


def window_table(corner_x, width):
    pos = jnp.arange(width, dtype=jnp.int32)[None, :] - corner_x[:, None]
    inside = (pos >= 0) & (pos < BOX)
    k = jnp.arange(BOX, dtype=jnp.int32)
    turn = k[None, None, :] * pos[:, :, None] % BOX
    phase_angle = angle_of(turn)
    mask = inside[:, :, None]
    cos_t = jnp.where(mask, bf(jnp.cos(phase_angle)), jnp.zeros((), jnp.bfloat16))
    sin_t = jnp.where(mask, -bf(jnp.sin(phase_angle)), jnp.zeros((), jnp.bfloat16))
    return jnp.stack([cos_t, sin_t], axis=2)


def band_table():
    lower_edge = jnp.arange(SHIFT, dtype=jnp.int32)[:, None] + shift_anchor()
    cell_index = jnp.arange(BOX, dtype=jnp.int32)[None, :]
    return ((cell_index >= lower_edge) & (cell_index < lower_edge + TMPL)).astype(jnp.float32)


def window_band(corner_x, width):
    lower_edge = jnp.arange(SHIFT, dtype=jnp.int32)[None, :, None] + shift_anchor() + corner_x[:, None, None]
    cell_index = jnp.arange(width, dtype=jnp.int32)[None, None, :]
    return ((cell_index >= lower_edge) & (cell_index < lower_edge + TMPL)).astype(jnp.float32)


def window_rms(rows, corner_x):
    width = rows.shape[-1]
    squares = rows.astype(jnp.float32) ** 2
    band_x = window_band(corner_x, width)
    band = band_table()
    hi = lax.Precision.HIGHEST
    sums_c = jnp.einsum("nabx,nux->nabu", squares, band_x, precision=hi)
    sums_b = jnp.einsum("nabu,tb->natu", sums_c, band, precision=hi)
    sums_a = jnp.einsum("natu,sa->nstu", sums_b, band, precision=hi)
    return jnp.sqrt(sums_a / float(TMPL**3) + epsilon)


def match(box_spectra, box_rms, spectra):
    values = lax.map(lambda one: match_one(box_spectra, box_rms, one[None]), spectra)
    return values[:, :, 0].T


def match_one(box_spectra, box_rms, spectra):
    real_t = spectra[:, 0].astype(jnp.float32)[None]
    imag_t = spectra[:, 1].astype(jnp.float32)[None]
    real_v = box_spectra[:, 0][:, None]
    imag_v = box_spectra[:, 1][:, None]
    real_p = real_t * real_v + imag_t * imag_v
    imag_p = real_t * imag_v - imag_t * real_v
    cross = jnp.stack([bf(real_p), bf(imag_p)], axis=2)
    cos_first, sin_first = phases(SHIFT, HALF, shift_anchor())
    freq_index = jnp.arange(HALF, dtype=jnp.int32)
    weight = jnp.where(freq_index % (BOX // 2) == 0, 1.0, 2.0) / float(BOX**3)
    cos_first = cos_first * weight[None, :]
    sin_first = sin_first * weight[None, :]
    t_first = complex_table(cos_first, sin_first, -1.0, 1.0)
    stage_g = section("nrchjk,chds->nrdsjk", cross, t_first)
    cos_rest, sin_rest = phases(SHIFT, BOX, shift_anchor())
    t_mid = complex_table(cos_rest, sin_rest, -1.0, 1.0)
    stage_h = section("nrcsjk,cjdt->nrdstk", stage_g, t_mid)
    t_last = jnp.stack([bf(cos_rest).T, -bf(sin_rest).T], axis=0)
    correlation = section("nrcstk,cku->nrstu", stage_h, t_last)
    scores = correlation / (box_rms[:, None] * math.sqrt(float(TMPL**3)))
    return jnp.max(scores, axis=(2, 3, 4))


def front_kernel(cz_ref, ys_ref, slab_ref, t1_ref, l2_ref, q2_ref):
    depth, window_y, width = slab_ref.shape
    rows_y = 2 * BOX
    chunk = 64
    t1 = t1_ref[...]
    l2 = l2_ref[...]

    def transform_chunk(ci, carry):
        z0 = pl.multiple_of(ci * chunk, chunk)
        rows = slab_ref[pl.ds(z0, chunk)].reshape(chunk * window_y, width)
        p1 = jnp.dot(rows, t1, preferred_element_type=jnp.float32)
        p1 = p1.astype(jnp.bfloat16).astype(jnp.float32).reshape(chunk, window_y, 2 * BOX)
        pad = jnp.zeros((chunk, rows_y - window_y, 2 * BOX), jnp.float32)
        p1 = jnp.concatenate([p1, pad], axis=1)
        p1t = jnp.swapaxes(p1, 1, 2)
        stacked = jnp.concatenate([p1t[:, :BOX], p1t[:, BOX:]], axis=2)
        stacked = stacked.reshape(chunk * BOX, 2 * rows_y).astype(jnp.bfloat16)
        m2 = jnp.dot(stacked, l2, preferred_element_type=jnp.float32).reshape(chunk, BOX, 2 * BOX)
        lane = lax.broadcasted_iota(jnp.int32, m2.shape, 2)
        sign = jnp.where(lane < BOX, 1.0, -1.0).astype(jnp.float32)
        out = m2.astype(jnp.bfloat16).astype(jnp.float32)
        q2_ref[0, pl.ds(z0, chunk)] = out.astype(jnp.bfloat16)
        swapped = sign * pltpu.roll(out, BOX, 2)
        q2_ref[1, pl.ds(z0, chunk)] = swapped.astype(jnp.bfloat16)
        return carry

    lax.fori_loop(0, depth // chunk, transform_chunk, 0)


def window_bands(corner, length):
    lower_edge = jnp.arange(SHIFT, dtype=jnp.int32)[None, :, None] + shift_anchor() + corner[:, None, None]
    cell_index = jnp.arange(length, dtype=jnp.int32)[None, None, :]
    return ((cell_index >= lower_edge) & (cell_index < lower_edge + TMPL)).astype(jnp.float32)


def block_rms(tomogram, corner_z, corner_y, corner_x):
    depth, rows_y, width = tomogram.shape
    count = corner_z.shape[0]
    hi = lax.Precision.HIGHEST
    values = tomogram.astype(jnp.float32)
    squares = (values * values).reshape(depth * rows_y, width)
    square_hi = bf(squares)
    square_lo = bf(squares - square_hi.astype(jnp.float32))
    band_x = bf(window_bands(corner_x, width).reshape(count * SHIFT, width).T)
    sums_x = jnp.dot(square_hi, band_x, preferred_element_type=jnp.float32)
    sums_x = sums_x + jnp.dot(square_lo, band_x, preferred_element_type=jnp.float32)
    sums_x = sums_x.reshape(depth, rows_y, count, SHIFT)
    band_y = window_bands(corner_y, rows_y)
    sums_y = jnp.einsum("zynu,nty->nztu", sums_x, band_y, precision=hi)
    band_z = window_bands(corner_z, depth)
    sums_z = jnp.einsum("nztu,nsz->nstu", sums_y, band_z, precision=hi)
    return jnp.sqrt(sums_z / float(TMPL**3) + epsilon)


def front(tomogram, corner_z, corner_y, corner_x):
    count = corner_z.shape[0]
    block_y = tomogram.shape[1]
    window_y = BOX + 16
    rows_y = 2 * BOX
    width = tomogram.shape[2]
    start_y = jnp.minimum((corner_y // 16) * 16, block_y - window_y).astype(jnp.int32)
    t1 = window_table(corner_x, width).reshape(count, width, 2 * BOX)
    pos_y = jnp.arange(rows_y, dtype=jnp.int32)[None, :] - (corner_y - start_y)[:, None]
    inside_y = (pos_y >= 0) & (pos_y < BOX)
    j = jnp.arange(BOX, dtype=jnp.int32)
    turn_y = pos_y[:, :, None] * j[None, None, :] % BOX
    angle_y = angle_of(turn_y)
    zero = jnp.zeros((), jnp.bfloat16)
    cos_y = jnp.where(inside_y[:, :, None], bf(jnp.cos(angle_y)), zero)
    sin_y = jnp.where(inside_y[:, :, None], bf(jnp.sin(angle_y)), zero)
    l2 = jnp.concatenate(
        [jnp.concatenate([cos_y, -sin_y], axis=2), jnp.concatenate([sin_y, cos_y], axis=2)], axis=1
    )

    grid_spec = pltpu.PrefetchScalarGridSpec(
        num_scalar_prefetch=2,
        grid=(count,),
        in_specs=[
            pl.BlockSpec(
                (pl.Element(BOX), pl.Element(window_y), pl.Element(width)), lambda n, cz, ys: (cz[n], pl.multiple_of(ys[n], 16), 0)
            ),
            pl.BlockSpec((None, width, 2 * BOX), lambda n, cz, ys: (n, 0, 0)),
            pl.BlockSpec((None, 2 * rows_y, 2 * BOX), lambda n, cz, ys: (n, 0, 0)),
        ],
        out_specs=pl.BlockSpec((None, 2, BOX, BOX, 2 * BOX), lambda n, cz, ys: (n, 0, 0, 0, 0)),
    )
    q2 = pl.pallas_call(
        front_kernel,
        grid_spec=grid_spec,
        out_shape=jax.ShapeDtypeStruct((count, 2, BOX, BOX, 2 * BOX), jnp.bfloat16),
        compiler_params=pltpu.CompilerParams(vmem_limit_bytes=48 * 1024 * 1024),
    )(corner_z, start_y, tomogram, t1, l2)
    return q2, block_rms(tomogram, corner_z, corner_y, corner_x)


def box_spectra_of(q2):
    cos_half, sin_half = phases(HALF, BOX, 0)
    l3 = jnp.stack([bf(cos_half).T, bf(sin_half).T], axis=0)
    return bf(jnp.einsum("nwzkq,wzh->nhkq", q2, l3, preferred_element_type=jnp.float32))


def match_kj(spectrum_v, box_rms, spectra):
    spectra_kj = spectra

    def one(spectrum):
        real_v = spectrum_v[..., :BOX]
        imag_v = spectrum_v[..., BOX:]
        real_t = spectrum[..., :BOX].astype(jnp.float32)[None, None]
        imag_t = spectrum[..., BOX:].astype(jnp.float32)[None, None]
        rv = real_v[:, None]
        iv = imag_v[:, None]
        real_p = real_t * rv + imag_t * iv
        imag_p = real_t * iv - imag_t * rv
        cross = jnp.stack([bf(real_p), bf(imag_p)], axis=2)
        cos_first, sin_first = phases(SHIFT, HALF, shift_anchor())
        freq_index = jnp.arange(HALF, dtype=jnp.int32)
        weight = jnp.where(freq_index % (BOX // 2) == 0, 1.0, 2.0) / float(BOX**3)
        t_first = complex_table(cos_first * weight[None, :], sin_first * weight[None, :], -1.0, 1.0)
        stage_g = section("nrchkj,chds->nrdskj", cross, t_first)
        cos_rest, sin_rest = phases(SHIFT, BOX, shift_anchor())
        t_mid = complex_table(cos_rest, sin_rest, -1.0, 1.0)
        stage_h = section("nrcskj,cjdt->nrdskt", stage_g, t_mid)
        t_last = jnp.stack([bf(cos_rest).T, -bf(sin_rest).T], axis=0)
        correlation = section("nrcskt,cku->nrstu", stage_h, t_last)
        scores = correlation / (box_rms[:, None] * math.sqrt(float(TMPL**3)))
        return jnp.max(scores, axis=(2, 3, 4))[:, 0]

    count_r = spectra_kj.shape[0]
    group = min(4, count_r)

    def one_group(block):
        return jnp.stack([one(block[i]) for i in range(group)], axis=0)

    blocks = spectra_kj.reshape((count_r // group, group) + spectra_kj.shape[1:])
    if count_r == group:
        values = one_group(blocks[0])
    else:
        values = lax.map(one_group, blocks).reshape((count_r,) + (spectrum_v.shape[0],))
    return values.T


def per_device(tomogram, templates, corner_z, corner_y, corner_x, loads):
    own_total = corner_z.shape[1]
    live_count = jnp.sum(loads[0, 0])
    q2, box_rms = front(tomogram, corner_z[0], corner_y[0], corner_x[0])
    spectrum_v = box_spectra_of(q2)

    own_spectra = template_spectra(templates.reshape(-1, TMPL, TMPL, TMPL))
    spectra = lax.all_gather(own_spectra, "orient", axis=0, tiled=True)
    values = match_kj(spectrum_v, box_rms, spectra)
    live = jnp.arange(own_total, dtype=jnp.int32) < live_count
    matched = jnp.where(live[:, None], values, 0.0)
    return (matched[None], jnp.max(matched, axis=1)[None])


def solution(mesh):
    return jax.shard_map(
        per_device,
        mesh=mesh,
        in_specs=(
            P("vol", "orient", None),
            P("orient", None, None),
            P("vol", "orient"),
            P("vol", "orient"),
            P("vol", "orient"),
            P("vol", "orient", None),
        ),
        out_specs=(P("vol", "orient", None), P("vol", "orient")),
        check_vma=False,
    )
```
